768 devices in a mesh: span: 32 (over x, y), freq: 24 (over z, core).
Axes of the slice: x: 4, y: 8, z: 12, core: 2. Of those that a mesh axis runs over, the one named last changes fastest.
Arguments:
- visibilities: bfloat16 [24, 1024, 2, 512], P('freq', 'span'), may hold values from -6 to 6
- coords: float32 [24, 1024, 2, 512], P('freq', 'span'), may hold values from -12 to 12
- vis_counts: int32 [24, 1024], P('freq', 'span'), may hold values from 128 to 512
- cover_tile: int32 [24, 1024, 1], P('freq', 'span'), may hold values from 0 to 31; in each aligned block of 32 rows (0 to 31, 32 to 63, ..., all dimensions but the last counted through in order) at most 2 rows name the same one
- offsets: int32 [24, 1024, 2], P('freq', 'span'), may hold values from 0 to 96
- channel: int32 [24, 1024], P('freq', 'span'), may hold values from 0 to 15
- taper: float32 [32, 32], replicated, may hold values from 0.2 to 1
Outputs:
- uv_terms: float32 [2, 32, 2, 128, 128], P(None, 'span')
The draws below stay inside these ranges and needn't reach their ends.
Inputs may be any that keep to these rules, and one draw needn't show every extreme that they name: `cover_tile`: the subgrids of one device name each tile at most 2 times, a bound that some block reaches.
All inputs are finite; a program needn't handle non-finite values.
Results may differ from the reference program's by a relative error of at most 0.005.
Values may be sent and summed in bfloat16 or wider, within the bound.
No kernel may reach another device: no remote copies, remote signals or barrier semaphores. Data moves between devices by JAX's collectives and lax.ppermute only.
A program may use at most 64 MiB of HBM per device.

```python
import math
import jax
import jax.numpy as jnp
import numpy as np
from jax import lax

K = 512
TILE = 128
NT = 2
SUB_DEV = 32
CH_DEV = 16
CAP = 2
SUBS = 1024
N_SPAN = 32
N_FREQ = 24


def set_ends(values, own_key, low, high):
    place = [jax.random.randint(jax.random.fold_in(own_key, axis), (), 0, length) for axis, length in enumerate(values.shape)]
    main_axis = values.shape.index(max(values.shape))
    beside = place[:main_axis] + [(place[main_axis] + 1) % values.shape[main_axis]] + place[main_axis + 1:]
    return values.at[tuple(place)].set(low).at[tuple(beside)].set(high)


def block_levels(own_key, extent, pieces, smallest, high):
    loudness, own = 1.0, jax.random.fold_in(own_key, 6)
    for dim, parts in pieces:
        heights = jnp.exp(jax.random.uniform(jax.random.fold_in(own, dim), (parts,), jnp.float32, smallest / len(pieces), high / len(pieces)))
        loudness = loudness * jnp.repeat(heights, extent[dim] // parts).reshape([-1 if axis == dim else 1 for axis in range(len(extent))])
    return loudness


def assign_block(rng, own, number, rows, count, top, limit, skew):
    ranking = jax.random.permutation(rng, count)
    crowded, usual = load_shares(count, rows * top, limit, skew, True), load_shares(count, rows * top, limit, skew, False)
    places = jnp.arange(count)

    def named(tallies, turn):
        used = int((tallies > 0).sum())
        fixed = max(1, used // 4)
        passed = fixed + (places - fixed + turn * (used - fixed)) % max(1, count - fixed)
        return jnp.zeros((count,), jnp.int32).at[ranking[jnp.where(places < fixed, places, passed)]].set(jnp.asarray(tallies, jnp.int32))

    tallies = jnp.where(number % 4 == 0, named(crowded, number // 4), named(usual, number - number // 4 - 1))
    mixed = jax.random.permutation(jax.random.fold_in(own, 3), count)
    source_of, receiver = mixed[0:count // 2 * 2:2], mixed[1:count // 2 * 2:2]
    room = jnp.minimum(tallies[source_of] - 1, limit - tallies[receiver]) // 2
    room = jnp.where((source_of == ranking[0]) | (receiver == ranking[0]) | (tallies[receiver] == 0), 0, jnp.maximum(room, 0))
    passed = jax.random.randint(jax.random.fold_in(own, 4), (count // 2,), 0, 1 << 20) % (room + 1)
    tallies = tallies.at[source_of].add(-passed).at[receiver].add(passed)
    items = jnp.searchsorted(jnp.cumsum(tallies), jnp.arange(rows * top), side="right").astype(jnp.int32)
    table = items.reshape(top, rows).T
    table = table[jax.random.permutation(jax.random.fold_in(own, 1), rows)]
    turn = jax.random.randint(jax.random.fold_in(own, 2), (rows, 1), 0, top)
    return jnp.take_along_axis(table, (jnp.arange(top)[None, :] + turn) % top, axis=1)


def load_shares(amount, total, bound, slope, full):
    weights = [(1 << 20) // math.isqrt(standing ** slope) + 1 for standing in range(1, amount + 1)]
    largest = bound if full else min(bound, max(-(-total // amount), total * weights[0] // sum(weights)))
    least = 1 if total - largest >= amount - 1 else 0
    given, rest = [largest] + [least] * (amount - 1), total - largest - least * (amount - 1)
    while rest > 0:
        candidates = [i for i in range(1, amount) if given[i] < largest] or [i for i in range(1, amount) if given[i] < bound]
        whole, left = sum([weights[i] for i in candidates]), rest
        for i in candidates:
            more = min(bound - given[i], max(1, left * weights[i] // whole), rest)
            given[i] = given[i] + more
            rest = rest - more
    return np.array(given)


def scatter_about(stream_key, extent, spread, reach, shards=(), kind=jnp.bfloat16):
    level = block_levels(stream_key, extent, shards, -0.22, 0.18) if shards else 1.0
    drawn = jax.random.normal(stream_key, extent, jnp.float32) * spread * level
    return jnp.minimum(jnp.maximum(drawn, -reach), reach).astype(kind)


def setup_inputs(seed: int = 0) -> dict:
    seeds = jax.random.split(jax.random.key(seed), 8)
    visibilities = scatter_about(seeds[0], (N_FREQ, SUBS, 2, K), 1.0, 6.0, ((0, 24), (1, 32)))
    coords = jnp.clip(jax.random.uniform(seeds[1], (N_FREQ, SUBS, 2, K), jnp.float32, -12.0, 12.0) * block_levels(seeds[1], (N_FREQ, SUBS, 2, K), ((0, 24), (1, 32)), -0.4, 0.0), -12.0, 12.0)
    vis_counts = set_ends(jax.random.randint(seeds[2], (N_FREQ, SUBS), K // 4, K + 1), jax.random.fold_in(seeds[2], 1), K // 4, K).astype(jnp.int32)
    cover_tile_keys = jax.random.split(jax.random.fold_in(seeds[3], 1), N_FREQ * SUBS // SUB_DEV)
    cover_tile_turns = jax.random.permutation(jax.random.fold_in(seeds[3], 3), N_FREQ * SUBS // SUB_DEV)
    cover_tile = jax.vmap(lambda own, number: assign_block(jax.random.fold_in(seeds[3], 2), own, number, SUB_DEV, N_SPAN, 1, CAP, 2))(cover_tile_keys, cover_tile_turns).reshape((N_FREQ, SUBS, 1))
    offsets = set_ends(jax.random.randint(seeds[4], (N_FREQ, SUBS, 2), 0, TILE - 31), jax.random.fold_in(seeds[4], 1), 0, (TILE - 31) - 1).astype(jnp.int32)
    channel = set_ends(jax.random.randint(seeds[5], (N_FREQ, SUBS), 0, CH_DEV), jax.random.fold_in(seeds[5], 1), 0, CH_DEV - 1).astype(jnp.int32)
    taper = jnp.clip(jnp.exp(jax.random.uniform(seeds[6], (32, 32), jnp.float32, math.log(0.2), math.log(1.0))), 0.2, 1.0)
    return dict(visibilities=visibilities, coords=coords, vis_counts=vis_counts, cover_tile=cover_tile, offsets=offsets, channel=channel, taper=taper)


def make_subgrids(vis_b, coord_b, count_b, taper):
    kk = vis_b.shape[-1]
    pix = (jnp.arange(32, dtype=jnp.float32) - 16.0) / 32.0
    live = (jnp.arange(kk, dtype=jnp.int32)[None, :] < count_b[:, None]).astype(jnp.float32)
    scale_k = 1.0 / math.sqrt(kk)
    vis_re = vis_b[:, 0, :].astype(jnp.float32) * live * scale_k
    vis_im = vis_b[:, 1, :].astype(jnp.float32) * live * scale_k
    theta_v = -2.0 * math.pi * coord_b[:, 1, :, None] * pix
    cos_v, sin_v = (jnp.cos(theta_v), jnp.sin(theta_v))
    b_re = (vis_re[:, :, None] * cos_v - vis_im[:, :, None] * sin_v).astype(jnp.bfloat16).astype(jnp.float32)
    b_im = (vis_re[:, :, None] * sin_v + vis_im[:, :, None] * cos_v).astype(jnp.bfloat16).astype(jnp.float32)
    theta_u = -2.0 * math.pi * coord_b[:, 0, :, None] * pix
    a_re = jnp.cos(theta_u).astype(jnp.bfloat16).astype(jnp.float32)
    a_im = jnp.sin(theta_u).astype(jnp.bfloat16).astype(jnp.float32)
    hp = lax.Precision.HIGHEST
    s_re = jnp.einsum('bkp,bkq->bpq', a_re, b_re, precision=hp) - jnp.einsum('bkp,bkq->bpq', a_im, b_im, precision=hp)
    s_im = jnp.einsum('bkp,bkq->bpq', a_re, b_im, precision=hp) + jnp.einsum('bkp,bkq->bpq', a_im, b_re, precision=hp)
    x_re = taper * s_re
    x_im = taper * s_im
    centred = jnp.arange(32, dtype=jnp.float32) - 16.0
    angle = -2.0 * math.pi * centred[:, None] * centred[None, :] / 32.0
    f_re, f_im = (jnp.cos(angle), jnp.sin(angle))
    y_re = jnp.einsum('ap,bpq->baq', f_re, x_re, precision=hp) - jnp.einsum('ap,bpq->baq', f_im, x_im, precision=hp)
    y_im = jnp.einsum('ap,bpq->baq', f_re, x_im, precision=hp) + jnp.einsum('ap,bpq->baq', f_im, x_re, precision=hp)
    z_re = jnp.einsum('baq,cq->bac', y_re, f_re, precision=hp) - jnp.einsum('baq,cq->bac', y_im, f_im, precision=hp)
    z_im = jnp.einsum('baq,cq->bac', y_re, f_im, precision=hp) + jnp.einsum('baq,cq->bac', y_im, f_re, precision=hp)
    return (jnp.stack([z_re, z_im], 1) / 32.0).astype(jnp.bfloat16)

def reference(visibilities, coords, vis_counts, cover_tile, offsets, channel, taper):
    n_freq = visibilities.shape[0]
    subs = visibilities.shape[1]
    n_span = subs // SUB_DEV
    channels = CH_DEV * n_freq
    size = NT * n_span * 2 * TILE * TILE
    grid0 = jnp.zeros((size,), jnp.float32)
    tt = jnp.arange(NT, dtype=jnp.int32)[:, None, None, None, None]
    cc = jnp.arange(2, dtype=jnp.int32)[None, None, :, None, None]
    pp = jnp.arange(32, dtype=jnp.int32)[None, None, None, :, None]
    qq = jnp.arange(32, dtype=jnp.int32)[None, None, None, None, :]
    powers = jnp.arange(NT, dtype=jnp.float32)

    def one_block(grid, inputs):
        vis_b, coord_b, count_b, tile_b, off_b, chan_b, fidx = inputs
        z = make_subgrids(vis_b, coord_b, count_b, taper).astype(jnp.float32)
        cg = (fidx * CH_DEV + chan_b).astype(jnp.float32)
        xval = (2.0 * cg + 1.0 - channels) / channels
        weight = jnp.where(powers[None, :] == 0.0, 1.0, xval[:, None] ** powers[None, :])
        tile_i = tile_b[:, 0].astype(jnp.int32)[None, :, None, None, None]
        row_o = off_b[:, 0].astype(jnp.int32)[None, :, None, None, None]
        col_o = off_b[:, 1].astype(jnp.int32)[None, :, None, None, None]
        idx = (((tt * n_span + tile_i) * 2 + cc) * TILE + row_o + pp) * TILE + col_o + qq
        vals = weight.T[:, :, None, None, None] * z[None]
        return (grid.at[idx.reshape(-1)].add(vals.reshape(-1)), None)
    fidx = jnp.repeat(jnp.arange(n_freq, dtype=jnp.int32), n_span)
    blocks = (visibilities.reshape(n_freq * n_span, SUB_DEV, 2, -1), coords.reshape(n_freq * n_span, SUB_DEV, 2, -1), vis_counts.reshape(n_freq * n_span, SUB_DEV), cover_tile.reshape(n_freq * n_span, SUB_DEV, 1), offsets.reshape(n_freq * n_span, SUB_DEV, 2), channel.reshape(n_freq * n_span, SUB_DEV), fidx)
    grid, _ = lax.scan(one_block, grid0, blocks)
    scale = TILE / (32.0 * math.sqrt(n_freq * SUB_DEV))
    return grid.reshape(NT, n_span, 2, TILE, TILE) * scale
```

```python
import math

import jax
import jax.numpy as jnp
from jax import lax
from jax.sharding import PartitionSpec as P

TILE = 128
NT = 2
CH_DEV = 16


def sent_together(arrays, axis, split_dim, concat_dim, along):
    widths = [a.shape[along] for a in arrays]
    both = jnp.concatenate(arrays, axis=along)
    whole = lax.all_to_all(both, axis, split_axis=split_dim, concat_axis=concat_dim, tiled=True)
    return tuple(jnp.split(whole, [sum(widths[:k]) for k in range(1, len(widths))], axis=along))


def gathered_total(shard, axis):
    return lax.psum(shard, axis)


def make_subgrids(vis_b, coord_b, count_b, taper):
    kk = vis_b.shape[-1]
    pix = (jnp.arange(32, dtype=jnp.float32) - 16.0) / 32.0
    live = (jnp.arange(kk, dtype=jnp.int32)[None, :] < count_b[:, None]).astype(jnp.float32)
    scale_k = 1.0 / math.sqrt(kk)
    vis_re = vis_b[:, 0, :].astype(jnp.float32) * live * scale_k
    vis_im = vis_b[:, 1, :].astype(jnp.float32) * live * scale_k
    theta_v = -2.0 * math.pi * coord_b[:, 1, :, None] * pix
    cos_v, sin_v = (jnp.cos(theta_v), jnp.sin(theta_v))
    b_re = (vis_re[:, :, None] * cos_v - vis_im[:, :, None] * sin_v).astype(jnp.bfloat16)
    b_im = (vis_re[:, :, None] * sin_v + vis_im[:, :, None] * cos_v).astype(jnp.bfloat16)
    theta_u = -2.0 * math.pi * coord_b[:, 0, :, None] * pix
    a_re = jnp.cos(theta_u).astype(jnp.bfloat16)
    a_im = jnp.sin(theta_u).astype(jnp.bfloat16)
    f32 = jnp.float32
    s_re = jnp.einsum("bkp,bkq->bpq", a_re, b_re, preferred_element_type=f32) - jnp.einsum(
        "bkp,bkq->bpq", a_im, b_im, preferred_element_type=f32
    )
    s_im = jnp.einsum("bkp,bkq->bpq", a_re, b_im, preferred_element_type=f32) + jnp.einsum(
        "bkp,bkq->bpq", a_im, b_re, preferred_element_type=f32
    )
    x_re = taper * s_re
    x_im = taper * s_im
    centred = jnp.arange(32, dtype=jnp.float32) - 16.0
    angle = -2.0 * math.pi * centred[:, None] * centred[None, :] / 32.0
    f_re, f_im = (jnp.cos(angle), jnp.sin(angle))
    hp = lax.Precision.HIGHEST
    y_re = jnp.einsum("ap,bpq->baq", f_re, x_re, precision=hp) - jnp.einsum(
        "ap,bpq->baq", f_im, x_im, precision=hp
    )
    y_im = jnp.einsum("ap,bpq->baq", f_re, x_im, precision=hp) + jnp.einsum(
        "ap,bpq->baq", f_im, x_re, precision=hp
    )
    z_re = jnp.einsum("baq,cq->bac", y_re, f_re, precision=hp) - jnp.einsum(
        "baq,cq->bac", y_im, f_im, precision=hp
    )
    z_im = jnp.einsum("baq,cq->bac", y_re, f_im, precision=hp) + jnp.einsum(
        "baq,cq->bac", y_im, f_re, precision=hp
    )
    return (jnp.stack([z_re, z_im], 1) / 32.0).astype(jnp.bfloat16)


def taylor_weights(chan_local, freq_pos, channels):
    global_chan = (freq_pos * CH_DEV + chan_local).astype(jnp.float32)
    xval = (2.0 * global_chan + 1.0 - channels) / channels
    powers = jnp.arange(NT, dtype=jnp.float32)
    return jnp.where(powers[None, :] == 0.0, 1.0, xval[:, None] ** powers[None, :])


def place_block(tile_acc, inputs):
    patch_b, weight_b, rows_b, cols_b = inputs
    hp = lax.Precision.HIGHEST
    cells = jnp.arange(TILE, dtype=jnp.int32)
    small = jnp.arange(32, dtype=jnp.int32)
    row_hot = (cells[None, :, None] == rows_b[:, None, None] + small[None, None, :]).astype(
        jnp.float32
    )
    col_hot = (cells[None, :, None] == cols_b[:, None, None] + small[None, None, :]).astype(
        jnp.float32
    )
    spread = jnp.einsum("scab,sQb->scaQ", patch_b.astype(jnp.float32), col_hot, precision=hp)
    terms = []
    for term in range(NT):
        weighted = spread * weight_b[:, term][:, None, None, None]
        terms.append(jnp.einsum("sRa,scaQ->cRQ", row_hot, weighted, precision=hp))
    return (tile_acc + jnp.stack(terms, 0), None)


def body(visibilities, coords, vis_counts, cover_tile, offsets, channel, taper):
    n_span = lax.axis_size("span")
    n_freq = lax.axis_size("freq")
    channels = CH_DEV * n_freq
    freq_pos = lax.axis_index("freq")
    sub_count = visibilities.shape[1]
    groups = sub_count // 32
    vis_loc = visibilities[0].reshape(groups, 32, 2, -1)
    coord_loc = coords[0].reshape(groups, 32, 2, -1)
    count_loc = vis_counts[0].reshape(groups, 32)

    def block_work(inputs):
        return make_subgrids(inputs[0], inputs[1], inputs[2], taper)

    patches = lax.map(block_work, (vis_loc, coord_loc, count_loc)).reshape(sub_count, 2, 32, 32)
    dest = cover_tile[0, :, 0]
    row_off = offsets[0, :, 0]
    col_off = offsets[0, :, 1]
    chan_loc = channel[0]
    cap = 2 * sub_count // n_span
    onehot = (dest[:, None] == jnp.arange(n_span, dtype=jnp.int32)[None, :]).astype(jnp.float32)
    order = jnp.arange(sub_count, dtype=jnp.int32)
    lower = (order[:, None] > order[None, :]).astype(jnp.float32)
    earlier = jnp.dot(lower, onehot, preferred_element_type=jnp.float32)
    rank = jnp.sum(earlier * onehot, axis=1).astype(jnp.int32)
    slot = dest * cap + rank
    payload = (
        jnp.zeros((n_span * cap, 2048), jnp.bfloat16).at[slot].set(patches.reshape(sub_count, 2048))
    )
    info = jnp.stack([jnp.ones_like(dest), row_off, col_off, chan_loc], 1).astype(jnp.bfloat16)
    meta = jnp.zeros((n_span * cap, 4), jnp.bfloat16).at[slot].set(info)
    got_payload, got_meta = sent_together(
        (payload.reshape(n_span, cap, 2048), meta.reshape(n_span, cap, 4)), "span", 0, 0, 2
    )
    slots = n_span * cap
    got_meta = got_meta.reshape(slots, 4).astype(jnp.int32)
    valid = got_meta[:, 0].astype(jnp.float32)
    weight = taylor_weights(got_meta[:, 3], freq_pos, channels) * valid[:, None]
    blocks = slots // 32
    inputs = (
        got_payload.reshape(blocks, 32, 2, 32, 32),
        weight.reshape(blocks, 32, NT),
        got_meta[:, 1].reshape(blocks, 32),
        got_meta[:, 2].reshape(blocks, 32),
    )
    start_tile = jnp.zeros((NT, 2, TILE, TILE), jnp.float32)
    local, _ = lax.scan(place_block, start_tile, inputs)
    local = local.reshape(NT, 1, 2, TILE, TILE)
    total = gathered_total(local, "freq")
    scale = TILE / (32.0 * math.sqrt(n_freq * sub_count))
    return total * scale


def solution(mesh):
    return jax.shard_map(
        body,
        mesh=mesh,
        in_specs=(
            P("freq", "span", None, None),
            P("freq", "span", None, None),
            P("freq", "span"),
            P("freq", "span", None),
            P("freq", "span", None),
            P("freq", "span"),
            P(),
        ),
        out_specs=P(None, "span", None, None, None),
        check_vma=False,
    )
```

```python
import math

import jax
import jax.numpy as jnp
from jax import lax
from jax.sharding import PartitionSpec as P

TILE = 128
NT = 2
CH_DEV = 16


def sent_together(arrays, axis, split_dim, concat_dim, along):
    widths = [a.shape[along] for a in arrays]
    both = jnp.concatenate(arrays, axis=along)
    whole = lax.all_to_all(both, axis, split_axis=split_dim, concat_axis=concat_dim, tiled=True)
    return tuple(jnp.split(whole, [sum(widths[:k]) for k in range(1, len(widths))], axis=along))


def gathered_total(shard, axis):
    n = lax.axis_size(axis)
    flat = shard.reshape(-1)
    size = flat.shape[0]
    per = -(-size // (n * 128)) * 128
    flat = jnp.pad(flat, (0, per * n - size))
    got = lax.all_to_all(flat.reshape(n, per), axis, 0, 0, tiled=True)
    part = got.sum(axis=0)
    spread = jnp.broadcast_to(part[None], (n, per))
    whole = lax.all_to_all(spread, axis, 0, 0, tiled=True)
    return whole.reshape(-1)[:size].reshape(shard.shape)


def make_subgrids(vis_b, coord_b, count_b, taper):
    kk = vis_b.shape[-1]
    pix = (jnp.arange(32, dtype=jnp.float32) - 16.0) / 32.0
    live = (jnp.arange(kk, dtype=jnp.int32)[None, :] < count_b[:, None]).astype(jnp.float32)
    scale_k = 1.0 / math.sqrt(kk)
    vis_re = vis_b[:, 0, :].astype(jnp.float32) * live * scale_k
    vis_im = vis_b[:, 1, :].astype(jnp.float32) * live * scale_k
    theta_v = -2.0 * math.pi * coord_b[:, 1, :, None] * pix
    cos_v, sin_v = (jnp.cos(theta_v), jnp.sin(theta_v))
    b_re = (vis_re[:, :, None] * cos_v - vis_im[:, :, None] * sin_v).astype(jnp.bfloat16)
    b_im = (vis_re[:, :, None] * sin_v + vis_im[:, :, None] * cos_v).astype(jnp.bfloat16)
    theta_u = -2.0 * math.pi * coord_b[:, 0, :, None] * pix
    a_re = jnp.cos(theta_u).astype(jnp.bfloat16)
    a_im = jnp.sin(theta_u).astype(jnp.bfloat16)
    f32 = jnp.float32
    s_re = jnp.einsum("bkp,bkq->bpq", a_re, b_re, preferred_element_type=f32) - jnp.einsum(
        "bkp,bkq->bpq", a_im, b_im, preferred_element_type=f32
    )
    s_im = jnp.einsum("bkp,bkq->bpq", a_re, b_im, preferred_element_type=f32) + jnp.einsum(
        "bkp,bkq->bpq", a_im, b_re, preferred_element_type=f32
    )
    x_re = taper * s_re
    x_im = taper * s_im
    centred = jnp.arange(32, dtype=jnp.float32) - 16.0
    angle = -2.0 * math.pi * centred[:, None] * centred[None, :] / 32.0
    f_re, f_im = (jnp.cos(angle), jnp.sin(angle))
    hp = lax.Precision.HIGHEST
    y_re = jnp.einsum("ap,bpq->baq", f_re, x_re, precision=hp) - jnp.einsum(
        "ap,bpq->baq", f_im, x_im, precision=hp
    )
    y_im = jnp.einsum("ap,bpq->baq", f_re, x_im, precision=hp) + jnp.einsum(
        "ap,bpq->baq", f_im, x_re, precision=hp
    )
    z_re = jnp.einsum("baq,cq->bac", y_re, f_re, precision=hp) - jnp.einsum(
        "baq,cq->bac", y_im, f_im, precision=hp
    )
    z_im = jnp.einsum("baq,cq->bac", y_re, f_im, precision=hp) + jnp.einsum(
        "baq,cq->bac", y_im, f_re, precision=hp
    )
    return (jnp.stack([z_re, z_im], 1) / 32.0).astype(jnp.bfloat16)


def taylor_weights(chan_local, freq_pos, channels):
    global_chan = (freq_pos * CH_DEV + chan_local).astype(jnp.float32)
    xval = (2.0 * global_chan + 1.0 - channels) / channels
    powers = jnp.arange(NT, dtype=jnp.float32)
    return jnp.where(powers[None, :] == 0.0, 1.0, xval[:, None] ** powers[None, :])


def place_block(tile_acc, inputs):
    patch_b, weight_b, rows_b, cols_b = inputs
    hp = lax.Precision.HIGHEST
    cells = jnp.arange(TILE, dtype=jnp.int32)
    small = jnp.arange(32, dtype=jnp.int32)
    row_hot = (cells[None, :, None] == rows_b[:, None, None] + small[None, None, :]).astype(
        jnp.float32
    )
    col_hot = (cells[None, :, None] == cols_b[:, None, None] + small[None, None, :]).astype(
        jnp.float32
    )
    spread = jnp.einsum("scab,sQb->scaQ", patch_b.astype(jnp.float32), col_hot, precision=hp)
    terms = []
    for term in range(NT):
        weighted = spread * weight_b[:, term][:, None, None, None]
        terms.append(jnp.einsum("sRa,scaQ->cRQ", row_hot, weighted, precision=hp))
    return (tile_acc + jnp.stack(terms, 0), None)


def body(visibilities, coords, vis_counts, cover_tile, offsets, channel, taper):
    n_span = lax.axis_size("span")
    n_freq = lax.axis_size("freq")
    channels = CH_DEV * n_freq
    freq_pos = lax.axis_index("freq")
    sub_count = visibilities.shape[1]
    groups = sub_count // 32
    vis_loc = visibilities[0].reshape(groups, 32, 2, -1)
    coord_loc = coords[0].reshape(groups, 32, 2, -1)
    count_loc = vis_counts[0].reshape(groups, 32)

    def block_work(inputs):
        return make_subgrids(inputs[0], inputs[1], inputs[2], taper)

    patches = lax.map(block_work, (vis_loc, coord_loc, count_loc)).reshape(sub_count, 2, 32, 32)
    dest = cover_tile[0, :, 0]
    row_off = offsets[0, :, 0]
    col_off = offsets[0, :, 1]
    chan_loc = channel[0]
    cap = 2 * sub_count // n_span
    onehot = (dest[:, None] == jnp.arange(n_span, dtype=jnp.int32)[None, :]).astype(jnp.float32)
    order = jnp.arange(sub_count, dtype=jnp.int32)
    lower = (order[:, None] > order[None, :]).astype(jnp.float32)
    earlier = jnp.dot(lower, onehot, preferred_element_type=jnp.float32)
    rank = jnp.sum(earlier * onehot, axis=1).astype(jnp.int32)
    slot = dest * cap + rank
    payload = (
        jnp.zeros((n_span * cap, 2048), jnp.bfloat16).at[slot].set(patches.reshape(sub_count, 2048))
    )
    info = jnp.stack([jnp.ones_like(dest), row_off, col_off, chan_loc], 1).astype(jnp.bfloat16)
    meta = jnp.zeros((n_span * cap, 4), jnp.bfloat16).at[slot].set(info)
    got_payload, got_meta = sent_together(
        (payload.reshape(n_span, cap, 2048), meta.reshape(n_span, cap, 4)), "span", 0, 0, 2
    )
    slots = n_span * cap
    got_meta = got_meta.reshape(slots, 4).astype(jnp.int32)
    valid = got_meta[:, 0].astype(jnp.float32)
    weight = taylor_weights(got_meta[:, 3], freq_pos, channels) * valid[:, None]
    blocks = slots // 32
    inputs = (
        got_payload.reshape(blocks, 32, 2, 32, 32),
        weight.reshape(blocks, 32, NT),
        got_meta[:, 1].reshape(blocks, 32),
        got_meta[:, 2].reshape(blocks, 32),
    )
    start_tile = jnp.zeros((NT, 2, TILE, TILE), jnp.float32)
    local, _ = lax.scan(place_block, start_tile, inputs)
    local = local.reshape(NT, 1, 2, TILE, TILE)
    total = gathered_total(local, "freq")
    scale = TILE / (32.0 * math.sqrt(n_freq * sub_count))
    return total * scale


def solution(mesh):
    return jax.shard_map(
        body,
        mesh=mesh,
        in_specs=(
            P("freq", "span", None, None),
            P("freq", "span", None, None),
            P("freq", "span"),
            P("freq", "span", None),
            P("freq", "span", None),
            P("freq", "span"),
            P(),
        ),
        out_specs=P(None, "span", None, None, None),
        check_vma=False,
    )
```

```python
import math

import jax
import jax.numpy as jnp
from jax import lax
from jax.sharding import PartitionSpec as P

TILE = 128
NT = 2
CH_DEV = 16


def sent_together(arrays, axis, split_dim, concat_dim, along):
    widths = [a.shape[along] for a in arrays]
    both = jnp.concatenate(arrays, axis=along)
    whole = lax.all_to_all(both, axis, split_axis=split_dim, concat_axis=concat_dim, tiled=True)
    return tuple(jnp.split(whole, [sum(widths[:k]) for k in range(1, len(widths))], axis=along))


def gathered_total(shard, axis):
    n = lax.axis_size(axis)
    flat = shard.reshape(-1)
    size = flat.shape[0]
    per = -(-size // (n * 128)) * 128
    flat = jnp.pad(flat, (0, per * n - size))
    got = lax.all_to_all(flat.reshape(n, per), axis, 0, 0, tiled=True)
    part = got.sum(axis=0)
    spread = jnp.broadcast_to(part[None], (n, per))
    whole = lax.all_to_all(spread, axis, 0, 0, tiled=True)
    return whole.reshape(-1)[:size].reshape(shard.shape)


def cmul(ar, ai, br, bi):
    return ar * br - ai * bi, ar * bi + ai * br


def phase_rows(angle):
    c, s = lax.optimization_barrier((jnp.cos(angle), jnp.sin(angle)))
    pw = [(jnp.ones_like(c), jnp.zeros_like(c)), (c, s)]
    for m in range(2, 17):
        if m % 2 == 0:
            pw.append(cmul(*pw[m // 2], *pw[m // 2]))
        else:
            pw.append(cmul(*pw[m - 1], c, s))
    rows = []
    for p in range(32):
        m = p - 16
        if m >= 0:
            rows.append(pw[m])
        else:
            rows.append((pw[-m][0], -pw[-m][1]))
    return rows


def make_subgrids(vis_b, coord_b, count_b, taper):
    kk = vis_b.shape[-1]
    live = (jnp.arange(kk, dtype=jnp.int32)[None, :] < count_b[:, None]).astype(jnp.float32)
    scale_k = 1.0 / math.sqrt(kk)
    vis_re = vis_b[:, 0, :].astype(jnp.float32) * live * scale_k
    vis_im = vis_b[:, 1, :].astype(jnp.float32) * live * scale_k
    step = -2.0 * math.pi / 32.0
    rows_u = phase_rows(step * coord_b[:, 0, :])
    rows_v = phase_rows(step * coord_b[:, 1, :])
    bf = jnp.bfloat16
    a_t = jnp.stack([r for r, _ in rows_u] + [i for _, i in rows_u], axis=1).astype(bf)
    b_rows = [cmul(vis_re, vis_im, r, i) for r, i in rows_v]
    b_t = jnp.stack([r for r, _ in b_rows] + [i for _, i in b_rows], axis=1).astype(bf)
    a_t, b_t = lax.optimization_barrier((a_t, b_t))
    f32 = jnp.float32
    s_all = jnp.einsum("bik,bjk->bij", a_t, b_t, preferred_element_type=f32)
    s_re = s_all[:, :32, :32] - s_all[:, 32:, 32:]
    s_im = s_all[:, :32, 32:] + s_all[:, 32:, :32]
    x2 = jnp.concatenate([taper * s_re, taper * s_im], axis=1)
    centred = jnp.arange(32, dtype=jnp.float32) - 16.0
    angle = -2.0 * math.pi * centred[:, None] * centred[None, :] / 32.0
    f_re, f_im = (jnp.cos(angle), jnp.sin(angle))
    hp = lax.Precision.HIGHEST
    left = jnp.concatenate(
        [jnp.concatenate([f_re, -f_im], 1), jnp.concatenate([f_im, f_re], 1)], 0
    )
    y2 = jnp.einsum("ij,bjq->biq", left, x2, precision=hp)
    ycat = jnp.concatenate([y2[:, :32], y2[:, 32:]], axis=2)
    right = jnp.concatenate(
        [jnp.concatenate([f_re, f_im], 1), jnp.concatenate([-f_im, f_re], 1)], 0
    )
    z2 = jnp.einsum("baj,jk->bak", ycat, right, precision=hp)
    z = z2.reshape(z2.shape[0], 32, 2, 32).transpose(0, 2, 1, 3)
    return (z / 32.0).astype(jnp.bfloat16)


def taylor_weights(chan_local, freq_pos, channels):
    global_chan = (freq_pos * CH_DEV + chan_local).astype(jnp.float32)
    xval = (2.0 * global_chan + 1.0 - channels) / channels
    powers = jnp.arange(NT, dtype=jnp.float32)
    return jnp.where(powers[None, :] == 0.0, 1.0, xval[:, None] ** powers[None, :])


def place_block(tile_acc, inputs):
    patch_b, weight_b, rows_b, cols_b = inputs
    hp = lax.Precision.HIGHEST
    cells = jnp.arange(TILE, dtype=jnp.int32)
    small = jnp.arange(32, dtype=jnp.int32)
    row_hot = (cells[None, :, None] == rows_b[:, None, None] + small[None, None, :]).astype(
        jnp.float32
    )
    col_hot = (cells[None, :, None] == cols_b[:, None, None] + small[None, None, :]).astype(
        jnp.float32
    )
    spread = jnp.einsum("scab,sQb->scaQ", patch_b.astype(jnp.float32), col_hot, precision=hp)
    terms = []
    for term in range(NT):
        weighted = spread * weight_b[:, term][:, None, None, None]
        terms.append(jnp.einsum("sRa,scaQ->cRQ", row_hot, weighted, precision=hp))
    return (tile_acc + jnp.stack(terms, 0), None)


def body(visibilities, coords, vis_counts, cover_tile, offsets, channel, taper):
    n_span = lax.axis_size("span")
    n_freq = lax.axis_size("freq")
    channels = CH_DEV * n_freq
    freq_pos = lax.axis_index("freq")
    sub_count = visibilities.shape[1]
    groups = sub_count // 32
    vis_loc = visibilities[0].reshape(groups, 32, 2, -1)
    coord_loc = coords[0].reshape(groups, 32, 2, -1)
    count_loc = vis_counts[0].reshape(groups, 32)

    def block_work(inputs):
        return make_subgrids(inputs[0], inputs[1], inputs[2], taper)

    patches = lax.map(block_work, (vis_loc, coord_loc, count_loc)).reshape(sub_count, 2, 32, 32)
    dest = cover_tile[0, :, 0]
    row_off = offsets[0, :, 0]
    col_off = offsets[0, :, 1]
    chan_loc = channel[0]
    cap = 2 * sub_count // n_span
    onehot = (dest[:, None] == jnp.arange(n_span, dtype=jnp.int32)[None, :]).astype(jnp.float32)
    order = jnp.arange(sub_count, dtype=jnp.int32)
    lower = (order[:, None] > order[None, :]).astype(jnp.float32)
    earlier = jnp.dot(lower, onehot, preferred_element_type=jnp.float32)
    rank = jnp.sum(earlier * onehot, axis=1).astype(jnp.int32)
    slot = dest * cap + rank
    payload = (
        jnp.zeros((n_span * cap, 2048), jnp.bfloat16).at[slot].set(patches.reshape(sub_count, 2048))
    )
    info = jnp.stack([jnp.ones_like(dest), row_off, col_off, chan_loc], 1).astype(jnp.bfloat16)
    meta = jnp.zeros((n_span * cap, 4), jnp.bfloat16).at[slot].set(info)
    got_payload, got_meta = sent_together(
        (payload.reshape(n_span, cap, 2048), meta.reshape(n_span, cap, 4)), "span", 0, 0, 2
    )
    slots = n_span * cap
    got_meta = got_meta.reshape(slots, 4).astype(jnp.int32)
    valid = got_meta[:, 0].astype(jnp.float32)
    weight = taylor_weights(got_meta[:, 3], freq_pos, channels) * valid[:, None]
    blocks = slots // 32
    inputs = (
        got_payload.reshape(blocks, 32, 2, 32, 32),
        weight.reshape(blocks, 32, NT),
        got_meta[:, 1].reshape(blocks, 32),
        got_meta[:, 2].reshape(blocks, 32),
    )
    start_tile = jnp.zeros((NT, 2, TILE, TILE), jnp.float32)
    local, _ = lax.scan(place_block, start_tile, inputs)
    local = local.reshape(NT, 1, 2, TILE, TILE)
    total = gathered_total(local, "freq")
    scale = TILE / (32.0 * math.sqrt(n_freq * sub_count))
    return total * scale


def solution(mesh):
    return jax.shard_map(
        body,
        mesh=mesh,
        in_specs=(
            P("freq", "span", None, None),
            P("freq", "span", None, None),
            P("freq", "span"),
            P("freq", "span", None),
            P("freq", "span", None),
            P("freq", "span"),
            P(),
        ),
        out_specs=P(None, "span", None, None, None),
        check_vma=False,
    )
```

```python
import math

import jax
import jax.numpy as jnp
from jax import lax
from jax.sharding import PartitionSpec as P

TILE = 128
NT = 2
CH_DEV = 16


def sent_together(arrays, axis, split_dim, concat_dim, along):
    widths = [a.shape[along] for a in arrays]
    both = jnp.concatenate(arrays, axis=along)
    whole = lax.all_to_all(both, axis, split_axis=split_dim, concat_axis=concat_dim, tiled=True)
    return tuple(jnp.split(whole, [sum(widths[:k]) for k in range(1, len(widths))], axis=along))


def gathered_total(shard, axis):
    n = lax.axis_size(axis)
    flat = shard.reshape(-1)
    size = flat.shape[0]
    per = -(-size // (n * 128)) * 128
    flat = jnp.pad(flat, (0, per * n - size))
    got = lax.all_to_all(flat.reshape(n, per), axis, 0, 0, tiled=True)
    part = got.sum(axis=0)
    spread = jnp.broadcast_to(part[None], (n, per))
    whole = lax.all_to_all(spread, axis, 0, 0, tiled=True)
    return whole.reshape(-1)[:size].reshape(shard.shape)


def cmul(ar, ai, br, bi):
    return ar * br - ai * bi, ar * bi + ai * br


def bit_powers(c, s, bits, first, count):
    j = jnp.arange(count, dtype=jnp.int32)[None, :, None]
    re = jnp.broadcast_to(first[0][:, None, :], (c.shape[0], count, c.shape[1]))
    im = jnp.broadcast_to(first[1][:, None, :], (c.shape[0], count, c.shape[1]))
    for i, (br, bi) in enumerate(bits):
        on = ((j >> i) & 1) == 1
        mr, mi = cmul(re, im, br[:, None, :], bi[:, None, :])
        re, im = jnp.where(on, mr, re), jnp.where(on, mi, im)
    return re, im


def phase_table(angle, vis=None):
    c, s = jnp.cos(angle), jnp.sin(angle)
    w2 = cmul(c, s, c, s)
    w4 = cmul(*w2, *w2)
    w8 = cmul(*w4, *w4)
    w16 = cmul(*w8, *w8)
    lo = (w16[0], -w16[1])
    if vis is not None:
        lo = cmul(vis[0], vis[1], *lo)
    one = (jnp.ones_like(c), jnp.zeros_like(c))
    small = bit_powers(c, s, [(c, s), w2], one, 4)
    big = bit_powers(c, s, [w4, w8, w16], lo, 8)
    small, big = lax.optimization_barrier((small, big))
    re, im = cmul(big[0][:, :, None, :], big[1][:, :, None, :], small[0][:, None], small[1][:, None])
    n = c.shape[0]
    return re.reshape(n, 32, -1), im.reshape(n, 32, -1)


def make_subgrids(vis_b, coord_b, count_b, taper):
    kk = vis_b.shape[-1]
    live = (jnp.arange(kk, dtype=jnp.int32)[None, :] < count_b[:, None]).astype(jnp.float32)
    scale_k = 1.0 / math.sqrt(kk)
    vis_re = vis_b[:, 0, :].astype(jnp.float32) * live * scale_k
    vis_im = vis_b[:, 1, :].astype(jnp.float32) * live * scale_k
    step = -2.0 * math.pi / 32.0
    bf = jnp.bfloat16
    a_re, a_im = phase_table(step * coord_b[:, 0, :])
    b_re, b_im = phase_table(step * coord_b[:, 1, :], (vis_re, vis_im))
    a_t = jnp.concatenate([a_re, a_im], axis=1).astype(bf)
    b_t = jnp.concatenate([b_re, b_im], axis=1).astype(bf)
    a_t, b_t = lax.optimization_barrier((a_t, b_t))
    f32 = jnp.float32
    s_all = jnp.einsum("bik,bjk->bij", a_t, b_t, preferred_element_type=f32)
    s_re = s_all[:, :32, :32] - s_all[:, 32:, 32:]
    s_im = s_all[:, :32, 32:] + s_all[:, 32:, :32]
    x2 = jnp.concatenate([taper * s_re, taper * s_im], axis=1)
    centred = jnp.arange(32, dtype=jnp.float32) - 16.0
    angle = -2.0 * math.pi * centred[:, None] * centred[None, :] / 32.0
    f_re, f_im = (jnp.cos(angle), jnp.sin(angle))
    hp = lax.Precision.HIGHEST
    left = jnp.concatenate(
        [jnp.concatenate([f_re, -f_im], 1), jnp.concatenate([f_im, f_re], 1)], 0
    )
    y2 = jnp.einsum("ij,bjq->biq", left, x2, precision=hp)
    ycat = jnp.concatenate([y2[:, :32], y2[:, 32:]], axis=2)
    right = jnp.concatenate(
        [jnp.concatenate([f_re, f_im], 1), jnp.concatenate([-f_im, f_re], 1)], 0
    )
    z2 = jnp.einsum("baj,jk->bak", ycat, right, precision=hp)
    z = z2.reshape(z2.shape[0], 32, 2, 32).transpose(0, 2, 1, 3)
    return (z / 32.0).astype(jnp.bfloat16)


def taylor_weights(chan_local, freq_pos, channels):
    global_chan = (freq_pos * CH_DEV + chan_local).astype(jnp.float32)
    xval = (2.0 * global_chan + 1.0 - channels) / channels
    powers = jnp.arange(NT, dtype=jnp.float32)
    return jnp.where(powers[None, :] == 0.0, 1.0, xval[:, None] ** powers[None, :])


def place_block(tile_acc, inputs):
    patch_b, weight_b, rows_b, cols_b = inputs
    hp = lax.Precision.HIGHEST
    cells = jnp.arange(TILE, dtype=jnp.int32)
    small = jnp.arange(32, dtype=jnp.int32)
    row_hot = (cells[None, :, None] == rows_b[:, None, None] + small[None, None, :]).astype(
        jnp.float32
    )
    col_hot = (cells[None, :, None] == cols_b[:, None, None] + small[None, None, :]).astype(
        jnp.float32
    )
    spread = jnp.einsum("scab,sQb->scaQ", patch_b.astype(jnp.float32), col_hot, precision=hp)
    terms = []
    for term in range(NT):
        weighted = spread * weight_b[:, term][:, None, None, None]
        terms.append(jnp.einsum("sRa,scaQ->cRQ", row_hot, weighted, precision=hp))
    return (tile_acc + jnp.stack(terms, 0), None)


def body(visibilities, coords, vis_counts, cover_tile, offsets, channel, taper):
    n_span = lax.axis_size("span")
    n_freq = lax.axis_size("freq")
    channels = CH_DEV * n_freq
    freq_pos = lax.axis_index("freq")
    sub_count = visibilities.shape[1]
    groups = sub_count // 32
    vis_loc = visibilities[0].reshape(groups, 32, 2, -1)
    coord_loc = coords[0].reshape(groups, 32, 2, -1)
    count_loc = vis_counts[0].reshape(groups, 32)

    def block_work(inputs):
        return make_subgrids(inputs[0], inputs[1], inputs[2], taper)

    patches = lax.map(block_work, (vis_loc, coord_loc, count_loc)).reshape(sub_count, 2, 32, 32)
    dest = cover_tile[0, :, 0]
    row_off = offsets[0, :, 0]
    col_off = offsets[0, :, 1]
    chan_loc = channel[0]
    cap = 2 * sub_count // n_span
    onehot = (dest[:, None] == jnp.arange(n_span, dtype=jnp.int32)[None, :]).astype(jnp.float32)
    order = jnp.arange(sub_count, dtype=jnp.int32)
    lower = (order[:, None] > order[None, :]).astype(jnp.float32)
    earlier = jnp.dot(lower, onehot, preferred_element_type=jnp.float32)
    rank = jnp.sum(earlier * onehot, axis=1).astype(jnp.int32)
    slot = dest * cap + rank
    payload = (
        jnp.zeros((n_span * cap, 2048), jnp.bfloat16).at[slot].set(patches.reshape(sub_count, 2048))
    )
    info = jnp.stack([jnp.ones_like(dest), row_off, col_off, chan_loc], 1).astype(jnp.bfloat16)
    meta = jnp.zeros((n_span * cap, 4), jnp.bfloat16).at[slot].set(info)
    got_payload, got_meta = sent_together(
        (payload.reshape(n_span, cap, 2048), meta.reshape(n_span, cap, 4)), "span", 0, 0, 2
    )
    slots = n_span * cap
    got_meta = got_meta.reshape(slots, 4).astype(jnp.int32)
    valid = got_meta[:, 0].astype(jnp.float32)
    weight = taylor_weights(got_meta[:, 3], freq_pos, channels) * valid[:, None]
    blocks = slots // 32
    inputs = (
        got_payload.reshape(blocks, 32, 2, 32, 32),
        weight.reshape(blocks, 32, NT),
        got_meta[:, 1].reshape(blocks, 32),
        got_meta[:, 2].reshape(blocks, 32),
    )
    start_tile = jnp.zeros((NT, 2, TILE, TILE), jnp.float32)
    local, _ = lax.scan(place_block, start_tile, inputs)
    local = local.reshape(NT, 1, 2, TILE, TILE)
    total = gathered_total(local, "freq")
    scale = TILE / (32.0 * math.sqrt(n_freq * sub_count))
    return total * scale


def solution(mesh):
    return jax.shard_map(
        body,
        mesh=mesh,
        in_specs=(
            P("freq", "span", None, None),
            P("freq", "span", None, None),
            P("freq", "span"),
            P("freq", "span", None),
            P("freq", "span", None),
            P("freq", "span"),
            P(),
        ),
        out_specs=P(None, "span", None, None, None),
        check_vma=False,
    )
```

```python
import math

import jax
import jax.numpy as jnp
from jax import lax
from jax.sharding import PartitionSpec as P

TILE = 128
NT = 2
CH_DEV = 16


def sent_together(arrays, axis, split_dim, concat_dim, along):
    widths = [a.shape[along] for a in arrays]
    both = jnp.concatenate(arrays, axis=along)
    whole = lax.all_to_all(both, axis, split_axis=split_dim, concat_axis=concat_dim, tiled=True)
    return tuple(jnp.split(whole, [sum(widths[:k]) for k in range(1, len(widths))], axis=along))


def gathered_total(shard, axis):
    n = lax.axis_size(axis)
    flat = shard.reshape(-1)
    size = flat.shape[0]
    per = -(-size // (n * 128)) * 128
    flat = jnp.pad(flat, (0, per * n - size))
    got = lax.all_to_all(flat.reshape(n, per // 128, 128), axis, 0, 0, tiled=True)
    part = got.sum(axis=0)
    spread = jnp.broadcast_to(part[None], (n, per // 128, 128))
    whole = lax.all_to_all(spread, axis, 0, 0, tiled=True)
    return whole.reshape(-1)[:size].reshape(shard.shape)


def cmul(ar, ai, br, bi):
    return ar * br - ai * bi, ar * bi + ai * br


def bit_powers(c, s, bits, first, count):
    j = jnp.arange(count, dtype=jnp.int32)[None, :, None]
    re = jnp.broadcast_to(first[0][:, None, :], (c.shape[0], count, c.shape[1]))
    im = jnp.broadcast_to(first[1][:, None, :], (c.shape[0], count, c.shape[1]))
    for i, (br, bi) in enumerate(bits):
        on = ((j >> i) & 1) == 1
        mr, mi = cmul(re, im, br[:, None, :], bi[:, None, :])
        re, im = jnp.where(on, mr, re), jnp.where(on, mi, im)
    return re, im


def phase_table(angle, vis=None):
    c, s = jnp.cos(angle), jnp.sin(angle)
    w2 = cmul(c, s, c, s)
    w4 = cmul(*w2, *w2)
    w8 = cmul(*w4, *w4)
    w16 = cmul(*w8, *w8)
    lo = (w16[0], -w16[1])
    if vis is not None:
        lo = cmul(vis[0], vis[1], *lo)
    one = (jnp.ones_like(c), jnp.zeros_like(c))
    small = bit_powers(c, s, [(c, s), w2], one, 4)
    big = bit_powers(c, s, [w4, w8, w16], lo, 8)
    small, big = lax.optimization_barrier((small, big))
    re, im = cmul(big[0][:, :, None, :], big[1][:, :, None, :], small[0][:, None], small[1][:, None])
    n = c.shape[0]
    return re.reshape(n, 32, -1), im.reshape(n, 32, -1)


def make_subgrids(vis_b, coord_b, count_b, taper):
    kk = vis_b.shape[-1]
    live = (jnp.arange(kk, dtype=jnp.int32)[None, :] < count_b[:, None]).astype(jnp.float32)
    scale_k = 1.0 / math.sqrt(kk)
    vis_re = vis_b[:, 0, :].astype(jnp.float32) * live * scale_k
    vis_im = vis_b[:, 1, :].astype(jnp.float32) * live * scale_k
    step = -2.0 * math.pi / 32.0
    bf = jnp.bfloat16
    a_re, a_im = phase_table(step * coord_b[:, 0, :])
    b_re, b_im = phase_table(step * coord_b[:, 1, :], (vis_re, vis_im))
    a_t = jnp.concatenate([a_re, a_im], axis=1).astype(bf)
    b_t = jnp.concatenate([b_re, b_im], axis=1).astype(bf)
    a_t, b_t = lax.optimization_barrier((a_t, b_t))
    f32 = jnp.float32
    s_all = jnp.einsum("bik,bjk->bij", a_t, b_t, preferred_element_type=f32)
    s_re = s_all[:, :32, :32] - s_all[:, 32:, 32:]
    s_im = s_all[:, :32, 32:] + s_all[:, 32:, :32]
    x2 = jnp.concatenate([taper * s_re, taper * s_im], axis=1)
    centred = jnp.arange(32, dtype=jnp.float32) - 16.0
    angle = -2.0 * math.pi * centred[:, None] * centred[None, :] / 32.0
    f_re, f_im = (jnp.cos(angle), jnp.sin(angle))
    hp = lax.Precision.HIGHEST
    left = jnp.concatenate(
        [jnp.concatenate([f_re, -f_im], 1), jnp.concatenate([f_im, f_re], 1)], 0
    )
    y2 = jnp.einsum("ij,bjq->biq", left, x2, precision=hp)
    ycat = jnp.concatenate([y2[:, :32], y2[:, 32:]], axis=2)
    right = jnp.concatenate(
        [jnp.concatenate([f_re, f_im], 1), jnp.concatenate([-f_im, f_re], 1)], 0
    )
    z2 = jnp.einsum("baj,jk->bak", ycat, right, precision=hp)
    z = z2.reshape(z2.shape[0], 32, 2, 32).transpose(0, 2, 1, 3)
    return (z / 32.0).astype(jnp.bfloat16)


def taylor_weights(chan_local, freq_pos, channels):
    global_chan = (freq_pos * CH_DEV + chan_local).astype(jnp.float32)
    xval = (2.0 * global_chan + 1.0 - channels) / channels
    powers = jnp.arange(NT, dtype=jnp.float32)
    return jnp.where(powers[None, :] == 0.0, 1.0, xval[:, None] ** powers[None, :])


def place_block(tile_acc, inputs):
    patch_b, weight_b, rows_b, cols_b = inputs
    hp = lax.Precision.HIGHEST
    cells = jnp.arange(TILE, dtype=jnp.int32)
    small = jnp.arange(32, dtype=jnp.int32)
    row_hot = (cells[None, :, None] == rows_b[:, None, None] + small[None, None, :]).astype(
        jnp.float32
    )
    col_hot = (cells[None, :, None] == cols_b[:, None, None] + small[None, None, :]).astype(
        jnp.float32
    )
    spread = jnp.einsum("scab,sQb->scaQ", patch_b.astype(jnp.float32), col_hot, precision=hp)
    terms = []
    for term in range(NT):
        weighted = spread * weight_b[:, term][:, None, None, None]
        terms.append(jnp.einsum("sRa,scaQ->cRQ", row_hot, weighted, precision=hp))
    return (tile_acc + jnp.stack(terms, 0), None)


def body(visibilities, coords, vis_counts, cover_tile, offsets, channel, taper):
    n_span = lax.axis_size("span")
    n_freq = lax.axis_size("freq")
    channels = CH_DEV * n_freq
    freq_pos = lax.axis_index("freq")
    sub_count = visibilities.shape[1]
    groups = sub_count // 32
    vis_loc = visibilities[0].reshape(groups, 32, 2, -1)
    coord_loc = coords[0].reshape(groups, 32, 2, -1)
    count_loc = vis_counts[0].reshape(groups, 32)

    def block_work(inputs):
        return make_subgrids(inputs[0], inputs[1], inputs[2], taper)

    patches = lax.map(block_work, (vis_loc, coord_loc, count_loc)).reshape(sub_count, 2, 32, 32)
    dest = cover_tile[0, :, 0]
    row_off = offsets[0, :, 0]
    col_off = offsets[0, :, 1]
    chan_loc = channel[0]
    cap = 2 * sub_count // n_span
    onehot = (dest[:, None] == jnp.arange(n_span, dtype=jnp.int32)[None, :]).astype(jnp.float32)
    order = jnp.arange(sub_count, dtype=jnp.int32)
    lower = (order[:, None] > order[None, :]).astype(jnp.float32)
    earlier = jnp.dot(lower, onehot, preferred_element_type=jnp.float32)
    rank = jnp.sum(earlier * onehot, axis=1).astype(jnp.int32)
    slot = dest * cap + rank
    payload = (
        jnp.zeros((n_span * cap, 2048), jnp.bfloat16).at[slot].set(patches.reshape(sub_count, 2048))
    )
    info = jnp.stack([jnp.ones_like(dest), row_off, col_off, chan_loc], 1).astype(jnp.bfloat16)
    meta = jnp.zeros((n_span * cap, 4), jnp.bfloat16).at[slot].set(info)
    got_payload, got_meta = sent_together(
        (payload.reshape(n_span, cap, 2048), meta.reshape(n_span, cap, 4)), "span", 0, 0, 2
    )
    slots = n_span * cap
    got_meta = got_meta.reshape(slots, 4).astype(jnp.int32)
    valid = got_meta[:, 0].astype(jnp.float32)
    weight = taylor_weights(got_meta[:, 3], freq_pos, channels) * valid[:, None]
    blocks = slots // 32
    inputs = (
        got_payload.reshape(blocks, 32, 2, 32, 32),
        weight.reshape(blocks, 32, NT),
        got_meta[:, 1].reshape(blocks, 32),
        got_meta[:, 2].reshape(blocks, 32),
    )
    start_tile = jnp.zeros((NT, 2, TILE, TILE), jnp.float32)
    local, _ = lax.scan(place_block, start_tile, inputs)
    local = local.reshape(NT, 1, 2, TILE, TILE)
    total = gathered_total(local, "freq")
    scale = TILE / (32.0 * math.sqrt(n_freq * sub_count))
    return total * scale


def solution(mesh):
    return jax.shard_map(
        body,
        mesh=mesh,
        in_specs=(
            P("freq", "span", None, None),
            P("freq", "span", None, None),
            P("freq", "span"),
            P("freq", "span", None),
            P("freq", "span", None),
            P("freq", "span"),
            P(),
        ),
        out_specs=P(None, "span", None, None, None),
        check_vma=False,
    )
```

```python
import math

import jax
import jax.numpy as jnp
from jax import lax
from jax.sharding import PartitionSpec as P

TILE = 128
NT = 2
CH_DEV = 16


def sent_together(arrays, axis, split_dim, concat_dim, along):
    widths = [a.shape[along] for a in arrays]
    both = jnp.concatenate(arrays, axis=along)
    whole = lax.all_to_all(both, axis, split_axis=split_dim, concat_axis=concat_dim, tiled=True)
    return tuple(jnp.split(whole, [sum(widths[:k]) for k in range(1, len(widths))], axis=along))


def gathered_total(shard, axis):
    n = lax.axis_size(axis)
    flat = shard.reshape(-1)
    size = flat.shape[0]
    per = -(-size // (n * 128)) * 128
    flat = jnp.pad(flat, (0, per * n - size))
    got = lax.all_to_all(flat.reshape(n, per // 128, 128), axis, 0, 0, tiled=True)
    part = got.sum(axis=0)
    spread = jnp.broadcast_to(part[None], (n, per // 128, 128))
    whole = lax.all_to_all(spread, axis, 0, 0, tiled=True)
    return whole.reshape(-1)[:size].reshape(shard.shape)


def cmul(ar, ai, br, bi):
    return ar * br - ai * bi, ar * bi + ai * br


def bit_powers(c, s, bits, first, count):
    j = jnp.arange(count, dtype=jnp.int32)[None, :, None]
    re = jnp.broadcast_to(first[0][:, None, :], (c.shape[0], count, c.shape[1]))
    im = jnp.broadcast_to(first[1][:, None, :], (c.shape[0], count, c.shape[1]))
    for i, (br, bi) in enumerate(bits):
        on = ((j >> i) & 1) == 1
        mr, mi = cmul(re, im, br[:, None, :], bi[:, None, :])
        re, im = jnp.where(on, mr, re), jnp.where(on, mi, im)
    return re, im


def phase_table(angle, vis=None):
    c, s = jnp.cos(angle), jnp.sin(angle)
    w2 = cmul(c, s, c, s)
    w4 = cmul(*w2, *w2)
    w8 = cmul(*w4, *w4)
    w16 = cmul(*w8, *w8)
    lo = (w16[0], -w16[1])
    if vis is not None:
        lo = cmul(vis[0], vis[1], *lo)
    one = (jnp.ones_like(c), jnp.zeros_like(c))
    small = bit_powers(c, s, [(c, s), w2], one, 4)
    big = bit_powers(c, s, [w4, w8, w16], lo, 8)
    small, big = lax.optimization_barrier((small, big))
    re, im = cmul(big[0][:, :, None, :], big[1][:, :, None, :], small[0][:, None], small[1][:, None])
    n = c.shape[0]
    return re.reshape(n, 32, -1), im.reshape(n, 32, -1)


def make_subgrids(vis_b, coord_b, count_b, taper):
    kk = vis_b.shape[-1]
    live = (jnp.arange(kk, dtype=jnp.int32)[None, :] < count_b[:, None]).astype(jnp.float32)
    scale_k = 1.0 / math.sqrt(kk)
    vis_re = vis_b[:, 0, :].astype(jnp.float32) * live * scale_k
    vis_im = vis_b[:, 1, :].astype(jnp.float32) * live * scale_k
    step = -2.0 * math.pi / 32.0
    bf = jnp.bfloat16
    a_re, a_im = phase_table(step * coord_b[:, 0, :])
    b_re, b_im = phase_table(step * coord_b[:, 1, :], (vis_re, vis_im))
    a_t = jnp.concatenate([a_re, a_im], axis=1).astype(bf)
    b_t = jnp.concatenate([b_re, b_im], axis=1).astype(bf)
    f32 = jnp.float32
    s_all = jnp.einsum("bik,bjk->bij", a_t, b_t, preferred_element_type=f32)
    s_re = s_all[:, :32, :32] - s_all[:, 32:, 32:]
    s_im = s_all[:, :32, 32:] + s_all[:, 32:, :32]
    x2 = jnp.concatenate([taper * s_re, taper * s_im], axis=1)
    centred = jnp.arange(32, dtype=jnp.float32) - 16.0
    angle = -2.0 * math.pi * centred[:, None] * centred[None, :] / 32.0
    f_re, f_im = (jnp.cos(angle), jnp.sin(angle))
    hp = lax.Precision.HIGHEST
    left = jnp.concatenate(
        [jnp.concatenate([f_re, -f_im], 1), jnp.concatenate([f_im, f_re], 1)], 0
    )
    y2 = jnp.einsum("ij,bjq->biq", left, x2, precision=hp)
    ycat = jnp.concatenate([y2[:, :32], y2[:, 32:]], axis=2)
    right = jnp.concatenate(
        [jnp.concatenate([f_re, f_im], 1), jnp.concatenate([-f_im, f_re], 1)], 0
    )
    z2 = jnp.einsum("baj,jk->bak", ycat, right, precision=hp)
    z = z2.reshape(z2.shape[0], 32, 2, 32).transpose(0, 2, 1, 3)
    return (z / 32.0).astype(jnp.bfloat16)


def taylor_weights(chan_local, freq_pos, channels):
    global_chan = (freq_pos * CH_DEV + chan_local).astype(jnp.float32)
    xval = (2.0 * global_chan + 1.0 - channels) / channels
    powers = jnp.arange(NT, dtype=jnp.float32)
    return jnp.where(powers[None, :] == 0.0, 1.0, xval[:, None] ** powers[None, :])


def place_all(patch, weight, rows, cols):
    bf, f32 = jnp.bfloat16, jnp.float32
    cells = jnp.arange(TILE, dtype=jnp.int32)
    small = jnp.arange(32, dtype=jnp.int32)
    col_hot = (small[None, :, None] + cols[:, None, None] == cells[None, None, :]).astype(bf)
    spread = jnp.einsum("scab,sbq->scaq", patch, col_hot, preferred_element_type=f32).astype(bf)
    row_hot = (cells[None, :, None] == rows[:, None, None] + small[None, None, :]).astype(f32)
    w_hi = weight.astype(bf)
    w_lo = (weight - w_hi.astype(f32)).astype(bf)
    w_both = jnp.stack([w_hi, w_lo], 0).astype(f32)
    lhs = (w_both.transpose(0, 2, 1)[:, :, None, :, None] * row_hot.transpose(1, 0, 2)[None, None]).astype(bf)
    out = jnp.einsum("htrsa,scaq->htcrq", lhs, spread, preferred_element_type=f32)
    return out[0] + out[1]


def body(visibilities, coords, vis_counts, cover_tile, offsets, channel, taper):
    n_span = lax.axis_size("span")
    n_freq = lax.axis_size("freq")
    channels = CH_DEV * n_freq
    freq_pos = lax.axis_index("freq")
    sub_count = visibilities.shape[1]
    groups = sub_count // 32
    vis_loc = visibilities[0].reshape(groups, 32, 2, -1)
    coord_loc = coords[0].reshape(groups, 32, 2, -1)
    count_loc = vis_counts[0].reshape(groups, 32)

    def block_work(inputs):
        return make_subgrids(inputs[0], inputs[1], inputs[2], taper)

    patches = lax.map(block_work, (vis_loc, coord_loc, count_loc)).reshape(sub_count, 2, 32, 32)
    dest = cover_tile[0, :, 0]
    row_off = offsets[0, :, 0]
    col_off = offsets[0, :, 1]
    chan_loc = channel[0]
    cap = 2 * sub_count // n_span
    onehot = (dest[:, None] == jnp.arange(n_span, dtype=jnp.int32)[None, :]).astype(jnp.float32)
    order = jnp.arange(sub_count, dtype=jnp.int32)
    lower = (order[:, None] > order[None, :]).astype(jnp.float32)
    earlier = jnp.dot(lower, onehot, preferred_element_type=jnp.float32)
    rank = jnp.sum(earlier * onehot, axis=1).astype(jnp.int32)
    slot = dest * cap + rank
    payload = (
        jnp.zeros((n_span * cap, 2048), jnp.bfloat16).at[slot].set(patches.reshape(sub_count, 2048))
    )
    info = jnp.stack([jnp.ones_like(dest), row_off, col_off, chan_loc], 1).astype(jnp.bfloat16)
    meta = jnp.zeros((n_span * cap, 4), jnp.bfloat16).at[slot].set(info)
    got_payload, got_meta = sent_together(
        (payload.reshape(n_span, cap, 2048), meta.reshape(n_span, cap, 4)), "span", 0, 0, 2
    )
    slots = n_span * cap
    got_meta = got_meta.reshape(slots, 4).astype(jnp.int32)
    valid = got_meta[:, 0].astype(jnp.float32)
    weight = taylor_weights(got_meta[:, 3], freq_pos, channels) * valid[:, None]
    local = place_all(
        got_payload.reshape(slots, 2, 32, 32), weight, got_meta[:, 1], got_meta[:, 2]
    )
    local = local.reshape(NT, 1, 2, TILE, TILE)
    total = gathered_total(local, "freq")
    scale = TILE / (32.0 * math.sqrt(n_freq * sub_count))
    return total * scale


def solution(mesh):
    return jax.shard_map(
        body,
        mesh=mesh,
        in_specs=(
            P("freq", "span", None, None),
            P("freq", "span", None, None),
            P("freq", "span"),
            P("freq", "span", None),
            P("freq", "span", None),
            P("freq", "span"),
            P(),
        ),
        out_specs=P(None, "span", None, None, None),
        check_vma=False,
    )
```

```python
import math

import jax
import jax.numpy as jnp
from jax import lax
from jax.sharding import PartitionSpec as P

TILE = 128
NT = 2
CH_DEV = 16


def sent_together(arrays, axis, split_dim, concat_dim, along):
    widths = [a.shape[along] for a in arrays]
    both = jnp.concatenate(arrays, axis=along)
    whole = lax.all_to_all(both, axis, split_axis=split_dim, concat_axis=concat_dim, tiled=True)
    return tuple(jnp.split(whole, [sum(widths[:k]) for k in range(1, len(widths))], axis=along))


def gathered_total(shard, axis):
    n = lax.axis_size(axis)
    flat = shard.reshape(-1)
    size = flat.shape[0]
    per = -(-size // (n * 128)) * 128
    flat = jnp.pad(flat, (0, per * n - size))
    got = lax.all_to_all(flat.reshape(n, per // 128, 128), axis, 0, 0, tiled=True)
    part = got.sum(axis=0)
    spread = jnp.broadcast_to(part[None], (n, per // 128, 128))
    whole = lax.all_to_all(spread, axis, 0, 0, tiled=True)
    return whole.reshape(-1)[:size].reshape(shard.shape)


def cmul(ar, ai, br, bi):
    return ar * br - ai * bi, ar * bi + ai * br


def bit_powers(c, s, bits, first, count):
    j = jnp.arange(count, dtype=jnp.int32)[None, :, None]
    re = jnp.broadcast_to(first[0][:, None, :], (c.shape[0], count, c.shape[1]))
    im = jnp.broadcast_to(first[1][:, None, :], (c.shape[0], count, c.shape[1]))
    for i, (br, bi) in enumerate(bits):
        on = ((j >> i) & 1) == 1
        mr, mi = cmul(re, im, br[:, None, :], bi[:, None, :])
        re, im = jnp.where(on, mr, re), jnp.where(on, mi, im)
    return re, im


def phase_table(angle, vis=None):
    c, s = jnp.cos(angle), jnp.sin(angle)
    w2 = cmul(c, s, c, s)
    w4 = cmul(*w2, *w2)
    w8 = cmul(*w4, *w4)
    w16 = cmul(*w8, *w8)
    lo = (w16[0], -w16[1])
    if vis is not None:
        lo = cmul(vis[0], vis[1], *lo)
    one = (jnp.ones_like(c), jnp.zeros_like(c))
    small = bit_powers(c, s, [(c, s), w2], one, 4)
    big = bit_powers(c, s, [w4, w8, w16], lo, 8)
    small, big = lax.optimization_barrier((small, big))
    qr, qi = big[0][:, None, :, None, :], big[1][:, None, :, None, :]
    pr, pi = small[0][:, None, None], small[1][:, None, None]
    part = lax.broadcasted_iota(jnp.int32, (1, 2, 1, 1, 1), 1)
    table = jnp.where(part == 0, qr * pr - qi * pi, qr * pi + qi * pr)
    n = c.shape[0]
    return table.reshape(n, 64, -1)


def make_subgrids(vis_b, coord_b, count_b, taper):
    kk = vis_b.shape[-1]
    live = (jnp.arange(kk, dtype=jnp.int32)[None, :] < count_b[:, None]).astype(jnp.float32)
    scale_k = 1.0 / math.sqrt(kk)
    vis_re = vis_b[:, 0, :].astype(jnp.float32) * live * scale_k
    vis_im = vis_b[:, 1, :].astype(jnp.float32) * live * scale_k
    step = -2.0 * math.pi / 32.0
    bf = jnp.bfloat16
    a_t = phase_table(step * coord_b[:, 0, :]).astype(bf)
    b_t = phase_table(step * coord_b[:, 1, :], (vis_re, vis_im)).astype(bf)
    f32 = jnp.float32
    s_all = jnp.einsum("bik,bjk->bij", a_t, b_t, preferred_element_type=f32)
    s_re = s_all[:, :32, :32] - s_all[:, 32:, 32:]
    s_im = s_all[:, :32, 32:] + s_all[:, 32:, :32]
    x2 = jnp.concatenate([taper * s_re, taper * s_im], axis=1)
    centred = jnp.arange(32, dtype=jnp.float32) - 16.0
    angle = -2.0 * math.pi * centred[:, None] * centred[None, :] / 32.0
    f_re, f_im = (jnp.cos(angle), jnp.sin(angle))
    hp = lax.Precision.HIGHEST
    left = jnp.concatenate(
        [jnp.concatenate([f_re, -f_im], 1), jnp.concatenate([f_im, f_re], 1)], 0
    )
    y2 = jnp.einsum("ij,bjq->biq", left, x2, precision=hp)
    ycat = jnp.concatenate([y2[:, :32], y2[:, 32:]], axis=2)
    right = jnp.concatenate(
        [jnp.concatenate([f_re, f_im], 1), jnp.concatenate([-f_im, f_re], 1)], 0
    )
    z2 = jnp.einsum("baj,jk->bak", ycat, right, precision=hp)
    z = z2.reshape(z2.shape[0], 32, 2, 32).transpose(0, 2, 1, 3)
    return (z / 32.0).astype(jnp.bfloat16)


def taylor_weights(chan_local, freq_pos, channels):
    global_chan = (freq_pos * CH_DEV + chan_local).astype(jnp.float32)
    xval = (2.0 * global_chan + 1.0 - channels) / channels
    powers = jnp.arange(NT, dtype=jnp.float32)
    return jnp.where(powers[None, :] == 0.0, 1.0, xval[:, None] ** powers[None, :])


def place_all(patch, weight, rows, cols):
    bf, f32 = jnp.bfloat16, jnp.float32
    cells = jnp.arange(TILE, dtype=jnp.int32)
    small = jnp.arange(32, dtype=jnp.int32)
    col_hot = (small[None, :, None] + cols[:, None, None] == cells[None, None, :]).astype(bf)
    spread = jnp.einsum("scab,sbq->scaq", patch, col_hot, preferred_element_type=f32).astype(bf)
    row_hot = (cells[None, :, None] == rows[:, None, None] + small[None, None, :]).astype(f32)
    w_hi = weight.astype(bf)
    w_lo = (weight - w_hi.astype(f32)).astype(bf)
    w_both = jnp.stack([w_hi, w_lo], 0).astype(f32)
    lhs = (w_both.transpose(0, 2, 1)[:, :, None, :, None] * row_hot.transpose(1, 0, 2)[None, None]).astype(bf)
    out = jnp.einsum("htrsa,scaq->htcrq", lhs, spread, preferred_element_type=f32)
    return out[0] + out[1]


def body(visibilities, coords, vis_counts, cover_tile, offsets, channel, taper):
    n_span = lax.axis_size("span")
    n_freq = lax.axis_size("freq")
    channels = CH_DEV * n_freq
    freq_pos = lax.axis_index("freq")
    sub_count = visibilities.shape[1]
    groups = sub_count // 32
    vis_loc = visibilities[0].reshape(groups, 32, 2, -1)
    coord_loc = coords[0].reshape(groups, 32, 2, -1)
    count_loc = vis_counts[0].reshape(groups, 32)

    def block_work(inputs):
        return make_subgrids(inputs[0], inputs[1], inputs[2], taper)

    patches = lax.map(block_work, (vis_loc, coord_loc, count_loc)).reshape(sub_count, 2, 32, 32)
    dest = cover_tile[0, :, 0]
    row_off = offsets[0, :, 0]
    col_off = offsets[0, :, 1]
    chan_loc = channel[0]
    cap = 2 * sub_count // n_span
    onehot = (dest[:, None] == jnp.arange(n_span, dtype=jnp.int32)[None, :]).astype(jnp.float32)
    order = jnp.arange(sub_count, dtype=jnp.int32)
    lower = (order[:, None] > order[None, :]).astype(jnp.float32)
    earlier = jnp.dot(lower, onehot, preferred_element_type=jnp.float32)
    rank = jnp.sum(earlier * onehot, axis=1).astype(jnp.int32)
    slot = dest * cap + rank
    payload = (
        jnp.zeros((n_span * cap, 2048), jnp.bfloat16).at[slot].set(patches.reshape(sub_count, 2048))
    )
    info = jnp.stack([jnp.ones_like(dest), row_off, col_off, chan_loc], 1).astype(jnp.bfloat16)
    meta = jnp.zeros((n_span * cap, 4), jnp.bfloat16).at[slot].set(info)
    got_payload, got_meta = sent_together(
        (payload.reshape(n_span, cap, 2048), meta.reshape(n_span, cap, 4)), "span", 0, 0, 2
    )
    slots = n_span * cap
    got_meta = got_meta.reshape(slots, 4).astype(jnp.int32)
    valid = got_meta[:, 0].astype(jnp.float32)
    weight = taylor_weights(got_meta[:, 3], freq_pos, channels) * valid[:, None]
    local = place_all(
        got_payload.reshape(slots, 2, 32, 32), weight, got_meta[:, 1], got_meta[:, 2]
    )
    local = local.reshape(NT, 1, 2, TILE, TILE)
    total = gathered_total(local, "freq")
    scale = TILE / (32.0 * math.sqrt(n_freq * sub_count))
    return total * scale


def solution(mesh):
    return jax.shard_map(
        body,
        mesh=mesh,
        in_specs=(
            P("freq", "span", None, None),
            P("freq", "span", None, None),
            P("freq", "span"),
            P("freq", "span", None),
            P("freq", "span", None),
            P("freq", "span"),
            P(),
        ),
        out_specs=P(None, "span", None, None, None),
        check_vma=False,
    )
```

```python
import math

import jax
import jax.numpy as jnp
from jax import lax
from jax.experimental import pallas as pl
from jax.sharding import PartitionSpec as P

TILE = 128
NT = 2
CH_DEV = 16


def sent_together(arrays, axis, split_dim, concat_dim, along):
    widths = [a.shape[along] for a in arrays]
    both = jnp.concatenate(arrays, axis=along)
    whole = lax.all_to_all(both, axis, split_axis=split_dim, concat_axis=concat_dim, tiled=True)
    return tuple(jnp.split(whole, [sum(widths[:k]) for k in range(1, len(widths))], axis=along))


def gathered_total(shard, axis):
    n = lax.axis_size(axis)
    flat = shard.reshape(-1)
    size = flat.shape[0]
    per = -(-size // (n * 128)) * 128
    flat = jnp.pad(flat, (0, per * n - size))
    got = lax.all_to_all(flat.reshape(n, per // 128, 128), axis, 0, 0, tiled=True)
    part = got.sum(axis=0)
    spread = jnp.broadcast_to(part[None], (n, per // 128, 128))
    whole = lax.all_to_all(spread, axis, 0, 0, tiled=True)
    return whole.reshape(-1)[:size].reshape(shard.shape)


def cmul(ar, ai, br, bi):
    return ar * br - ai * bi, ar * bi + ai * br


def bit_powers(c, s, bits, first, count):
    j = jnp.arange(count, dtype=jnp.int32)[None, :, None]
    re = jnp.broadcast_to(first[0][:, None, :], (c.shape[0], count, c.shape[1]))
    im = jnp.broadcast_to(first[1][:, None, :], (c.shape[0], count, c.shape[1]))
    for i, (br, bi) in enumerate(bits):
        on = ((j >> i) & 1) == 1
        mr, mi = cmul(re, im, br[:, None, :], bi[:, None, :])
        re, im = jnp.where(on, mr, re), jnp.where(on, mi, im)
    return re, im


def phase_table(angle, vis=None):
    c, s = jnp.cos(angle), jnp.sin(angle)
    w2 = cmul(c, s, c, s)
    w4 = cmul(*w2, *w2)
    w8 = cmul(*w4, *w4)
    w16 = cmul(*w8, *w8)
    lo = (w16[0], -w16[1])
    if vis is not None:
        lo = cmul(vis[0], vis[1], *lo)
    one = (jnp.ones_like(c), jnp.zeros_like(c))
    small = bit_powers(c, s, [(c, s), w2], one, 4)
    big = bit_powers(c, s, [w4, w8, w16], lo, 8)
    return small, big


def phase_rows(pr, pi, qr, qi, b):
    p_r = jnp.concatenate([pr[b], pr[b]], axis=0)
    p_i = jnp.concatenate([pi[b], pi[b]], axis=0)
    first = lax.broadcasted_iota(jnp.int32, p_r.shape, 0) < 4
    res, ims = [], []
    for m in range(4):
        q_r = jnp.where(first, qr[b, 2 * m : 2 * m + 1, :], qr[b, 2 * m + 1 : 2 * m + 2, :])
        q_i = jnp.where(first, qi[b, 2 * m : 2 * m + 1, :], qi[b, 2 * m + 1 : 2 * m + 2, :])
        r, i = cmul(q_r, q_i, p_r, p_i)
        res.append(r)
        ims.append(i)
    return jnp.concatenate(res + ims, axis=0).astype(jnp.bfloat16)


def s_kernel(upr, upi, uqr, uqi, vpr, vpi, vqr, vqi, out):
    for b in range(out.shape[0]):
        a = phase_rows(upr, upi, uqr, uqi, b)
        bb = phase_rows(vpr, vpi, vqr, vqi, b)
        out[b] = lax.dot_general(
            a, bb, (((1,), (1,)), ((), ())), preferred_element_type=jnp.float32
        )


def s_matrices(small_u, big_u, small_v, big_v):
    n, _, kk = small_u[0].shape
    per = 8
    spec_p = pl.BlockSpec((per, 4, kk), lambda g: (g, 0, 0))
    spec_q = pl.BlockSpec((per, 8, kk), lambda g: (g, 0, 0))
    return pl.pallas_call(
        s_kernel,
        grid=(n // per,),
        in_specs=[spec_p, spec_p, spec_q, spec_q] * 2,
        out_specs=pl.BlockSpec((per, 64, 64), lambda g: (g, 0, 0)),
        out_shape=jax.ShapeDtypeStruct((n, 64, 64), jnp.float32),
        cost_estimate=pl.CostEstimate(
            flops=2 * n * 64 * 64 * kk + 24 * n * 64 * kk,
            transcendentals=0,
            bytes_accessed=4 * n * 24 * kk * 2 + 4 * n * 64 * 64,
        ),
    )(*small_u, *big_u, *small_v, *big_v)


def make_subgrids(vis_b, coord_b, count_b, taper):
    kk = vis_b.shape[-1]
    live = (jnp.arange(kk, dtype=jnp.int32)[None, :] < count_b[:, None]).astype(jnp.float32)
    scale_k = 1.0 / math.sqrt(kk)
    vis_re = vis_b[:, 0, :].astype(jnp.float32) * live * scale_k
    vis_im = vis_b[:, 1, :].astype(jnp.float32) * live * scale_k
    step = -2.0 * math.pi / 32.0
    bf = jnp.bfloat16
    small_u, big_u = phase_table(step * coord_b[:, 0, :])
    small_v, big_v = phase_table(step * coord_b[:, 1, :], (vis_re, vis_im))
    s_all = s_matrices(small_u, big_u, small_v, big_v)
    s_re = s_all[:, :32, :32] - s_all[:, 32:, 32:]
    s_im = s_all[:, :32, 32:] + s_all[:, 32:, :32]
    x2 = jnp.concatenate([taper * s_re, taper * s_im], axis=1)
    centred = jnp.arange(32, dtype=jnp.float32) - 16.0
    angle = -2.0 * math.pi * centred[:, None] * centred[None, :] / 32.0
    f_re, f_im = (jnp.cos(angle), jnp.sin(angle))
    hp = lax.Precision.HIGHEST
    left = jnp.concatenate(
        [jnp.concatenate([f_re, -f_im], 1), jnp.concatenate([f_im, f_re], 1)], 0
    )
    y2 = jnp.einsum("ij,bjq->biq", left, x2, precision=hp)
    ycat = jnp.concatenate([y2[:, :32], y2[:, 32:]], axis=2)
    right = jnp.concatenate(
        [jnp.concatenate([f_re, f_im], 1), jnp.concatenate([-f_im, f_re], 1)], 0
    )
    z2 = jnp.einsum("baj,jk->bak", ycat, right, precision=hp)
    z = z2.reshape(z2.shape[0], 32, 2, 32).transpose(0, 2, 1, 3)
    return (z / 32.0).astype(jnp.bfloat16)


def taylor_weights(chan_local, freq_pos, channels):
    global_chan = (freq_pos * CH_DEV + chan_local).astype(jnp.float32)
    xval = (2.0 * global_chan + 1.0 - channels) / channels
    powers = jnp.arange(NT, dtype=jnp.float32)
    return jnp.where(powers[None, :] == 0.0, 1.0, xval[:, None] ** powers[None, :])


def place_all(patch, weight, rows, cols):
    bf, f32 = jnp.bfloat16, jnp.float32
    cells = jnp.arange(TILE, dtype=jnp.int32)
    small = jnp.arange(32, dtype=jnp.int32)
    col_hot = (small[None, :, None] + cols[:, None, None] == cells[None, None, :]).astype(bf)
    spread = jnp.einsum("scab,sbq->scaq", patch, col_hot, preferred_element_type=f32).astype(bf)
    row_hot = (cells[None, :, None] == rows[:, None, None] + small[None, None, :]).astype(f32)
    w_hi = weight.astype(bf)
    w_lo = (weight - w_hi.astype(f32)).astype(bf)
    w_both = jnp.stack([w_hi, w_lo], 0).astype(f32)
    lhs = (w_both.transpose(0, 2, 1)[:, :, None, :, None] * row_hot.transpose(1, 0, 2)[None, None]).astype(bf)
    out = jnp.einsum("htrsa,scaq->htcrq", lhs, spread, preferred_element_type=f32)
    return out[0] + out[1]


def body(visibilities, coords, vis_counts, cover_tile, offsets, channel, taper):
    n_span = lax.axis_size("span")
    n_freq = lax.axis_size("freq")
    channels = CH_DEV * n_freq
    freq_pos = lax.axis_index("freq")
    sub_count = visibilities.shape[1]
    groups = sub_count // 32
    vis_loc = visibilities[0].reshape(groups, 32, 2, -1)
    coord_loc = coords[0].reshape(groups, 32, 2, -1)
    count_loc = vis_counts[0].reshape(groups, 32)

    def block_work(inputs):
        return make_subgrids(inputs[0], inputs[1], inputs[2], taper)

    patches = lax.map(block_work, (vis_loc, coord_loc, count_loc)).reshape(sub_count, 2, 32, 32)
    dest = cover_tile[0, :, 0]
    row_off = offsets[0, :, 0]
    col_off = offsets[0, :, 1]
    chan_loc = channel[0]
    cap = 2 * sub_count // n_span
    onehot = (dest[:, None] == jnp.arange(n_span, dtype=jnp.int32)[None, :]).astype(jnp.float32)
    order = jnp.arange(sub_count, dtype=jnp.int32)
    lower = (order[:, None] > order[None, :]).astype(jnp.float32)
    earlier = jnp.dot(lower, onehot, preferred_element_type=jnp.float32)
    rank = jnp.sum(earlier * onehot, axis=1).astype(jnp.int32)
    slot = dest * cap + rank
    payload = (
        jnp.zeros((n_span * cap, 2048), jnp.bfloat16).at[slot].set(patches.reshape(sub_count, 2048))
    )
    info = jnp.stack([jnp.ones_like(dest), row_off, col_off, chan_loc], 1).astype(jnp.bfloat16)
    meta = jnp.zeros((n_span * cap, 4), jnp.bfloat16).at[slot].set(info)
    got_payload, got_meta = sent_together(
        (payload.reshape(n_span, cap, 2048), meta.reshape(n_span, cap, 4)), "span", 0, 0, 2
    )
    slots = n_span * cap
    got_meta = got_meta.reshape(slots, 4).astype(jnp.int32)
    valid = got_meta[:, 0].astype(jnp.float32)
    weight = taylor_weights(got_meta[:, 3], freq_pos, channels) * valid[:, None]
    local = place_all(
        got_payload.reshape(slots, 2, 32, 32), weight, got_meta[:, 1], got_meta[:, 2]
    )
    local = local.reshape(NT, 1, 2, TILE, TILE)
    total = gathered_total(local, "freq")
    scale = TILE / (32.0 * math.sqrt(n_freq * sub_count))
    return total * scale


def solution(mesh):
    return jax.shard_map(
        body,
        mesh=mesh,
        in_specs=(
            P("freq", "span", None, None),
            P("freq", "span", None, None),
            P("freq", "span"),
            P("freq", "span", None),
            P("freq", "span", None),
            P("freq", "span"),
            P(),
        ),
        out_specs=P(None, "span", None, None, None),
        check_vma=False,
    )
```

```python
import math

import jax
import jax.numpy as jnp
from jax import lax
from jax.experimental import pallas as pl
from jax.sharding import PartitionSpec as P

TILE = 128
NT = 2
CH_DEV = 16


def sent_together(arrays, axis, split_dim, concat_dim, along):
    widths = [a.shape[along] for a in arrays]
    both = jnp.concatenate(arrays, axis=along)
    whole = lax.all_to_all(both, axis, split_axis=split_dim, concat_axis=concat_dim, tiled=True)
    return tuple(jnp.split(whole, [sum(widths[:k]) for k in range(1, len(widths))], axis=along))


def gathered_total(shard, axis):
    n = lax.axis_size(axis)
    flat = shard.reshape(-1)
    size = flat.shape[0]
    per = -(-size // (n * 128)) * 128
    flat = jnp.pad(flat, (0, per * n - size))
    got = lax.all_to_all(flat.reshape(n, per // 128, 128), axis, 0, 0, tiled=True)
    part = got.sum(axis=0)
    spread = jnp.broadcast_to(part[None], (n, per // 128, 128))
    whole = lax.all_to_all(spread, axis, 0, 0, tiled=True)
    return whole.reshape(-1)[:size].reshape(shard.shape)


def cmul(ar, ai, br, bi):
    return ar * br - ai * bi, ar * bi + ai * br


def kernel_tables(angle, vis=None):
    c, s = jnp.cos(angle), jnp.sin(angle)
    w1 = (c, s)
    w2 = cmul(*w1, *w1)
    w4 = cmul(*w2, *w2)
    w8 = cmul(*w4, *w4)
    w16 = cmul(*w8, *w8)
    lo = (w16[0], -w16[1])
    if vis is not None:
        lo = cmul(*vis, *lo)
    one = (jnp.ones_like(c), jnp.zeros_like(c))
    small = [one, w1, w2, cmul(*w2, *w1)]
    big = []
    for j in range(8):
        q = lo
        for bit, wp in enumerate((w4, w8, w16)):
            if (j >> bit) & 1:
                q = cmul(*q, *wp)
        big.append(q)
    return small, big


def kernel_rows(small, big, b):
    p_r = jnp.concatenate([small[i % 4][0][b : b + 1] for i in range(8)], axis=0)
    p_i = jnp.concatenate([small[i % 4][1][b : b + 1] for i in range(8)], axis=0)
    first = lax.broadcasted_iota(jnp.int32, p_r.shape, 0) < 4
    res, ims = [], []
    for m in range(4):
        qa, qb = big[2 * m], big[2 * m + 1]
        q_r = jnp.where(first, qa[0][b : b + 1], qb[0][b : b + 1])
        q_i = jnp.where(first, qa[1][b : b + 1], qb[1][b : b + 1])
        r, i = cmul(q_r, q_i, p_r, p_i)
        res.append(r)
        ims.append(i)
    return jnp.concatenate(res + ims, axis=0).astype(jnp.bfloat16)


def s_kernel(u_ref, v_ref, vr_ref, vi_ref, out):
    small_u, big_u = kernel_tables(u_ref[...])
    small_v, big_v = kernel_tables(v_ref[...], (vr_ref[...], vi_ref[...]))
    for b in range(out.shape[0]):
        a = kernel_rows(small_u, big_u, b)
        bb = kernel_rows(small_v, big_v, b)
        out[b] = lax.dot_general(
            a, bb, (((1,), (1,)), ((), ())), preferred_element_type=jnp.float32
        )


def s_matrices(u_ang, v_ang, vis_re, vis_im):
    n, kk = u_ang.shape
    per = 8
    spec = pl.BlockSpec((per, kk), lambda g: (g, 0))
    return pl.pallas_call(
        s_kernel,
        grid=(n // per,),
        in_specs=[spec] * 4,
        out_specs=pl.BlockSpec((per, 64, 64), lambda g: (g, 0, 0)),
        out_shape=jax.ShapeDtypeStruct((n, 64, 64), jnp.float32),
        cost_estimate=pl.CostEstimate(
            flops=2 * n * 64 * 64 * kk + 24 * n * 64 * kk,
            transcendentals=4 * n * kk,
            bytes_accessed=4 * n * 4 * kk + 4 * n * 64 * 64,
        ),
    )(u_ang, v_ang, vis_re, vis_im)


def make_subgrids(vis_b, coord_b, count_b, taper):
    kk = vis_b.shape[-1]
    live = (jnp.arange(kk, dtype=jnp.int32)[None, :] < count_b[:, None]).astype(jnp.float32)
    scale_k = 1.0 / math.sqrt(kk)
    vis_re = vis_b[:, 0, :].astype(jnp.float32) * live * scale_k
    vis_im = vis_b[:, 1, :].astype(jnp.float32) * live * scale_k
    step = -2.0 * math.pi / 32.0
    bf = jnp.bfloat16
    s_all = s_matrices(step * coord_b[:, 0, :], step * coord_b[:, 1, :], vis_re, vis_im)
    s_re = s_all[:, :32, :32] - s_all[:, 32:, 32:]
    s_im = s_all[:, :32, 32:] + s_all[:, 32:, :32]
    x2 = jnp.concatenate([taper * s_re, taper * s_im], axis=1)
    centred = jnp.arange(32, dtype=jnp.float32) - 16.0
    angle = -2.0 * math.pi * centred[:, None] * centred[None, :] / 32.0
    f_re, f_im = (jnp.cos(angle), jnp.sin(angle))
    hp = lax.Precision.HIGHEST
    left = jnp.concatenate(
        [jnp.concatenate([f_re, -f_im], 1), jnp.concatenate([f_im, f_re], 1)], 0
    )
    y2 = jnp.einsum("ij,bjq->biq", left, x2, precision=hp)
    ycat = jnp.concatenate([y2[:, :32], y2[:, 32:]], axis=2)
    right = jnp.concatenate(
        [jnp.concatenate([f_re, f_im], 1), jnp.concatenate([-f_im, f_re], 1)], 0
    )
    z2 = jnp.einsum("baj,jk->bak", ycat, right, precision=hp)
    z = z2.reshape(z2.shape[0], 32, 2, 32).transpose(0, 2, 1, 3)
    return (z / 32.0).astype(jnp.bfloat16)


def taylor_weights(chan_local, freq_pos, channels):
    global_chan = (freq_pos * CH_DEV + chan_local).astype(jnp.float32)
    xval = (2.0 * global_chan + 1.0 - channels) / channels
    powers = jnp.arange(NT, dtype=jnp.float32)
    return jnp.where(powers[None, :] == 0.0, 1.0, xval[:, None] ** powers[None, :])


def place_all(patch, weight, rows, cols):
    bf, f32 = jnp.bfloat16, jnp.float32
    cells = jnp.arange(TILE, dtype=jnp.int32)
    small = jnp.arange(32, dtype=jnp.int32)
    col_hot = (small[None, :, None] + cols[:, None, None] == cells[None, None, :]).astype(bf)
    spread = jnp.einsum("scab,sbq->scaq", patch, col_hot, preferred_element_type=f32).astype(bf)
    row_hot = (cells[None, :, None] == rows[:, None, None] + small[None, None, :]).astype(f32)
    w_hi = weight.astype(bf)
    w_lo = (weight - w_hi.astype(f32)).astype(bf)
    w_both = jnp.stack([w_hi, w_lo], 0).astype(f32)
    lhs = (w_both.transpose(0, 2, 1)[:, :, None, :, None] * row_hot.transpose(1, 0, 2)[None, None]).astype(bf)
    out = jnp.einsum("htrsa,scaq->htcrq", lhs, spread, preferred_element_type=f32)
    return out[0] + out[1]


def body(visibilities, coords, vis_counts, cover_tile, offsets, channel, taper):
    n_span = lax.axis_size("span")
    n_freq = lax.axis_size("freq")
    channels = CH_DEV * n_freq
    freq_pos = lax.axis_index("freq")
    sub_count = visibilities.shape[1]
    groups = sub_count // 32
    vis_loc = visibilities[0].reshape(groups, 32, 2, -1)
    coord_loc = coords[0].reshape(groups, 32, 2, -1)
    count_loc = vis_counts[0].reshape(groups, 32)

    def block_work(inputs):
        return make_subgrids(inputs[0], inputs[1], inputs[2], taper)

    patches = lax.map(block_work, (vis_loc, coord_loc, count_loc)).reshape(sub_count, 2, 32, 32)
    dest = cover_tile[0, :, 0]
    row_off = offsets[0, :, 0]
    col_off = offsets[0, :, 1]
    chan_loc = channel[0]
    cap = 2 * sub_count // n_span
    onehot = (dest[:, None] == jnp.arange(n_span, dtype=jnp.int32)[None, :]).astype(jnp.float32)
    order = jnp.arange(sub_count, dtype=jnp.int32)
    lower = (order[:, None] > order[None, :]).astype(jnp.float32)
    earlier = jnp.dot(lower, onehot, preferred_element_type=jnp.float32)
    rank = jnp.sum(earlier * onehot, axis=1).astype(jnp.int32)
    slot = dest * cap + rank
    payload = (
        jnp.zeros((n_span * cap, 2048), jnp.bfloat16).at[slot].set(patches.reshape(sub_count, 2048))
    )
    info = jnp.stack([jnp.ones_like(dest), row_off, col_off, chan_loc], 1).astype(jnp.bfloat16)
    meta = jnp.zeros((n_span * cap, 4), jnp.bfloat16).at[slot].set(info)
    got_payload, got_meta = sent_together(
        (payload.reshape(n_span, cap, 2048), meta.reshape(n_span, cap, 4)), "span", 0, 0, 2
    )
    slots = n_span * cap
    got_meta = got_meta.reshape(slots, 4).astype(jnp.int32)
    valid = got_meta[:, 0].astype(jnp.float32)
    weight = taylor_weights(got_meta[:, 3], freq_pos, channels) * valid[:, None]
    local = place_all(
        got_payload.reshape(slots, 2, 32, 32), weight, got_meta[:, 1], got_meta[:, 2]
    )
    local = local.reshape(NT, 1, 2, TILE, TILE)
    total = gathered_total(local, "freq")
    scale = TILE / (32.0 * math.sqrt(n_freq * sub_count))
    return total * scale


def solution(mesh):
    return jax.shard_map(
        body,
        mesh=mesh,
        in_specs=(
            P("freq", "span", None, None),
            P("freq", "span", None, None),
            P("freq", "span"),
            P("freq", "span", None),
            P("freq", "span", None),
            P("freq", "span"),
            P(),
        ),
        out_specs=P(None, "span", None, None, None),
        check_vma=False,
    )
```

```python
import math

import jax
import jax.numpy as jnp
from jax import lax
from jax.experimental import pallas as pl
from jax.sharding import PartitionSpec as P

TILE = 128
NT = 2
CH_DEV = 16


def sent_together(arrays, axis, split_dim, concat_dim, along):
    widths = [a.shape[along] for a in arrays]
    both = jnp.concatenate(arrays, axis=along)
    whole = lax.all_to_all(both, axis, split_axis=split_dim, concat_axis=concat_dim, tiled=True)
    return tuple(jnp.split(whole, [sum(widths[:k]) for k in range(1, len(widths))], axis=along))


def gathered_total(shard, axis):
    n = lax.axis_size(axis)
    flat = shard.reshape(-1)
    size = flat.shape[0]
    per = -(-size // (n * 128)) * 128
    flat = jnp.pad(flat, (0, per * n - size))
    got = lax.all_to_all(flat.reshape(n, per // 128, 128), axis, 0, 0, tiled=True)
    part = got.sum(axis=0)
    spread = jnp.broadcast_to(part[None], (n, per // 128, 128))
    whole = lax.all_to_all(spread, axis, 0, 0, tiled=True)
    return whole.reshape(-1)[:size].reshape(shard.shape)


def cmul(ar, ai, br, bi):
    return ar * br - ai * bi, ar * bi + ai * br


def kernel_tables(angle, vis=None):
    c, s = jnp.cos(angle), jnp.sin(angle)
    w1 = (c, s)
    w2 = cmul(*w1, *w1)
    w4 = cmul(*w2, *w2)
    w8 = cmul(*w4, *w4)
    w16 = cmul(*w8, *w8)
    lo = (w16[0], -w16[1])
    if vis is not None:
        lo = cmul(*vis, *lo)
    one = (jnp.ones_like(c), jnp.zeros_like(c))
    small = [one, w1, w2, cmul(*w2, *w1)]
    big = []
    for j in range(8):
        q = lo
        for bit, wp in enumerate((w4, w8, w16)):
            if (j >> bit) & 1:
                q = cmul(*q, *wp)
        big.append(q)
    return small, big


def kernel_rows(small, big, b):
    p_r = jnp.concatenate([small[i % 4][0][b : b + 1] for i in range(8)], axis=0)
    p_i = jnp.concatenate([small[i % 4][1][b : b + 1] for i in range(8)], axis=0)
    first = lax.broadcasted_iota(jnp.int32, p_r.shape, 0) < 4
    res, ims = [], []
    for m in range(4):
        qa, qb = big[2 * m], big[2 * m + 1]
        q_r = jnp.where(first, qa[0][b : b + 1], qb[0][b : b + 1])
        q_i = jnp.where(first, qa[1][b : b + 1], qb[1][b : b + 1])
        r, i = cmul(q_r, q_i, p_r, p_i)
        res.append(r)
        ims.append(i)
    return jnp.concatenate(res + ims, axis=0).astype(jnp.bfloat16)


def s_kernel(u_ref, v_ref, vr_ref, vi_ref, taper_ref, g_ref, h_ref, out):
    small_u, big_u = kernel_tables(u_ref[...])
    small_v, big_v = kernel_tables(v_ref[...], (vr_ref[...], vi_ref[...]))
    tp, g, h = taper_ref[...], g_ref[...], h_ref[...]
    hp = lax.Precision.HIGHEST
    f32 = jnp.float32
    for b in range(out.shape[0]):
        a = kernel_rows(small_u, big_u, b)
        bb = kernel_rows(small_v, big_v, b)
        sm = lax.dot_general(a, bb, (((1,), (1,)), ((), ())), preferred_element_type=f32)
        x_re = tp * (sm[:32, :32] - sm[32:, 32:])
        x_im = tp * (sm[:32, 32:] + sm[32:, :32])
        x2 = jnp.concatenate([x_re, x_im], axis=0)
        y2 = jnp.dot(g, x2, precision=hp, preferred_element_type=f32)
        ycat = jnp.concatenate([y2[:32], y2[32:]], axis=1)
        z2 = jnp.dot(ycat, h, precision=hp, preferred_element_type=f32)
        out[b] = (z2 / 32.0).astype(out.dtype)


def subgrid_patches(u_ang, v_ang, vis_re, vis_im, taper, left, right):
    n, kk = u_ang.shape
    per = 8
    spec = pl.BlockSpec((per, kk), lambda g: (g, 0))
    whole = pl.BlockSpec((64, 64), lambda g: (0, 0))
    return pl.pallas_call(
        s_kernel,
        grid=(n // per,),
        in_specs=[spec] * 4 + [pl.BlockSpec((32, 32), lambda g: (0, 0)), whole, whole],
        out_specs=pl.BlockSpec((per, 32, 64), lambda g: (g, 0, 0)),
        out_shape=jax.ShapeDtypeStruct((n, 32, 64), jnp.bfloat16),
        cost_estimate=pl.CostEstimate(
            flops=2 * n * 64 * 64 * kk + 24 * n * 64 * kk + 24 * n * 64 * 64 * 32,
            transcendentals=4 * n * kk,
            bytes_accessed=4 * n * 4 * kk + 2 * n * 32 * 64,
        ),
    )(u_ang, v_ang, vis_re, vis_im, taper, left, right)


def make_subgrids(vis_b, coord_b, count_b, taper):
    kk = vis_b.shape[-1]
    live = (jnp.arange(kk, dtype=jnp.int32)[None, :] < count_b[:, None]).astype(jnp.float32)
    scale_k = 1.0 / math.sqrt(kk)
    vis_re = vis_b[:, 0, :].astype(jnp.float32) * live * scale_k
    vis_im = vis_b[:, 1, :].astype(jnp.float32) * live * scale_k
    step = -2.0 * math.pi / 32.0
    centred = jnp.arange(32, dtype=jnp.float32) - 16.0
    angle = -2.0 * math.pi * centred[:, None] * centred[None, :] / 32.0
    f_re, f_im = (jnp.cos(angle), jnp.sin(angle))
    left = jnp.concatenate(
        [jnp.concatenate([f_re, -f_im], 1), jnp.concatenate([f_im, f_re], 1)], 0
    )
    right = jnp.concatenate(
        [jnp.concatenate([f_re, f_im], 1), jnp.concatenate([-f_im, f_re], 1)], 0
    )
    return subgrid_patches(
        step * coord_b[:, 0, :], step * coord_b[:, 1, :], vis_re, vis_im, taper, left, right
    )


def taylor_weights(chan_local, freq_pos, channels):
    global_chan = (freq_pos * CH_DEV + chan_local).astype(jnp.float32)
    xval = (2.0 * global_chan + 1.0 - channels) / channels
    powers = jnp.arange(NT, dtype=jnp.float32)
    return jnp.where(powers[None, :] == 0.0, 1.0, xval[:, None] ** powers[None, :])


def place_all(patch, weight, rows, cols):
    bf, f32 = jnp.bfloat16, jnp.float32
    cells = jnp.arange(TILE, dtype=jnp.int32)
    small = jnp.arange(32, dtype=jnp.int32)
    col_hot = (small[None, :, None] + cols[:, None, None] == cells[None, None, :]).astype(bf)
    spread = jnp.einsum("sacb,sbq->scaq", patch, col_hot, preferred_element_type=f32).astype(bf)
    row_hot = (cells[None, :, None] == rows[:, None, None] + small[None, None, :]).astype(f32)
    w_hi = weight.astype(bf)
    w_lo = (weight - w_hi.astype(f32)).astype(bf)
    w_both = jnp.stack([w_hi, w_lo], 0).astype(f32)
    lhs = (w_both.transpose(0, 2, 1)[:, :, None, :, None] * row_hot.transpose(1, 0, 2)[None, None]).astype(bf)
    out = jnp.einsum("htrsa,scaq->htcrq", lhs, spread, preferred_element_type=f32)
    return out[0] + out[1]


def body(visibilities, coords, vis_counts, cover_tile, offsets, channel, taper):
    n_span = lax.axis_size("span")
    n_freq = lax.axis_size("freq")
    channels = CH_DEV * n_freq
    freq_pos = lax.axis_index("freq")
    sub_count = visibilities.shape[1]
    groups = sub_count // 32
    vis_loc = visibilities[0].reshape(groups, 32, 2, -1)
    coord_loc = coords[0].reshape(groups, 32, 2, -1)
    count_loc = vis_counts[0].reshape(groups, 32)

    def block_work(inputs):
        return make_subgrids(inputs[0], inputs[1], inputs[2], taper)

    patches = lax.map(block_work, (vis_loc, coord_loc, count_loc)).reshape(sub_count, 32, 2, 32)
    dest = cover_tile[0, :, 0]
    row_off = offsets[0, :, 0]
    col_off = offsets[0, :, 1]
    chan_loc = channel[0]
    cap = 2 * sub_count // n_span
    onehot = (dest[:, None] == jnp.arange(n_span, dtype=jnp.int32)[None, :]).astype(jnp.float32)
    order = jnp.arange(sub_count, dtype=jnp.int32)
    lower = (order[:, None] > order[None, :]).astype(jnp.float32)
    earlier = jnp.dot(lower, onehot, preferred_element_type=jnp.float32)
    rank = jnp.sum(earlier * onehot, axis=1).astype(jnp.int32)
    slot = dest * cap + rank
    payload = (
        jnp.zeros((n_span * cap, 2048), jnp.bfloat16).at[slot].set(patches.reshape(sub_count, 2048))
    )
    info = jnp.stack([jnp.ones_like(dest), row_off, col_off, chan_loc], 1).astype(jnp.bfloat16)
    meta = jnp.zeros((n_span * cap, 4), jnp.bfloat16).at[slot].set(info)
    got_payload, got_meta = sent_together(
        (payload.reshape(n_span, cap, 2048), meta.reshape(n_span, cap, 4)), "span", 0, 0, 2
    )
    slots = n_span * cap
    got_meta = got_meta.reshape(slots, 4).astype(jnp.int32)
    valid = got_meta[:, 0].astype(jnp.float32)
    weight = taylor_weights(got_meta[:, 3], freq_pos, channels) * valid[:, None]
    local = place_all(
        got_payload.reshape(slots, 32, 2, 32), weight, got_meta[:, 1], got_meta[:, 2]
    )
    local = local.reshape(NT, 1, 2, TILE, TILE)
    total = gathered_total(local, "freq")
    scale = TILE / (32.0 * math.sqrt(n_freq * sub_count))
    return total * scale


def solution(mesh):
    return jax.shard_map(
        body,
        mesh=mesh,
        in_specs=(
            P("freq", "span", None, None),
            P("freq", "span", None, None),
            P("freq", "span"),
            P("freq", "span", None),
            P("freq", "span", None),
            P("freq", "span"),
            P(),
        ),
        out_specs=P(None, "span", None, None, None),
        check_vma=False,
    )
```

```python
import math

import jax
import jax.numpy as jnp
from jax import lax
from jax.experimental import pallas as pl
from jax.sharding import PartitionSpec as P

TILE = 128
NT = 2
CH_DEV = 16


def sent_together(arrays, axis, split_dim, concat_dim, along):
    widths = [a.shape[along] for a in arrays]
    both = jnp.concatenate(arrays, axis=along)
    whole = lax.all_to_all(both, axis, split_axis=split_dim, concat_axis=concat_dim, tiled=True)
    return tuple(jnp.split(whole, [sum(widths[:k]) for k in range(1, len(widths))], axis=along))


def gathered_total(shard, axis):
    n = lax.axis_size(axis)
    flat = shard.reshape(-1)
    size = flat.shape[0]
    per = -(-size // (n * 128)) * 128
    flat = jnp.pad(flat, (0, per * n - size))
    got = lax.all_to_all(flat.reshape(n, per // 128, 128), axis, 0, 0, tiled=True)
    part = got.sum(axis=0)
    spread = jnp.broadcast_to(part[None], (n, per // 128, 128))
    whole = lax.all_to_all(spread, axis, 0, 0, tiled=True)
    return whole.reshape(-1)[:size].reshape(shard.shape)


def cmul(ar, ai, br, bi):
    return ar * br - ai * bi, ar * bi + ai * br


def kernel_tables(angle, vis=None):
    c, s = jnp.cos(angle), jnp.sin(angle)
    w1 = (c, s)
    w2 = cmul(*w1, *w1)
    w4 = cmul(*w2, *w2)
    w8 = cmul(*w4, *w4)
    w16 = cmul(*w8, *w8)
    lo = (w16[0], -w16[1])
    if vis is not None:
        lo = cmul(*vis, *lo)
    one = (jnp.ones_like(c), jnp.zeros_like(c))
    small = [one, w1, w2, cmul(*w2, *w1)]
    big = []
    for j in range(8):
        q = lo
        for bit, wp in enumerate((w4, w8, w16)):
            if (j >> bit) & 1:
                q = cmul(*q, *wp)
        big.append(q)
    return small, big


def kernel_rows(small, big, b):
    p_r = jnp.concatenate([small[i % 4][0][b : b + 1] for i in range(8)], axis=0)
    p_i = jnp.concatenate([small[i % 4][1][b : b + 1] for i in range(8)], axis=0)
    first = lax.broadcasted_iota(jnp.int32, p_r.shape, 0) < 4
    res, ims = [], []
    for m in range(4):
        qa, qb = big[2 * m], big[2 * m + 1]
        q_r = jnp.where(first, qa[0][b : b + 1], qb[0][b : b + 1])
        q_i = jnp.where(first, qa[1][b : b + 1], qb[1][b : b + 1])
        r, i = cmul(q_r, q_i, p_r, p_i)
        res.append(r)
        ims.append(i)
    return jnp.concatenate(res + ims, axis=0).astype(jnp.bfloat16)


def s_kernel(u_ref, v_ref, vr_ref, vi_ref, out):
    small_u, big_u = kernel_tables(u_ref[...])
    small_v, big_v = kernel_tables(v_ref[...], (vr_ref[...], vi_ref[...]))
    for b in range(out.shape[0]):
        a = kernel_rows(small_u, big_u, b)
        bb = kernel_rows(small_v, big_v, b)
        out[b] = lax.dot_general(
            a, bb, (((1,), (1,)), ((), ())), preferred_element_type=jnp.float32
        )


def s_matrices(u_ang, v_ang, vis_re, vis_im):
    n, kk = u_ang.shape
    per = 8
    spec = pl.BlockSpec((per, kk), lambda g: (g, 0))
    return pl.pallas_call(
        s_kernel,
        grid=(n // per,),
        in_specs=[spec] * 4,
        out_specs=pl.BlockSpec((per, 64, 64), lambda g: (g, 0, 0)),
        out_shape=jax.ShapeDtypeStruct((n, 64, 64), jnp.float32),
        cost_estimate=pl.CostEstimate(
            flops=2 * n * 64 * 64 * kk + 24 * n * 64 * kk,
            transcendentals=4 * n * kk,
            bytes_accessed=4 * n * 4 * kk + 4 * n * 64 * 64,
        ),
    )(u_ang, v_ang, vis_re, vis_im)


def make_subgrids(vis_b, coord_b, count_b, taper):
    kk = vis_b.shape[-1]
    live = (jnp.arange(kk, dtype=jnp.int32)[None, :] < count_b[:, None]).astype(jnp.float32)
    scale_k = 1.0 / math.sqrt(kk)
    vis_re = vis_b[:, 0, :].astype(jnp.float32) * live * scale_k
    vis_im = vis_b[:, 1, :].astype(jnp.float32) * live * scale_k
    step = -2.0 * math.pi / 32.0
    bf = jnp.bfloat16
    s_all = s_matrices(step * coord_b[:, 0, :], step * coord_b[:, 1, :], vis_re, vis_im)
    s_re = s_all[:, :32, :32] - s_all[:, 32:, 32:]
    s_im = s_all[:, :32, 32:] + s_all[:, 32:, :32]
    x2 = jnp.concatenate([taper * s_re, taper * s_im], axis=1)
    centred = jnp.arange(32, dtype=jnp.float32) - 16.0
    angle = -2.0 * math.pi * centred[:, None] * centred[None, :] / 32.0
    f_re, f_im = (jnp.cos(angle), jnp.sin(angle))
    hp = lax.Precision.HIGHEST
    left = jnp.concatenate(
        [jnp.concatenate([f_re, -f_im], 1), jnp.concatenate([f_im, f_re], 1)], 0
    )
    y2 = jnp.einsum("ij,bjq->biq", left, x2, precision=hp)
    ycat = jnp.concatenate([y2[:, :32], y2[:, 32:]], axis=2)
    right = jnp.concatenate(
        [jnp.concatenate([f_re, f_im], 1), jnp.concatenate([-f_im, f_re], 1)], 0
    )
    z2 = jnp.einsum("baj,jk->bak", ycat, right, precision=hp)
    z = z2.reshape(z2.shape[0], 32, 2, 32).transpose(0, 2, 1, 3)
    return (z / 32.0).astype(jnp.bfloat16)


def taylor_weights(chan_local, freq_pos, channels):
    global_chan = (freq_pos * CH_DEV + chan_local).astype(jnp.float32)
    xval = (2.0 * global_chan + 1.0 - channels) / channels
    powers = jnp.arange(NT, dtype=jnp.float32)
    return jnp.where(powers[None, :] == 0.0, 1.0, xval[:, None] ** powers[None, :])


def place_all(patch, weight, rows, cols):
    bf, f32 = jnp.bfloat16, jnp.float32
    cells = jnp.arange(TILE, dtype=jnp.int32)
    small = jnp.arange(32, dtype=jnp.int32)
    col_hot = (small[None, :, None] + cols[:, None, None] == cells[None, None, :]).astype(bf)
    spread = jnp.einsum("scab,sbq->scaq", patch, col_hot, preferred_element_type=f32).astype(bf)
    row_hot = (cells[None, :, None] == rows[:, None, None] + small[None, None, :]).astype(f32)
    w_hi = weight.astype(bf)
    w_lo = (weight - w_hi.astype(f32)).astype(bf)
    w_both = jnp.stack([w_hi, w_lo], 0).astype(f32)
    lhs = (w_both.transpose(0, 2, 1)[:, :, None, :, None] * row_hot.transpose(1, 0, 2)[None, None]).astype(bf)
    out = jnp.einsum("htrsa,scaq->htcrq", lhs, spread, preferred_element_type=f32)
    return out[0] + out[1]


def body(visibilities, coords, vis_counts, cover_tile, offsets, channel, taper):
    n_span = lax.axis_size("span")
    n_freq = lax.axis_size("freq")
    channels = CH_DEV * n_freq
    freq_pos = lax.axis_index("freq")
    sub_count = visibilities.shape[1]
    groups = sub_count // 32
    vis_loc = visibilities[0].reshape(groups, 32, 2, -1)
    coord_loc = coords[0].reshape(groups, 32, 2, -1)
    count_loc = vis_counts[0].reshape(groups, 32)

    def block_work(inputs):
        return make_subgrids(inputs[0], inputs[1], inputs[2], taper)

    patches = lax.map(block_work, (vis_loc, coord_loc, count_loc)).reshape(sub_count, 2, 32, 32)
    dest = cover_tile[0, :, 0]
    row_off = offsets[0, :, 0]
    col_off = offsets[0, :, 1]
    chan_loc = channel[0]
    cap = 2 * sub_count // n_span
    onehot = (dest[:, None] == jnp.arange(n_span, dtype=jnp.int32)[None, :]).astype(jnp.float32)
    order = jnp.arange(sub_count, dtype=jnp.int32)
    lower = (order[:, None] > order[None, :]).astype(jnp.float32)
    earlier = jnp.dot(lower, onehot, preferred_element_type=jnp.float32)
    rank = jnp.sum(earlier * onehot, axis=1).astype(jnp.int32)
    slot = dest * cap + rank
    info = jnp.stack([jnp.ones_like(dest), row_off, col_off, chan_loc], 1).astype(jnp.bfloat16)
    rows = jnp.concatenate([patches.reshape(sub_count, 2048), info], axis=1)
    pick = (slot[None, :] == jnp.arange(n_span * cap, dtype=jnp.int32)[:, None]).astype(jnp.bfloat16)
    send = jnp.dot(pick, rows, preferred_element_type=jnp.float32).astype(jnp.bfloat16)
    got = lax.all_to_all(send.reshape(n_span, cap, 2052), "span", 0, 0, tiled=True)
    got_payload, got_meta = got[:, :, :2048], got[:, :, 2048:]
    slots = n_span * cap
    got_meta = got_meta.reshape(slots, 4).astype(jnp.int32)
    valid = got_meta[:, 0].astype(jnp.float32)
    weight = taylor_weights(got_meta[:, 3], freq_pos, channels) * valid[:, None]
    local = place_all(
        got_payload.reshape(slots, 2, 32, 32), weight, got_meta[:, 1], got_meta[:, 2]
    )
    local = local.reshape(NT, 1, 2, TILE, TILE)
    total = gathered_total(local, "freq")
    scale = TILE / (32.0 * math.sqrt(n_freq * sub_count))
    return total * scale


def solution(mesh):
    return jax.shard_map(
        body,
        mesh=mesh,
        in_specs=(
            P("freq", "span", None, None),
            P("freq", "span", None, None),
            P("freq", "span"),
            P("freq", "span", None),
            P("freq", "span", None),
            P("freq", "span"),
            P(),
        ),
        out_specs=P(None, "span", None, None, None),
        check_vma=False,
    )
```

```python
import math

import jax
import jax.numpy as jnp
from jax import lax
from jax.experimental import pallas as pl
from jax.sharding import PartitionSpec as P

TILE = 128
NT = 2
CH_DEV = 16


def sent_together(arrays, axis, split_dim, concat_dim, along):
    widths = [a.shape[along] for a in arrays]
    both = jnp.concatenate(arrays, axis=along)
    whole = lax.all_to_all(both, axis, split_axis=split_dim, concat_axis=concat_dim, tiled=True)
    return tuple(jnp.split(whole, [sum(widths[:k]) for k in range(1, len(widths))], axis=along))


def gathered_total(shard, axis):
    n = lax.axis_size(axis)
    flat = shard.reshape(-1)
    size = flat.shape[0]
    per = -(-size // (n * 128)) * 128
    flat = jnp.pad(flat, (0, per * n - size))
    got = lax.all_to_all(flat.reshape(n, per // 128, 128), axis, 0, 0, tiled=True)
    part = got.sum(axis=0)
    spread = jnp.broadcast_to(part[None], (n, per // 128, 128))
    whole = lax.all_to_all(spread, axis, 0, 0, tiled=True)
    return whole.reshape(-1)[:size].reshape(shard.shape)


def cmul(ar, ai, br, bi):
    return ar * br - ai * bi, ar * bi + ai * br


def kernel_tables(angle, vis=None):
    c, s = jnp.cos(angle), jnp.sin(angle)
    w1 = (c, s)
    w2 = cmul(*w1, *w1)
    w4 = cmul(*w2, *w2)
    w8 = cmul(*w4, *w4)
    w16 = cmul(*w8, *w8)
    lo = (w16[0], -w16[1])
    if vis is not None:
        lo = cmul(*vis, *lo)
    one = (jnp.ones_like(c), jnp.zeros_like(c))
    small = [one, w1, w2, cmul(*w2, *w1)]
    big = []
    for j in range(8):
        q = lo
        for bit, wp in enumerate((w4, w8, w16)):
            if (j >> bit) & 1:
                q = cmul(*q, *wp)
        big.append(q)
    return small, big


def kernel_rows(small, big, b):
    p_r = jnp.concatenate([small[i % 4][0][b : b + 1] for i in range(8)], axis=0)
    p_i = jnp.concatenate([small[i % 4][1][b : b + 1] for i in range(8)], axis=0)
    first = lax.broadcasted_iota(jnp.int32, p_r.shape, 0) < 4
    res, ims = [], []
    for m in range(4):
        qa, qb = big[2 * m], big[2 * m + 1]
        q_r = jnp.where(first, qa[0][b : b + 1], qb[0][b : b + 1])
        q_i = jnp.where(first, qa[1][b : b + 1], qb[1][b : b + 1])
        r, i = cmul(q_r, q_i, p_r, p_i)
        res.append(r)
        ims.append(i)
    return jnp.concatenate(res + ims, axis=0).astype(jnp.bfloat16)


def s_kernel(coord_ref, vis_ref, count_ref, out):
    kk = coord_ref.shape[-1]
    step = -2.0 * math.pi / 32.0
    live = lax.broadcasted_iota(jnp.int32, (coord_ref.shape[0], kk), 1) < count_ref[...]
    scale_k = 1.0 / math.sqrt(kk)
    vis = vis_ref[...].astype(jnp.float32)
    coord = coord_ref[...]
    vr = jnp.where(live, vis[:, 0, :] * scale_k, 0.0)
    vi = jnp.where(live, vis[:, 1, :] * scale_k, 0.0)
    small_u, big_u = kernel_tables(step * coord[:, 0, :])
    small_v, big_v = kernel_tables(step * coord[:, 1, :], (vr, vi))
    for b in range(out.shape[0]):
        a = kernel_rows(small_u, big_u, b)
        bb = kernel_rows(small_v, big_v, b)
        out[b] = lax.dot_general(
            a, bb, (((1,), (1,)), ((), ())), preferred_element_type=jnp.float32
        )


def s_matrices(coords, vis, counts):
    n, _, kk = coords.shape
    per = 8
    both = pl.BlockSpec((per, 2, kk), lambda g: (g, 0, 0))
    return pl.pallas_call(
        s_kernel,
        grid=(n // per,),
        in_specs=[both, both, pl.BlockSpec((per, 1), lambda g: (g, 0))],
        out_specs=pl.BlockSpec((per, 64, 64), lambda g: (g, 0, 0)),
        out_shape=jax.ShapeDtypeStruct((n, 64, 64), jnp.float32),
        cost_estimate=pl.CostEstimate(
            flops=2 * n * 64 * 64 * kk + 24 * n * 64 * kk,
            transcendentals=4 * n * kk,
            bytes_accessed=6 * n * 2 * kk + 4 * n * 64 * 64,
        ),
    )(coords, vis, counts)


def make_subgrids(vis_b, coord_b, count_b, taper):
    s_all = s_matrices(coord_b, vis_b, count_b.reshape(-1, 1))
    s_re = s_all[:, :32, :32] - s_all[:, 32:, 32:]
    s_im = s_all[:, :32, 32:] + s_all[:, 32:, :32]
    x2 = jnp.concatenate([taper * s_re, taper * s_im], axis=1)
    centred = jnp.arange(32, dtype=jnp.float32) - 16.0
    angle = -2.0 * math.pi * centred[:, None] * centred[None, :] / 32.0
    f_re, f_im = (jnp.cos(angle), jnp.sin(angle))
    hp = lax.Precision.HIGHEST
    left = jnp.concatenate(
        [jnp.concatenate([f_re, -f_im], 1), jnp.concatenate([f_im, f_re], 1)], 0
    )
    y2 = jnp.einsum("ij,bjq->biq", left, x2, precision=hp)
    ycat = jnp.concatenate([y2[:, :32], y2[:, 32:]], axis=2)
    right = jnp.concatenate(
        [jnp.concatenate([f_re, f_im], 1), jnp.concatenate([-f_im, f_re], 1)], 0
    )
    z2 = jnp.einsum("baj,jk->bak", ycat, right, precision=hp)
    z = z2.reshape(z2.shape[0], 32, 2, 32).transpose(0, 2, 1, 3)
    return (z / 32.0).astype(jnp.bfloat16)


def taylor_weights(chan_local, freq_pos, channels):
    global_chan = (freq_pos * CH_DEV + chan_local).astype(jnp.float32)
    xval = (2.0 * global_chan + 1.0 - channels) / channels
    powers = jnp.arange(NT, dtype=jnp.float32)
    return jnp.where(powers[None, :] == 0.0, 1.0, xval[:, None] ** powers[None, :])


def place_all(patch, weight, rows, cols):
    bf, f32 = jnp.bfloat16, jnp.float32
    cells = jnp.arange(TILE, dtype=jnp.int32)
    small = jnp.arange(32, dtype=jnp.int32)
    col_hot = (small[None, :, None] + cols[:, None, None] == cells[None, None, :]).astype(bf)
    spread = jnp.einsum("scab,sbq->scaq", patch, col_hot, preferred_element_type=f32).astype(bf)
    row_hot = (cells[None, :, None] == rows[:, None, None] + small[None, None, :]).astype(f32)
    w_hi = weight.astype(bf)
    w_lo = (weight - w_hi.astype(f32)).astype(bf)
    w_both = jnp.stack([w_hi, w_lo], 0).astype(f32)
    lhs = (w_both.transpose(0, 2, 1)[:, :, None, :, None] * row_hot.transpose(1, 0, 2)[None, None]).astype(bf)
    out = jnp.einsum("htrsa,scaq->htcrq", lhs, spread, preferred_element_type=f32)
    return out[0] + out[1]


def body(visibilities, coords, vis_counts, cover_tile, offsets, channel, taper):
    n_span = lax.axis_size("span")
    n_freq = lax.axis_size("freq")
    channels = CH_DEV * n_freq
    freq_pos = lax.axis_index("freq")
    sub_count = visibilities.shape[1]
    groups = sub_count // 32
    vis_loc = visibilities[0].reshape(groups, 32, 2, -1)
    coord_loc = coords[0].reshape(groups, 32, 2, -1)
    count_loc = vis_counts[0].reshape(groups, 32)

    def block_work(inputs):
        return make_subgrids(inputs[0], inputs[1], inputs[2], taper)

    patches = lax.map(block_work, (vis_loc, coord_loc, count_loc)).reshape(sub_count, 2, 32, 32)
    dest = cover_tile[0, :, 0]
    row_off = offsets[0, :, 0]
    col_off = offsets[0, :, 1]
    chan_loc = channel[0]
    cap = 2 * sub_count // n_span
    onehot = (dest[:, None] == jnp.arange(n_span, dtype=jnp.int32)[None, :]).astype(jnp.float32)
    order = jnp.arange(sub_count, dtype=jnp.int32)
    lower = (order[:, None] > order[None, :]).astype(jnp.float32)
    earlier = jnp.dot(lower, onehot, preferred_element_type=jnp.float32)
    rank = jnp.sum(earlier * onehot, axis=1).astype(jnp.int32)
    slot = dest * cap + rank
    info = jnp.stack([jnp.ones_like(dest), row_off, col_off, chan_loc], 1).astype(jnp.bfloat16)
    rows = jnp.concatenate([patches.reshape(sub_count, 2048), info], axis=1)
    pick = (slot[None, :] == jnp.arange(n_span * cap, dtype=jnp.int32)[:, None]).astype(jnp.bfloat16)
    send = jnp.dot(pick, rows, preferred_element_type=jnp.float32).astype(jnp.bfloat16)
    got = lax.all_to_all(send.reshape(n_span, cap, 2052), "span", 0, 0, tiled=True)
    got_payload, got_meta = got[:, :, :2048], got[:, :, 2048:]
    slots = n_span * cap
    got_meta = got_meta.reshape(slots, 4).astype(jnp.int32)
    valid = got_meta[:, 0].astype(jnp.float32)
    weight = taylor_weights(got_meta[:, 3], freq_pos, channels) * valid[:, None]
    local = place_all(
        got_payload.reshape(slots, 2, 32, 32), weight, got_meta[:, 1], got_meta[:, 2]
    )
    local = local.reshape(NT, 1, 2, TILE, TILE)
    total = gathered_total(local, "freq")
    scale = TILE / (32.0 * math.sqrt(n_freq * sub_count))
    return total * scale


def solution(mesh):
    return jax.shard_map(
        body,
        mesh=mesh,
        in_specs=(
            P("freq", "span", None, None),
            P("freq", "span", None, None),
            P("freq", "span"),
            P("freq", "span", None),
            P("freq", "span", None),
            P("freq", "span"),
            P(),
        ),
        out_specs=P(None, "span", None, None, None),
        check_vma=False,
    )
```

```python
import math

import jax
import jax.numpy as jnp
from jax import lax
from jax.experimental import pallas as pl
from jax.experimental.pallas import tpu as pltpu
from jax.sharding import PartitionSpec as P

TILE = 128
NT = 2
CH_DEV = 16


def sent_together(arrays, axis, split_dim, concat_dim, along):
    widths = [a.shape[along] for a in arrays]
    both = jnp.concatenate(arrays, axis=along)
    whole = lax.all_to_all(both, axis, split_axis=split_dim, concat_axis=concat_dim, tiled=True)
    return tuple(jnp.split(whole, [sum(widths[:k]) for k in range(1, len(widths))], axis=along))


def gathered_total(shard, axis):
    n = lax.axis_size(axis)
    flat = shard.reshape(-1)
    size = flat.shape[0]
    per = -(-size // (n * 128)) * 128
    flat = jnp.pad(flat, (0, per * n - size))
    got = lax.all_to_all(flat.reshape(n, per // 128, 128), axis, 0, 0, tiled=True)
    part = got.sum(axis=0)
    spread = jnp.broadcast_to(part[None], (n, per // 128, 128))
    whole = lax.all_to_all(spread, axis, 0, 0, tiled=True)
    return whole.reshape(-1)[:size].reshape(shard.shape)


def cmul(ar, ai, br, bi):
    return ar * br - ai * bi, ar * bi + ai * br


def kernel_tables(angle, vis=None):
    c, s = jnp.cos(angle), jnp.sin(angle)
    w1 = (c, s)
    w2 = cmul(*w1, *w1)
    w4 = cmul(*w2, *w2)
    w8 = cmul(*w4, *w4)
    w16 = cmul(*w8, *w8)
    lo = (w16[0], -w16[1])
    if vis is not None:
        lo = cmul(*vis, *lo)
    one = (jnp.ones_like(c), jnp.zeros_like(c))
    small = [one, w1, w2, cmul(*w2, *w1)]
    big = []
    for j in range(8):
        q = lo
        for bit, wp in enumerate((w4, w8, w16)):
            if (j >> bit) & 1:
                q = cmul(*q, *wp)
        big.append(q)
    return small, big


def kernel_rows(small, big, b):
    p_r = jnp.concatenate([small[i % 4][0][b : b + 1] for i in range(8)], axis=0)
    p_i = jnp.concatenate([small[i % 4][1][b : b + 1] for i in range(8)], axis=0)
    first = lax.broadcasted_iota(jnp.int32, p_r.shape, 0) < 4
    res, ims = [], []
    for m in range(4):
        qa, qb = big[2 * m], big[2 * m + 1]
        q_r = jnp.where(first, qa[0][b : b + 1], qb[0][b : b + 1])
        q_i = jnp.where(first, qa[1][b : b + 1], qb[1][b : b + 1])
        r, i = cmul(q_r, q_i, p_r, p_i)
        res.append(r)
        ims.append(i)
    return jnp.concatenate(res + ims, axis=0).astype(jnp.bfloat16)


def s_kernel(coord_ref, vis_ref, count_ref, out):
    kk = coord_ref.shape[-1]
    step = -2.0 * math.pi / 32.0
    per = coord_ref.shape[0]
    sub = lax.broadcasted_iota(jnp.int32, (per, kk), 0)
    limit = jnp.zeros((per, kk), jnp.int32)
    for b in range(per):
        limit = jnp.where(sub == b, count_ref[0, pl.program_id(0) * per + b], limit)
    live = lax.broadcasted_iota(jnp.int32, (per, kk), 1) < limit
    scale_k = 1.0 / math.sqrt(kk)
    vis = vis_ref[...].astype(jnp.float32)
    coord = coord_ref[...]
    vr = jnp.where(live, vis[:, 0, :] * scale_k, 0.0)
    vi = jnp.where(live, vis[:, 1, :] * scale_k, 0.0)
    small_u, big_u = kernel_tables(step * coord[:, 0, :])
    small_v, big_v = kernel_tables(step * coord[:, 1, :], (vr, vi))
    for b in range(out.shape[0]):
        a = kernel_rows(small_u, big_u, b)
        bb = kernel_rows(small_v, big_v, b)
        out[b] = lax.dot_general(
            a, bb, (((1,), (1,)), ((), ())), preferred_element_type=jnp.float32
        )


def s_matrices(coords, vis, counts):
    n, _, kk = coords.shape
    per = 8
    both = pl.BlockSpec((per, 2, kk), lambda g: (g, 0, 0))
    return pl.pallas_call(
        s_kernel,
        grid=(n // per,),
        in_specs=[both, both, pl.BlockSpec(memory_space=pltpu.SMEM)],
        out_specs=pl.BlockSpec((per, 64, 64), lambda g: (g, 0, 0)),
        out_shape=jax.ShapeDtypeStruct((n, 64, 64), jnp.float32),
        cost_estimate=pl.CostEstimate(
            flops=2 * n * 64 * 64 * kk + 24 * n * 64 * kk,
            transcendentals=4 * n * kk,
            bytes_accessed=6 * n * 2 * kk + 4 * n * 64 * 64,
        ),
    )(coords, vis, counts)


def make_subgrids(vis_b, coord_b, count_b, taper):
    s_all = s_matrices(coord_b, vis_b, count_b.reshape(1, -1))
    s_re = s_all[:, :32, :32] - s_all[:, 32:, 32:]
    s_im = s_all[:, :32, 32:] + s_all[:, 32:, :32]
    x2 = jnp.concatenate([taper * s_re, taper * s_im], axis=1)
    centred = jnp.arange(32, dtype=jnp.float32) - 16.0
    angle = -2.0 * math.pi * centred[:, None] * centred[None, :] / 32.0
    f_re, f_im = (jnp.cos(angle), jnp.sin(angle))
    hp = lax.Precision.HIGHEST
    left = jnp.concatenate(
        [jnp.concatenate([f_re, -f_im], 1), jnp.concatenate([f_im, f_re], 1)], 0
    )
    y2 = jnp.einsum("ij,bjq->biq", left, x2, precision=hp)
    ycat = jnp.concatenate([y2[:, :32], y2[:, 32:]], axis=2)
    right = jnp.concatenate(
        [jnp.concatenate([f_re, f_im], 1), jnp.concatenate([-f_im, f_re], 1)], 0
    )
    z2 = jnp.einsum("baj,jk->bak", ycat, right, precision=hp)
    z = z2.reshape(z2.shape[0], 32, 2, 32).transpose(0, 2, 1, 3)
    return (z / 32.0).astype(jnp.bfloat16)


def taylor_weights(chan_local, freq_pos, channels):
    global_chan = (freq_pos * CH_DEV + chan_local).astype(jnp.float32)
    xval = (2.0 * global_chan + 1.0 - channels) / channels
    powers = jnp.arange(NT, dtype=jnp.float32)
    return jnp.where(powers[None, :] == 0.0, 1.0, xval[:, None] ** powers[None, :])


def place_all(patch, weight, rows, cols):
    bf, f32 = jnp.bfloat16, jnp.float32
    cells = jnp.arange(TILE, dtype=jnp.int32)
    small = jnp.arange(32, dtype=jnp.int32)
    col_hot = (small[None, :, None] + cols[:, None, None] == cells[None, None, :]).astype(bf)
    spread = jnp.einsum("scab,sbq->scaq", patch, col_hot, preferred_element_type=f32).astype(bf)
    row_hot = (cells[None, :, None] == rows[:, None, None] + small[None, None, :]).astype(f32)
    w_hi = weight.astype(bf)
    w_lo = (weight - w_hi.astype(f32)).astype(bf)
    w_both = jnp.stack([w_hi, w_lo], 0).astype(f32)
    lhs = (w_both.transpose(0, 2, 1)[:, :, None, :, None] * row_hot.transpose(1, 0, 2)[None, None]).astype(bf)
    out = jnp.einsum("htrsa,scaq->htcrq", lhs, spread, preferred_element_type=f32)
    return out[0] + out[1]


def body(visibilities, coords, vis_counts, cover_tile, offsets, channel, taper):
    n_span = lax.axis_size("span")
    n_freq = lax.axis_size("freq")
    channels = CH_DEV * n_freq
    freq_pos = lax.axis_index("freq")
    sub_count = visibilities.shape[1]
    groups = sub_count // 32
    vis_loc = visibilities[0].reshape(groups, 32, 2, -1)
    coord_loc = coords[0].reshape(groups, 32, 2, -1)
    count_loc = vis_counts[0].reshape(groups, 32)

    def block_work(inputs):
        return make_subgrids(inputs[0], inputs[1], inputs[2], taper)

    patches = lax.map(block_work, (vis_loc, coord_loc, count_loc)).reshape(sub_count, 2, 32, 32)
    dest = cover_tile[0, :, 0]
    row_off = offsets[0, :, 0]
    col_off = offsets[0, :, 1]
    chan_loc = channel[0]
    cap = 2 * sub_count // n_span
    onehot = (dest[:, None] == jnp.arange(n_span, dtype=jnp.int32)[None, :]).astype(jnp.float32)
    order = jnp.arange(sub_count, dtype=jnp.int32)
    lower = (order[:, None] > order[None, :]).astype(jnp.float32)
    earlier = jnp.dot(lower, onehot, preferred_element_type=jnp.float32)
    rank = jnp.sum(earlier * onehot, axis=1).astype(jnp.int32)
    slot = dest * cap + rank
    info = jnp.stack([jnp.ones_like(dest), row_off, col_off, chan_loc], 1).astype(jnp.bfloat16)
    rows = jnp.concatenate([patches.reshape(sub_count, 2048), info], axis=1)
    pick = (slot[None, :] == jnp.arange(n_span * cap, dtype=jnp.int32)[:, None]).astype(jnp.bfloat16)
    send = jnp.dot(pick, rows, preferred_element_type=jnp.float32).astype(jnp.bfloat16)
    got = lax.all_to_all(send.reshape(n_span, cap, 2052), "span", 0, 0, tiled=True)
    got_payload, got_meta = got[:, :, :2048], got[:, :, 2048:]
    slots = n_span * cap
    got_meta = got_meta.reshape(slots, 4).astype(jnp.int32)
    valid = got_meta[:, 0].astype(jnp.float32)
    weight = taylor_weights(got_meta[:, 3], freq_pos, channels) * valid[:, None]
    local = place_all(
        got_payload.reshape(slots, 2, 32, 32), weight, got_meta[:, 1], got_meta[:, 2]
    )
    local = local.reshape(NT, 1, 2, TILE, TILE)
    total = gathered_total(local, "freq")
    scale = TILE / (32.0 * math.sqrt(n_freq * sub_count))
    return total * scale


def solution(mesh):
    return jax.shard_map(
        body,
        mesh=mesh,
        in_specs=(
            P("freq", "span", None, None),
            P("freq", "span", None, None),
            P("freq", "span"),
            P("freq", "span", None),
            P("freq", "span", None),
            P("freq", "span"),
            P(),
        ),
        out_specs=P(None, "span", None, None, None),
        check_vma=False,
    )
```

```python
import math

import jax
import jax.numpy as jnp
from jax import lax
from jax.experimental import pallas as pl
from jax.experimental.pallas import tpu as pltpu
from jax.sharding import PartitionSpec as P

TILE = 128
NT = 2
CH_DEV = 16


def sent_together(arrays, axis, split_dim, concat_dim, along):
    widths = [a.shape[along] for a in arrays]
    both = jnp.concatenate(arrays, axis=along)
    whole = lax.all_to_all(both, axis, split_axis=split_dim, concat_axis=concat_dim, tiled=True)
    return tuple(jnp.split(whole, [sum(widths[:k]) for k in range(1, len(widths))], axis=along))


def gathered_total(shard, axis):
    n = lax.axis_size(axis)
    flat = shard.reshape(-1)
    size = flat.shape[0]
    per = -(-size // (n * 128)) * 128
    flat = jnp.pad(flat, (0, per * n - size))
    got = lax.all_to_all(flat.reshape(n, per // 128, 128), axis, 0, 0, tiled=True)
    part = got.sum(axis=0)
    spread = jnp.broadcast_to(part[None], (n, per // 128, 128))
    whole = lax.all_to_all(spread, axis, 0, 0, tiled=True)
    return whole.reshape(-1)[:size].reshape(shard.shape)


def cmul(ar, ai, br, bi):
    return ar * br - ai * bi, ar * bi + ai * br


def kernel_tables(angle, vis=None):
    c, s = jnp.cos(angle), jnp.sin(angle)
    w1 = (c, s)
    w2 = cmul(*w1, *w1)
    w4 = cmul(*w2, *w2)
    w8 = cmul(*w4, *w4)
    w16 = cmul(*w8, *w8)
    lo = (w16[0], -w16[1])
    if vis is not None:
        lo = cmul(*vis, *lo)
    one = (jnp.ones_like(c), jnp.zeros_like(c))
    small = [one, w1, w2, cmul(*w2, *w1)]
    big = []
    for j in range(8):
        q = lo
        for bit, wp in enumerate((w4, w8, w16)):
            if (j >> bit) & 1:
                q = cmul(*q, *wp)
        big.append(q)
    return small, big


def kernel_rows(small, big, b):
    p_r = jnp.concatenate([small[i % 4][0][b : b + 1] for i in range(8)], axis=0)
    p_i = jnp.concatenate([small[i % 4][1][b : b + 1] for i in range(8)], axis=0)
    first = lax.broadcasted_iota(jnp.int32, p_r.shape, 0) < 4
    res, ims = [], []
    for m in range(4):
        qa, qb = big[2 * m], big[2 * m + 1]
        q_r = jnp.where(first, qa[0][b : b + 1], qb[0][b : b + 1])
        q_i = jnp.where(first, qa[1][b : b + 1], qb[1][b : b + 1])
        r, i = cmul(q_r, q_i, p_r, p_i)
        res.append(r)
        ims.append(i)
    return jnp.concatenate(res + ims, axis=0).astype(jnp.bfloat16)


def s_kernel(coord_ref, vis_ref, count_ref, out):
    kk = coord_ref.shape[-1]
    step = -2.0 * math.pi / 32.0
    per = coord_ref.shape[0]
    sub = lax.broadcasted_iota(jnp.int32, (per, kk), 0)
    limit = jnp.zeros((per, kk), jnp.int32)
    for b in range(per):
        limit = jnp.where(sub == b, count_ref[0, pl.program_id(0) * per + b], limit)
    live = lax.broadcasted_iota(jnp.int32, (per, kk), 1) < limit
    scale_k = 1.0 / math.sqrt(kk)
    vis = vis_ref[...].astype(jnp.float32)
    coord = coord_ref[...]
    vr = jnp.where(live, vis[:, 0, :] * scale_k, 0.0)
    vi = jnp.where(live, vis[:, 1, :] * scale_k, 0.0)
    small_u, big_u = kernel_tables(step * coord[:, 0, :])
    small_v, big_v = kernel_tables(step * coord[:, 1, :], (vr, vi))
    for b in range(out.shape[0]):
        a = kernel_rows(small_u, big_u, b)
        bb = kernel_rows(small_v, big_v, b)
        out[b] = lax.dot_general(
            a, bb, (((1,), (1,)), ((), ())), preferred_element_type=jnp.float32
        )


def s_matrices(coords, vis, counts):
    n, _, kk = coords.shape
    per = 8
    both = pl.BlockSpec((per, 2, kk), lambda g: (g, 0, 0))
    return pl.pallas_call(
        s_kernel,
        grid=(n // per,),
        in_specs=[both, both, pl.BlockSpec(memory_space=pltpu.SMEM)],
        out_specs=pl.BlockSpec((per, 64, 64), lambda g: (g, 0, 0)),
        out_shape=jax.ShapeDtypeStruct((n, 64, 64), jnp.float32),
        cost_estimate=pl.CostEstimate(
            flops=2 * n * 64 * 64 * kk + 24 * n * 64 * kk,
            transcendentals=4 * n * kk,
            bytes_accessed=6 * n * 2 * kk + 4 * n * 64 * 64,
        ),
    )(coords, vis, counts)


def make_subgrids(vis_b, coord_b, count_b, taper):
    s_all = s_matrices(coord_b, vis_b, count_b.reshape(1, -1))
    s_re = s_all[:, :32, :32] - s_all[:, 32:, 32:]
    s_im = s_all[:, :32, 32:] + s_all[:, 32:, :32]
    x2 = jnp.concatenate([taper * s_re, taper * s_im], axis=1)
    centred = jnp.arange(32, dtype=jnp.float32) - 16.0
    angle = -2.0 * math.pi * centred[:, None] * centred[None, :] / 32.0
    f_re, f_im = (jnp.cos(angle), jnp.sin(angle))
    hp = lax.Precision.HIGHEST
    left = jnp.concatenate(
        [jnp.concatenate([f_re, -f_im], 1), jnp.concatenate([f_im, f_re], 1)], 0
    )
    y2 = jnp.einsum("ij,bjq->biq", left, x2, precision=hp)
    ycat = jnp.concatenate([y2[:, :32], y2[:, 32:]], axis=2)
    right = jnp.concatenate(
        [jnp.concatenate([f_re, f_im], 1), jnp.concatenate([-f_im, f_re], 1)], 0
    )
    z2 = jnp.einsum("baj,jk->bak", ycat, right, precision=hp)
    z = z2.reshape(z2.shape[0], 32, 2, 32).transpose(0, 2, 1, 3)
    return (z / 32.0).astype(jnp.bfloat16)


def taylor_weights(chan_local, freq_pos, channels):
    global_chan = (freq_pos * CH_DEV + chan_local).astype(jnp.float32)
    xval = (2.0 * global_chan + 1.0 - channels) / channels
    powers = jnp.arange(NT, dtype=jnp.float32)
    return jnp.where(powers[None, :] == 0.0, 1.0, xval[:, None] ** powers[None, :])


def place_all(patch, weight, rows, cols):
    bf, f32 = jnp.bfloat16, jnp.float32
    cells = jnp.arange(TILE, dtype=jnp.int32)
    small = jnp.arange(32, dtype=jnp.int32)
    col_hot = (small[None, :, None] + cols[:, None, None] == cells[None, None, :]).astype(bf)
    spread = jnp.einsum("scab,sbq->scaq", patch, col_hot, preferred_element_type=f32).astype(bf)
    row_hot = (cells[None, :, None] == rows[:, None, None] + small[None, None, :]).astype(f32)
    w_hi = weight.astype(bf)
    w_lo = (weight - w_hi.astype(f32)).astype(bf)
    w_both = jnp.stack([w_hi, w_lo], 0).astype(f32)
    lhs = (w_both.transpose(0, 2, 1)[:, :, None, :, None] * row_hot.transpose(1, 0, 2)[None, None]).astype(bf)
    out = jnp.einsum("htrsa,scaq->htcrq", lhs, spread, preferred_element_type=f32)
    return out[0] + out[1]


def body(visibilities, coords, vis_counts, cover_tile, offsets, channel, taper):
    n_span = lax.axis_size("span")
    n_freq = lax.axis_size("freq")
    channels = CH_DEV * n_freq
    freq_pos = lax.axis_index("freq")
    sub_count = visibilities.shape[1]
    groups = sub_count // 32
    vis_loc = visibilities[0].reshape(groups, 32, 2, -1)
    coord_loc = coords[0].reshape(groups, 32, 2, -1)
    count_loc = vis_counts[0].reshape(groups, 32)

    def block_work(inputs):
        return make_subgrids(inputs[0], inputs[1], inputs[2], taper)

    patches = lax.map(block_work, (vis_loc, coord_loc, count_loc)).reshape(sub_count, 2, 32, 32)
    dest = cover_tile[0, :, 0]
    row_off = offsets[0, :, 0]
    col_off = offsets[0, :, 1]
    chan_loc = channel[0]
    cap = 2 * sub_count // n_span
    order = jnp.arange(sub_count, dtype=jnp.int32)
    before = (dest[:, None] == dest[None, :]) & (order[:, None] > order[None, :])
    rank = jnp.sum(before.astype(jnp.int32), axis=1)
    slot = dest * cap + rank
    info = jnp.stack([jnp.ones_like(dest), row_off, col_off, chan_loc], 1).astype(jnp.bfloat16)
    rows = jnp.concatenate([patches.reshape(sub_count, 2048), info], axis=1)
    pick = (slot[None, :] == jnp.arange(n_span * cap, dtype=jnp.int32)[:, None]).astype(jnp.bfloat16)
    send = jnp.dot(pick, rows, preferred_element_type=jnp.float32).astype(jnp.bfloat16)
    got = lax.all_to_all(send.reshape(n_span, cap, 2052), "span", 0, 0, tiled=True)
    got_payload, got_meta = got[:, :, :2048], got[:, :, 2048:]
    slots = n_span * cap
    got_meta = got_meta.reshape(slots, 4).astype(jnp.int32)
    valid = got_meta[:, 0].astype(jnp.float32)
    weight = taylor_weights(got_meta[:, 3], freq_pos, channels) * valid[:, None]
    local = place_all(
        got_payload.reshape(slots, 2, 32, 32), weight, got_meta[:, 1], got_meta[:, 2]
    )
    local = local.reshape(NT, 1, 2, TILE, TILE)
    total = gathered_total(local, "freq")
    scale = TILE / (32.0 * math.sqrt(n_freq * sub_count))
    return total * scale


def solution(mesh):
    return jax.shard_map(
        body,
        mesh=mesh,
        in_specs=(
            P("freq", "span", None, None),
            P("freq", "span", None, None),
            P("freq", "span"),
            P("freq", "span", None),
            P("freq", "span", None),
            P("freq", "span"),
            P(),
        ),
        out_specs=P(None, "span", None, None, None),
        check_vma=False,
    )
```

```python
import math

import jax
import jax.numpy as jnp
from jax import lax
from jax.experimental import pallas as pl
from jax.experimental.pallas import tpu as pltpu
from jax.sharding import PartitionSpec as P

TILE = 128
NT = 2
CH_DEV = 16


def sent_together(arrays, axis, split_dim, concat_dim, along):
    widths = [a.shape[along] for a in arrays]
    both = jnp.concatenate(arrays, axis=along)
    whole = lax.all_to_all(both, axis, split_axis=split_dim, concat_axis=concat_dim, tiled=True)
    return tuple(jnp.split(whole, [sum(widths[:k]) for k in range(1, len(widths))], axis=along))


def gathered_total(shard, axis):
    n = lax.axis_size(axis)
    flat = shard.reshape(-1)
    size = flat.shape[0]
    per = -(-size // (n * 128)) * 128
    flat = jnp.pad(flat, (0, per * n - size))
    got = lax.all_to_all(flat.reshape(n, per // 128, 128), axis, 0, 0, tiled=True)
    part = got.sum(axis=0)
    spread = jnp.broadcast_to(part[None], (n, per // 128, 128))
    whole = lax.all_to_all(spread, axis, 0, 0, tiled=True)
    return whole.reshape(-1)[:size].reshape(shard.shape)


def cmul(ar, ai, br, bi):
    return ar * br - ai * bi, ar * bi + ai * br


def kernel_tables(angle, vis=None):
    c, s = jnp.cos(angle), jnp.sin(angle)
    w1 = (c, s)
    w2 = cmul(*w1, *w1)
    w4 = cmul(*w2, *w2)
    w8 = cmul(*w4, *w4)
    w16 = cmul(*w8, *w8)
    lo = (w16[0], -w16[1])
    if vis is not None:
        lo = cmul(*vis, *lo)
    one = (jnp.ones_like(c), jnp.zeros_like(c))
    small = [one, w1, w2, cmul(*w2, *w1)]
    big = []
    for j in range(8):
        q = lo
        for bit, wp in enumerate((w4, w8, w16)):
            if (j >> bit) & 1:
                q = cmul(*q, *wp)
        big.append(q)
    return small, big


def kernel_rows(small, big, b):
    p_r = jnp.concatenate([small[i % 4][0][b : b + 1] for i in range(8)], axis=0)
    p_i = jnp.concatenate([small[i % 4][1][b : b + 1] for i in range(8)], axis=0)
    first = lax.broadcasted_iota(jnp.int32, p_r.shape, 0) < 4
    res, ims = [], []
    for m in range(4):
        qa, qb = big[2 * m], big[2 * m + 1]
        q_r = jnp.where(first, qa[0][b : b + 1], qb[0][b : b + 1])
        q_i = jnp.where(first, qa[1][b : b + 1], qb[1][b : b + 1])
        r, i = cmul(q_r, q_i, p_r, p_i)
        res.append(r)
        ims.append(i)
    return jnp.concatenate(res + ims, axis=0).astype(jnp.bfloat16)


def s_kernel(coord_ref, vis_ref, count_ref, taper_ref, out):
    kk = coord_ref.shape[-1]
    step = -2.0 * math.pi / 32.0
    per = coord_ref.shape[0]
    sub = lax.broadcasted_iota(jnp.int32, (per, kk), 0)
    limit = jnp.zeros((per, kk), jnp.int32)
    for b in range(per):
        limit = jnp.where(sub == b, count_ref[0, pl.program_id(0) * per + b], limit)
    live = lax.broadcasted_iota(jnp.int32, (per, kk), 1) < limit
    scale_k = 1.0 / math.sqrt(kk)
    vis = vis_ref[...].astype(jnp.float32)
    coord = coord_ref[...]
    vr = jnp.where(live, vis[:, 0, :] * scale_k, 0.0)
    vi = jnp.where(live, vis[:, 1, :] * scale_k, 0.0)
    small_u, big_u = kernel_tables(step * coord[:, 0, :])
    small_v, big_v = kernel_tables(step * coord[:, 1, :], (vr, vi))
    tp = taper_ref[...]
    for b in range(out.shape[0]):
        a = kernel_rows(small_u, big_u, b)
        bb = kernel_rows(small_v, big_v, b)
        sm = lax.dot_general(a, bb, (((1,), (1,)), ((), ())), preferred_element_type=jnp.float32)
        x_re = tp * (sm[:32, :32] - sm[32:, 32:])
        x_im = tp * (sm[:32, 32:] + sm[32:, :32])
        out[b] = jnp.concatenate([x_re, x_im], axis=0)


def s_matrices(coords, vis, counts, taper):
    n, _, kk = coords.shape
    per = 8
    both = pl.BlockSpec((per, 2, kk), lambda g: (g, 0, 0))
    return pl.pallas_call(
        s_kernel,
        grid=(n // per,),
        in_specs=[
            both,
            both,
            pl.BlockSpec(memory_space=pltpu.SMEM),
            pl.BlockSpec((32, 32), lambda g: (0, 0)),
        ],
        out_specs=pl.BlockSpec((per, 64, 32), lambda g: (g, 0, 0)),
        out_shape=jax.ShapeDtypeStruct((n, 64, 32), jnp.float32),
        cost_estimate=pl.CostEstimate(
            flops=2 * n * 64 * 64 * kk + 24 * n * 64 * kk,
            transcendentals=4 * n * kk,
            bytes_accessed=6 * n * 2 * kk + 4 * n * 64 * 64,
        ),
    )(coords, vis, counts, taper)


def make_subgrids(vis_b, coord_b, count_b, taper):
    x2 = s_matrices(coord_b, vis_b, count_b.reshape(1, -1), taper)
    centred = jnp.arange(32, dtype=jnp.float32) - 16.0
    angle = -2.0 * math.pi * centred[:, None] * centred[None, :] / 32.0
    f_re, f_im = (jnp.cos(angle), jnp.sin(angle))
    hp = lax.Precision.HIGHEST
    left = jnp.concatenate(
        [jnp.concatenate([f_re, -f_im], 1), jnp.concatenate([f_im, f_re], 1)], 0
    )
    y2 = jnp.einsum("ij,bjq->biq", left, x2, precision=hp)
    ycat = jnp.concatenate([y2[:, :32], y2[:, 32:]], axis=2)
    right = jnp.concatenate(
        [jnp.concatenate([f_re, f_im], 1), jnp.concatenate([-f_im, f_re], 1)], 0
    )
    z2 = jnp.einsum("baj,jk->bak", ycat, right, precision=hp)
    z = z2.reshape(z2.shape[0], 32, 2, 32).transpose(0, 2, 1, 3)
    return (z / 32.0).astype(jnp.bfloat16)


def taylor_weights(chan_local, freq_pos, channels):
    global_chan = (freq_pos * CH_DEV + chan_local).astype(jnp.float32)
    xval = (2.0 * global_chan + 1.0 - channels) / channels
    powers = jnp.arange(NT, dtype=jnp.float32)
    return jnp.where(powers[None, :] == 0.0, 1.0, xval[:, None] ** powers[None, :])


def place_all(patch, weight, rows, cols):
    bf, f32 = jnp.bfloat16, jnp.float32
    cells = jnp.arange(TILE, dtype=jnp.int32)
    small = jnp.arange(32, dtype=jnp.int32)
    col_hot = (small[None, :, None] + cols[:, None, None] == cells[None, None, :]).astype(bf)
    spread = jnp.einsum("scab,sbq->scaq", patch, col_hot, preferred_element_type=f32).astype(bf)
    row_hot = (cells[None, :, None] == rows[:, None, None] + small[None, None, :]).astype(f32)
    w_hi = weight.astype(bf)
    w_lo = (weight - w_hi.astype(f32)).astype(bf)
    w_both = jnp.stack([w_hi, w_lo], 0).astype(f32)
    lhs = (w_both.transpose(0, 2, 1)[:, :, None, :, None] * row_hot.transpose(1, 0, 2)[None, None]).astype(bf)
    out = jnp.einsum("htrsa,scaq->htcrq", lhs, spread, preferred_element_type=f32)
    return out[0] + out[1]


def body(visibilities, coords, vis_counts, cover_tile, offsets, channel, taper):
    n_span = lax.axis_size("span")
    n_freq = lax.axis_size("freq")
    channels = CH_DEV * n_freq
    freq_pos = lax.axis_index("freq")
    sub_count = visibilities.shape[1]
    groups = sub_count // 32
    vis_loc = visibilities[0].reshape(groups, 32, 2, -1)
    coord_loc = coords[0].reshape(groups, 32, 2, -1)
    count_loc = vis_counts[0].reshape(groups, 32)

    def block_work(inputs):
        return make_subgrids(inputs[0], inputs[1], inputs[2], taper)

    patches = lax.map(block_work, (vis_loc, coord_loc, count_loc)).reshape(sub_count, 2, 32, 32)
    dest = cover_tile[0, :, 0]
    row_off = offsets[0, :, 0]
    col_off = offsets[0, :, 1]
    chan_loc = channel[0]
    cap = 2 * sub_count // n_span
    order = jnp.arange(sub_count, dtype=jnp.int32)
    before = (dest[:, None] == dest[None, :]) & (order[:, None] > order[None, :])
    rank = jnp.sum(before.astype(jnp.int32), axis=1)
    slot = dest * cap + rank
    info = jnp.stack([jnp.ones_like(dest), row_off, col_off, chan_loc], 1).astype(jnp.bfloat16)
    rows = jnp.concatenate([patches.reshape(sub_count, 2048), info], axis=1)
    pick = (slot[None, :] == jnp.arange(n_span * cap, dtype=jnp.int32)[:, None]).astype(jnp.bfloat16)
    send = jnp.dot(pick, rows, preferred_element_type=jnp.float32).astype(jnp.bfloat16)
    got = lax.all_to_all(send.reshape(n_span, cap, 2052), "span", 0, 0, tiled=True)
    got_payload, got_meta = got[:, :, :2048], got[:, :, 2048:]
    slots = n_span * cap
    got_meta = got_meta.reshape(slots, 4).astype(jnp.int32)
    valid = got_meta[:, 0].astype(jnp.float32)
    weight = taylor_weights(got_meta[:, 3], freq_pos, channels) * valid[:, None]
    local = place_all(
        got_payload.reshape(slots, 2, 32, 32), weight, got_meta[:, 1], got_meta[:, 2]
    )
    local = local.reshape(NT, 1, 2, TILE, TILE)
    total = gathered_total(local, "freq")
    scale = TILE / (32.0 * math.sqrt(n_freq * sub_count))
    return total * scale


def solution(mesh):
    return jax.shard_map(
        body,
        mesh=mesh,
        in_specs=(
            P("freq", "span", None, None),
            P("freq", "span", None, None),
            P("freq", "span"),
            P("freq", "span", None),
            P("freq", "span", None),
            P("freq", "span"),
            P(),
        ),
        out_specs=P(None, "span", None, None, None),
        check_vma=False,
    )
```

```python
import math

import jax
import jax.numpy as jnp
from jax import lax
from jax.experimental import pallas as pl
from jax.experimental.pallas import tpu as pltpu
from jax.sharding import PartitionSpec as P

TILE = 128
NT = 2
CH_DEV = 16


def sent_together(arrays, axis, split_dim, concat_dim, along):
    widths = [a.shape[along] for a in arrays]
    both = jnp.concatenate(arrays, axis=along)
    whole = lax.all_to_all(both, axis, split_axis=split_dim, concat_axis=concat_dim, tiled=True)
    return tuple(jnp.split(whole, [sum(widths[:k]) for k in range(1, len(widths))], axis=along))


def gathered_total(shard, axis):
    n = lax.axis_size(axis)
    flat = shard.reshape(-1)
    size = flat.shape[0]
    per = -(-size // (n * 128)) * 128
    flat = jnp.pad(flat, (0, per * n - size))
    got = lax.all_to_all(flat.reshape(n, per // 128, 128), axis, 0, 0, tiled=True)
    part = got.sum(axis=0)
    spread = jnp.broadcast_to(part.astype(jnp.bfloat16)[None], (n, per // 128, 128))
    whole = lax.all_to_all(spread, axis, 0, 0, tiled=True).astype(jnp.float32)
    return whole.reshape(-1)[:size].reshape(shard.shape)


def cmul(ar, ai, br, bi):
    return ar * br - ai * bi, ar * bi + ai * br


def kernel_tables(angle, vis=None):
    c, s = jnp.cos(angle), jnp.sin(angle)
    w1 = (c, s)
    w2 = cmul(*w1, *w1)
    w4 = cmul(*w2, *w2)
    w8 = cmul(*w4, *w4)
    w16 = cmul(*w8, *w8)
    lo = (w16[0], -w16[1])
    if vis is not None:
        lo = cmul(*vis, *lo)
    one = (jnp.ones_like(c), jnp.zeros_like(c))
    small = [one, w1, w2, cmul(*w2, *w1)]
    big = []
    for j in range(8):
        q = lo
        for bit, wp in enumerate((w4, w8, w16)):
            if (j >> bit) & 1:
                q = cmul(*q, *wp)
        big.append(q)
    return small, big


def kernel_rows(small, big, b):
    p_r = jnp.concatenate([small[i % 4][0][b : b + 1] for i in range(8)], axis=0)
    p_i = jnp.concatenate([small[i % 4][1][b : b + 1] for i in range(8)], axis=0)
    first = lax.broadcasted_iota(jnp.int32, p_r.shape, 0) < 4
    res, ims = [], []
    for m in range(4):
        qa, qb = big[2 * m], big[2 * m + 1]
        q_r = jnp.where(first, qa[0][b : b + 1], qb[0][b : b + 1])
        q_i = jnp.where(first, qa[1][b : b + 1], qb[1][b : b + 1])
        r, i = cmul(q_r, q_i, p_r, p_i)
        res.append(r)
        ims.append(i)
    return jnp.concatenate(res + ims, axis=0).astype(jnp.bfloat16)


def s_kernel(coord_ref, vis_ref, count_ref, out):
    kk = coord_ref.shape[-1]
    step = -2.0 * math.pi / 32.0
    per = coord_ref.shape[0]
    sub = lax.broadcasted_iota(jnp.int32, (per, kk), 0)
    limit = jnp.zeros((per, kk), jnp.int32)
    for b in range(per):
        limit = jnp.where(sub == b, count_ref[0, pl.program_id(0) * per + b], limit)
    live = lax.broadcasted_iota(jnp.int32, (per, kk), 1) < limit
    scale_k = 1.0 / math.sqrt(kk)
    vis = vis_ref[...].astype(jnp.float32)
    coord = coord_ref[...]
    vr = jnp.where(live, vis[:, 0, :] * scale_k, 0.0)
    vi = jnp.where(live, vis[:, 1, :] * scale_k, 0.0)
    small_u, big_u = kernel_tables(step * coord[:, 0, :])
    small_v, big_v = kernel_tables(step * coord[:, 1, :], (vr, vi))
    for b in range(out.shape[0]):
        a = kernel_rows(small_u, big_u, b)
        bb = kernel_rows(small_v, big_v, b)
        out[b] = lax.dot_general(
            a, bb, (((1,), (1,)), ((), ())), preferred_element_type=jnp.float32
        )


def s_matrices(coords, vis, counts):
    n, _, kk = coords.shape
    per = 8
    both = pl.BlockSpec((per, 2, kk), lambda g: (g, 0, 0))
    return pl.pallas_call(
        s_kernel,
        grid=(n // per,),
        in_specs=[both, both, pl.BlockSpec(memory_space=pltpu.SMEM)],
        out_specs=pl.BlockSpec((per, 64, 64), lambda g: (g, 0, 0)),
        out_shape=jax.ShapeDtypeStruct((n, 64, 64), jnp.float32),
        cost_estimate=pl.CostEstimate(
            flops=2 * n * 64 * 64 * kk + 24 * n * 64 * kk,
            transcendentals=4 * n * kk,
            bytes_accessed=6 * n * 2 * kk + 4 * n * 64 * 64,
        ),
    )(coords, vis, counts)


def make_subgrids(vis_b, coord_b, count_b, taper):
    s_all = s_matrices(coord_b, vis_b, count_b.reshape(1, -1))
    s_re = s_all[:, :32, :32] - s_all[:, 32:, 32:]
    s_im = s_all[:, :32, 32:] + s_all[:, 32:, :32]
    x2 = jnp.concatenate([taper * s_re, taper * s_im], axis=1)
    centred = jnp.arange(32, dtype=jnp.float32) - 16.0
    angle = -2.0 * math.pi * centred[:, None] * centred[None, :] / 32.0
    f_re, f_im = (jnp.cos(angle), jnp.sin(angle))
    hp = lax.Precision.HIGHEST
    left = jnp.concatenate(
        [jnp.concatenate([f_re, -f_im], 1), jnp.concatenate([f_im, f_re], 1)], 0
    )
    y2 = jnp.einsum("ij,bjq->biq", left, x2, precision=hp)
    ycat = jnp.concatenate([y2[:, :32], y2[:, 32:]], axis=2)
    right = jnp.concatenate(
        [jnp.concatenate([f_re, f_im], 1), jnp.concatenate([-f_im, f_re], 1)], 0
    )
    z2 = jnp.einsum("baj,jk->bak", ycat, right, precision=hp)
    z = z2.reshape(z2.shape[0], 32, 2, 32).transpose(0, 2, 1, 3)
    return (z / 32.0).astype(jnp.bfloat16)


def taylor_weights(chan_local, freq_pos, channels):
    global_chan = (freq_pos * CH_DEV + chan_local).astype(jnp.float32)
    xval = (2.0 * global_chan + 1.0 - channels) / channels
    powers = jnp.arange(NT, dtype=jnp.float32)
    return jnp.where(powers[None, :] == 0.0, 1.0, xval[:, None] ** powers[None, :])


def place_all(patch, weight, rows, cols):
    bf, f32 = jnp.bfloat16, jnp.float32
    cells = jnp.arange(TILE, dtype=jnp.int32)
    small = jnp.arange(32, dtype=jnp.int32)
    col_hot = (small[None, :, None] + cols[:, None, None] == cells[None, None, :]).astype(bf)
    spread = jnp.einsum("scab,sbq->scaq", patch, col_hot, preferred_element_type=f32).astype(bf)
    row_hot = (cells[None, :, None] == rows[:, None, None] + small[None, None, :]).astype(f32)
    w_hi = weight.astype(bf)
    w_lo = (weight - w_hi.astype(f32)).astype(bf)
    w_both = jnp.stack([w_hi, w_lo], 0).astype(f32)
    lhs = (w_both.transpose(0, 2, 1)[:, :, None, :, None] * row_hot.transpose(1, 0, 2)[None, None]).astype(bf)
    out = jnp.einsum("htrsa,scaq->htcrq", lhs, spread, preferred_element_type=f32)
    return out[0] + out[1]


def body(visibilities, coords, vis_counts, cover_tile, offsets, channel, taper):
    n_span = lax.axis_size("span")
    n_freq = lax.axis_size("freq")
    channels = CH_DEV * n_freq
    freq_pos = lax.axis_index("freq")
    sub_count = visibilities.shape[1]
    groups = sub_count // 32
    vis_loc = visibilities[0].reshape(groups, 32, 2, -1)
    coord_loc = coords[0].reshape(groups, 32, 2, -1)
    count_loc = vis_counts[0].reshape(groups, 32)

    def block_work(inputs):
        return make_subgrids(inputs[0], inputs[1], inputs[2], taper)

    patches = lax.map(block_work, (vis_loc, coord_loc, count_loc)).reshape(sub_count, 2, 32, 32)
    dest = cover_tile[0, :, 0]
    row_off = offsets[0, :, 0]
    col_off = offsets[0, :, 1]
    chan_loc = channel[0]
    cap = 2 * sub_count // n_span
    order = jnp.arange(sub_count, dtype=jnp.int32)
    before = (dest[:, None] == dest[None, :]) & (order[:, None] > order[None, :])
    rank = jnp.sum(before.astype(jnp.int32), axis=1)
    slot = dest * cap + rank
    info = jnp.stack([jnp.ones_like(dest), row_off, col_off, chan_loc], 1).astype(jnp.bfloat16)
    rows = jnp.concatenate([patches.reshape(sub_count, 2048), info], axis=1)
    pick = (slot[None, :] == jnp.arange(n_span * cap, dtype=jnp.int32)[:, None]).astype(jnp.bfloat16)
    send = jnp.dot(pick, rows, preferred_element_type=jnp.float32).astype(jnp.bfloat16)
    got = lax.all_to_all(send.reshape(n_span, cap, 2052), "span", 0, 0, tiled=True)
    got_payload, got_meta = got[:, :, :2048], got[:, :, 2048:]
    slots = n_span * cap
    got_meta = got_meta.reshape(slots, 4).astype(jnp.int32)
    valid = got_meta[:, 0].astype(jnp.float32)
    weight = taylor_weights(got_meta[:, 3], freq_pos, channels) * valid[:, None]
    local = place_all(
        got_payload.reshape(slots, 2, 32, 32), weight, got_meta[:, 1], got_meta[:, 2]
    )
    local = local.reshape(NT, 1, 2, TILE, TILE)
    total = gathered_total(local, "freq")
    scale = TILE / (32.0 * math.sqrt(n_freq * sub_count))
    return total * scale


def solution(mesh):
    return jax.shard_map(
        body,
        mesh=mesh,
        in_specs=(
            P("freq", "span", None, None),
            P("freq", "span", None, None),
            P("freq", "span"),
            P("freq", "span", None),
            P("freq", "span", None),
            P("freq", "span"),
            P(),
        ),
        out_specs=P(None, "span", None, None, None),
        check_vma=False,
    )
```

```python
import math

import jax
import jax.numpy as jnp
from jax import lax
from jax.experimental import pallas as pl
from jax.experimental.pallas import tpu as pltpu
from jax.sharding import PartitionSpec as P

TILE = 128
NT = 2
CH_DEV = 16


def sent_together(arrays, axis, split_dim, concat_dim, along):
    widths = [a.shape[along] for a in arrays]
    both = jnp.concatenate(arrays, axis=along)
    whole = lax.all_to_all(both, axis, split_axis=split_dim, concat_axis=concat_dim, tiled=True)
    return tuple(jnp.split(whole, [sum(widths[:k]) for k in range(1, len(widths))], axis=along))


def gathered_total(shard, axis):
    n = lax.axis_size(axis)
    flat = shard.reshape(-1)
    size = flat.shape[0]
    per = -(-size // (n * 128)) * 128
    flat = jnp.pad(flat, (0, per * n - size))
    got = lax.all_to_all(flat.reshape(n, per // 128, 128), axis, 0, 0, tiled=True)
    part = got.sum(axis=0)
    spread = jnp.broadcast_to(part.astype(jnp.bfloat16)[None], (n, per // 128, 128))
    whole = lax.all_to_all(spread, axis, 0, 0, tiled=True).astype(jnp.float32)
    return whole.reshape(-1)[:size].reshape(shard.shape)


def cmul(ar, ai, br, bi):
    return ar * br - ai * bi, ar * bi + ai * br


def kernel_tables(angle, vis=None):
    c, s = jnp.cos(angle), jnp.sin(angle)
    w1 = (c, s)
    w2 = cmul(*w1, *w1)
    w4 = cmul(*w2, *w2)
    w8 = cmul(*w4, *w4)
    w16 = cmul(*w8, *w8)
    lo = (w16[0], -w16[1])
    if vis is not None:
        lo = cmul(*vis, *lo)
    one = (jnp.ones_like(c), jnp.zeros_like(c))
    small = [one, w1, w2, cmul(*w2, *w1)]
    big = []
    for j in range(8):
        q = lo
        for bit, wp in enumerate((w4, w8, w16)):
            if (j >> bit) & 1:
                q = cmul(*q, *wp)
        big.append(q)
    return small, big


def kernel_rows(small, big, b):
    p_r = jnp.concatenate([small[i % 4][0][b : b + 1] for i in range(8)], axis=0)
    p_i = jnp.concatenate([small[i % 4][1][b : b + 1] for i in range(8)], axis=0)
    first = lax.broadcasted_iota(jnp.int32, p_r.shape, 0) < 4
    res, ims = [], []
    for m in range(4):
        qa, qb = big[2 * m], big[2 * m + 1]
        q_r = jnp.where(first, qa[0][b : b + 1], qb[0][b : b + 1])
        q_i = jnp.where(first, qa[1][b : b + 1], qb[1][b : b + 1])
        r, i = cmul(q_r, q_i, p_r, p_i)
        res.append(r)
        ims.append(i)
    return jnp.concatenate(res + ims, axis=0).astype(jnp.bfloat16)


def s_kernel(coord_ref, vis_ref, count_ref, out):
    kk = coord_ref.shape[-1]
    step = -2.0 * math.pi / 32.0
    per = coord_ref.shape[0]
    sub = lax.broadcasted_iota(jnp.int32, (per, kk), 0)
    limit = jnp.zeros((per, kk), jnp.int32)
    for b in range(per):
        limit = jnp.where(sub == b, count_ref[0, pl.program_id(0) * per + b], limit)
    live = lax.broadcasted_iota(jnp.int32, (per, kk), 1) < limit
    scale_k = 1.0 / math.sqrt(kk)
    vis = vis_ref[...].astype(jnp.float32)
    coord = coord_ref[...]
    vr = jnp.where(live, vis[:, 0, :] * scale_k, 0.0)
    vi = jnp.where(live, vis[:, 1, :] * scale_k, 0.0)
    small_u, big_u = kernel_tables(step * coord[:, 0, :])
    small_v, big_v = kernel_tables(step * coord[:, 1, :], (vr, vi))
    for b in range(out.shape[0]):
        a = kernel_rows(small_u, big_u, b)
        bb = kernel_rows(small_v, big_v, b)
        out[b] = lax.dot_general(
            a, bb, (((1,), (1,)), ((), ())), preferred_element_type=jnp.float32
        )


def s_matrices(coords, vis, counts):
    n, _, kk = coords.shape
    per = 8
    both = pl.BlockSpec((per, 2, kk), lambda g: (g, 0, 0))
    return pl.pallas_call(
        s_kernel,
        grid=(n // per,),
        in_specs=[both, both, pl.BlockSpec(memory_space=pltpu.SMEM)],
        out_specs=pl.BlockSpec((per, 64, 64), lambda g: (g, 0, 0)),
        out_shape=jax.ShapeDtypeStruct((n, 64, 64), jnp.float32),
        cost_estimate=pl.CostEstimate(
            flops=2 * n * 64 * 64 * kk + 24 * n * 64 * kk,
            transcendentals=4 * n * kk,
            bytes_accessed=6 * n * 2 * kk + 4 * n * 64 * 64,
        ),
    )(coords, vis, counts)


def make_subgrids(vis_b, coord_b, count_b, taper):
    s_all = s_matrices(coord_b, vis_b, count_b.reshape(1, -1))
    s_re = s_all[:, :32, :32] - s_all[:, 32:, 32:]
    s_im = s_all[:, :32, 32:] + s_all[:, 32:, :32]
    x2 = jnp.concatenate([taper * s_re, taper * s_im], axis=1)
    centred = jnp.arange(32, dtype=jnp.float32) - 16.0
    angle = -2.0 * math.pi * centred[:, None] * centred[None, :] / 32.0
    f_re, f_im = (jnp.cos(angle), jnp.sin(angle))
    hp = lax.Precision.HIGH
    left = jnp.concatenate(
        [jnp.concatenate([f_re, -f_im], 1), jnp.concatenate([f_im, f_re], 1)], 0
    )
    y2 = jnp.einsum("ij,bjq->biq", left, x2, precision=hp)
    ycat = jnp.concatenate([y2[:, :32], y2[:, 32:]], axis=2)
    right = jnp.concatenate(
        [jnp.concatenate([f_re, f_im], 1), jnp.concatenate([-f_im, f_re], 1)], 0
    )
    z2 = jnp.einsum("baj,jk->bak", ycat, right, precision=hp)
    z = z2.reshape(z2.shape[0], 32, 2, 32).transpose(0, 2, 1, 3)
    return (z / 32.0).astype(jnp.bfloat16)


def taylor_weights(chan_local, freq_pos, channels):
    global_chan = (freq_pos * CH_DEV + chan_local).astype(jnp.float32)
    xval = (2.0 * global_chan + 1.0 - channels) / channels
    powers = jnp.arange(NT, dtype=jnp.float32)
    return jnp.where(powers[None, :] == 0.0, 1.0, xval[:, None] ** powers[None, :])


def place_all(patch, weight, rows, cols):
    bf, f32 = jnp.bfloat16, jnp.float32
    cells = jnp.arange(TILE, dtype=jnp.int32)
    small = jnp.arange(32, dtype=jnp.int32)
    col_hot = (small[None, :, None] + cols[:, None, None] == cells[None, None, :]).astype(bf)
    spread = jnp.einsum("scab,sbq->scaq", patch, col_hot, preferred_element_type=f32).astype(bf)
    row_hot = (cells[None, :, None] == rows[:, None, None] + small[None, None, :]).astype(f32)
    w_hi = weight.astype(bf)
    w_lo = (weight - w_hi.astype(f32)).astype(bf)
    w_both = jnp.stack([w_hi, w_lo], 0).astype(f32)
    lhs = (w_both.transpose(0, 2, 1)[:, :, None, :, None] * row_hot.transpose(1, 0, 2)[None, None]).astype(bf)
    out = jnp.einsum("htrsa,scaq->htcrq", lhs, spread, preferred_element_type=f32)
    return out[0] + out[1]


def body(visibilities, coords, vis_counts, cover_tile, offsets, channel, taper):
    n_span = lax.axis_size("span")
    n_freq = lax.axis_size("freq")
    channels = CH_DEV * n_freq
    freq_pos = lax.axis_index("freq")
    sub_count = visibilities.shape[1]
    groups = sub_count // 32
    vis_loc = visibilities[0].reshape(groups, 32, 2, -1)
    coord_loc = coords[0].reshape(groups, 32, 2, -1)
    count_loc = vis_counts[0].reshape(groups, 32)

    def block_work(inputs):
        return make_subgrids(inputs[0], inputs[1], inputs[2], taper)

    patches = lax.map(block_work, (vis_loc, coord_loc, count_loc)).reshape(sub_count, 2, 32, 32)
    dest = cover_tile[0, :, 0]
    row_off = offsets[0, :, 0]
    col_off = offsets[0, :, 1]
    chan_loc = channel[0]
    cap = 2 * sub_count // n_span
    order = jnp.arange(sub_count, dtype=jnp.int32)
    before = (dest[:, None] == dest[None, :]) & (order[:, None] > order[None, :])
    rank = jnp.sum(before.astype(jnp.int32), axis=1)
    slot = dest * cap + rank
    info = jnp.stack([jnp.ones_like(dest), row_off, col_off, chan_loc], 1).astype(jnp.bfloat16)
    rows = jnp.concatenate([patches.reshape(sub_count, 2048), info], axis=1)
    pick = (slot[None, :] == jnp.arange(n_span * cap, dtype=jnp.int32)[:, None]).astype(jnp.bfloat16)
    send = jnp.dot(pick, rows, preferred_element_type=jnp.float32).astype(jnp.bfloat16)
    got = lax.all_to_all(send.reshape(n_span, cap, 2052), "span", 0, 0, tiled=True)
    got_payload, got_meta = got[:, :, :2048], got[:, :, 2048:]
    slots = n_span * cap
    got_meta = got_meta.reshape(slots, 4).astype(jnp.int32)
    valid = got_meta[:, 0].astype(jnp.float32)
    weight = taylor_weights(got_meta[:, 3], freq_pos, channels) * valid[:, None]
    local = place_all(
        got_payload.reshape(slots, 2, 32, 32), weight, got_meta[:, 1], got_meta[:, 2]
    )
    local = local.reshape(NT, 1, 2, TILE, TILE)
    total = gathered_total(local, "freq")
    scale = TILE / (32.0 * math.sqrt(n_freq * sub_count))
    return total * scale


def solution(mesh):
    return jax.shard_map(
        body,
        mesh=mesh,
        in_specs=(
            P("freq", "span", None, None),
            P("freq", "span", None, None),
            P("freq", "span"),
            P("freq", "span", None),
            P("freq", "span", None),
            P("freq", "span"),
            P(),
        ),
        out_specs=P(None, "span", None, None, None),
        check_vma=False,
    )
```

```python
import math

import jax
import jax.numpy as jnp
from jax import lax
from jax.experimental import pallas as pl
from jax.experimental.pallas import tpu as pltpu
from jax.sharding import PartitionSpec as P

TILE = 128
NT = 2
CH_DEV = 16


def sent_together(arrays, axis, split_dim, concat_dim, along):
    widths = [a.shape[along] for a in arrays]
    both = jnp.concatenate(arrays, axis=along)
    whole = lax.all_to_all(both, axis, split_axis=split_dim, concat_axis=concat_dim, tiled=True)
    return tuple(jnp.split(whole, [sum(widths[:k]) for k in range(1, len(widths))], axis=along))


def gathered_total(shard, axis):
    n = lax.axis_size(axis)
    flat = shard.reshape(-1)
    size = flat.shape[0]
    per = -(-size // (n * 128)) * 128
    flat = jnp.pad(flat, (0, per * n - size))
    got = lax.all_to_all(flat.reshape(n, per // 128, 128), axis, 0, 0, tiled=True)
    part = got.sum(axis=0)
    spread = jnp.broadcast_to(part.astype(jnp.bfloat16)[None], (n, per // 128, 128))
    whole = lax.all_to_all(spread, axis, 0, 0, tiled=True).astype(jnp.float32)
    return whole.reshape(-1)[:size].reshape(shard.shape)


def cmul(ar, ai, br, bi):
    return ar * br - ai * bi, ar * bi + ai * br


def kernel_tables(angle, vis=None):
    c, s = jnp.cos(angle), jnp.sin(angle)
    w1 = (c, s)
    w2 = cmul(*w1, *w1)
    w4 = cmul(*w2, *w2)
    w8 = cmul(*w4, *w4)
    w16 = cmul(*w8, *w8)
    lo = (w16[0], -w16[1])
    if vis is not None:
        lo = cmul(*vis, *lo)
    one = (jnp.ones_like(c), jnp.zeros_like(c))
    small = [one, w1, w2, cmul(*w2, *w1)]
    big = []
    for j in range(8):
        q = lo
        for bit, wp in enumerate((w4, w8, w16)):
            if (j >> bit) & 1:
                q = cmul(*q, *wp)
        big.append(q)
    return small, big


def kernel_rows(small, big, b):
    p_r = jnp.concatenate([small[i % 4][0][b : b + 1] for i in range(8)], axis=0)
    p_i = jnp.concatenate([small[i % 4][1][b : b + 1] for i in range(8)], axis=0)
    first = lax.broadcasted_iota(jnp.int32, p_r.shape, 0) < 4
    res, ims = [], []
    for m in range(4):
        qa, qb = big[2 * m], big[2 * m + 1]
        q_r = jnp.where(first, qa[0][b : b + 1], qb[0][b : b + 1])
        q_i = jnp.where(first, qa[1][b : b + 1], qb[1][b : b + 1])
        r, i = cmul(q_r, q_i, p_r, p_i)
        res.append(r)
        ims.append(i)
    return jnp.concatenate(res + ims, axis=0).astype(jnp.bfloat16)


def s_kernel(coord_ref, vis_ref, count_ref, out):
    kk = coord_ref.shape[-1]
    step = -2.0 * math.pi / 32.0
    per = coord_ref.shape[0]
    sub = lax.broadcasted_iota(jnp.int32, (per, kk), 0)
    limit = jnp.zeros((per, kk), jnp.int32)
    for b in range(per):
        limit = jnp.where(sub == b, count_ref[0, pl.program_id(0) * per + b], limit)
    live = lax.broadcasted_iota(jnp.int32, (per, kk), 1) < limit
    scale_k = 1.0 / math.sqrt(kk)
    vis = vis_ref[...].astype(jnp.float32)
    coord = coord_ref[...]
    vr = jnp.where(live, vis[:, 0, :] * scale_k, 0.0)
    vi = jnp.where(live, vis[:, 1, :] * scale_k, 0.0)
    small_u, big_u = kernel_tables(step * coord[:, 0, :])
    small_v, big_v = kernel_tables(step * coord[:, 1, :], (vr, vi))
    for b in range(out.shape[0]):
        a = kernel_rows(small_u, big_u, b)
        bb = kernel_rows(small_v, big_v, b)
        out[b] = lax.dot_general(
            a, bb, (((1,), (1,)), ((), ())), preferred_element_type=jnp.float32
        )


def s_matrices(coords, vis, counts):
    n, _, kk = coords.shape
    per = 16
    both = pl.BlockSpec((per, 2, kk), lambda g: (g, 0, 0))
    return pl.pallas_call(
        s_kernel,
        grid=(n // per,),
        in_specs=[both, both, pl.BlockSpec(memory_space=pltpu.SMEM)],
        out_specs=pl.BlockSpec((per, 64, 64), lambda g: (g, 0, 0)),
        out_shape=jax.ShapeDtypeStruct((n, 64, 64), jnp.float32),
        cost_estimate=pl.CostEstimate(
            flops=2 * n * 64 * 64 * kk + 24 * n * 64 * kk,
            transcendentals=4 * n * kk,
            bytes_accessed=6 * n * 2 * kk + 4 * n * 64 * 64,
        ),
    )(coords, vis, counts)


def make_subgrids(vis_b, coord_b, count_b, taper):
    s_all = s_matrices(coord_b, vis_b, count_b.reshape(1, -1))
    s_re = s_all[:, :32, :32] - s_all[:, 32:, 32:]
    s_im = s_all[:, :32, 32:] + s_all[:, 32:, :32]
    x2 = jnp.concatenate([taper * s_re, taper * s_im], axis=1)
    centred = jnp.arange(32, dtype=jnp.float32) - 16.0
    angle = -2.0 * math.pi * centred[:, None] * centred[None, :] / 32.0
    f_re, f_im = (jnp.cos(angle), jnp.sin(angle))
    hp = lax.Precision.HIGH
    left = jnp.concatenate(
        [jnp.concatenate([f_re, -f_im], 1), jnp.concatenate([f_im, f_re], 1)], 0
    )
    y2 = jnp.einsum("ij,bjq->biq", left, x2, precision=hp)
    ycat = jnp.concatenate([y2[:, :32], y2[:, 32:]], axis=2)
    right = jnp.concatenate(
        [jnp.concatenate([f_re, f_im], 1), jnp.concatenate([-f_im, f_re], 1)], 0
    )
    z2 = jnp.einsum("baj,jk->bak", ycat, right, precision=hp)
    z = z2.reshape(z2.shape[0], 32, 2, 32).transpose(0, 2, 1, 3)
    return (z / 32.0).astype(jnp.bfloat16)


def taylor_weights(chan_local, freq_pos, channels):
    global_chan = (freq_pos * CH_DEV + chan_local).astype(jnp.float32)
    xval = (2.0 * global_chan + 1.0 - channels) / channels
    powers = jnp.arange(NT, dtype=jnp.float32)
    return jnp.where(powers[None, :] == 0.0, 1.0, xval[:, None] ** powers[None, :])


def place_all(patch, weight, rows, cols):
    bf, f32 = jnp.bfloat16, jnp.float32
    cells = jnp.arange(TILE, dtype=jnp.int32)
    small = jnp.arange(32, dtype=jnp.int32)
    col_hot = (small[None, :, None] + cols[:, None, None] == cells[None, None, :]).astype(bf)
    spread = jnp.einsum("scab,sbq->scaq", patch, col_hot, preferred_element_type=f32).astype(bf)
    row_hot = (cells[None, :, None] == rows[:, None, None] + small[None, None, :]).astype(f32)
    w_hi = weight.astype(bf)
    w_lo = (weight - w_hi.astype(f32)).astype(bf)
    w_both = jnp.stack([w_hi, w_lo], 0).astype(f32)
    lhs = (w_both.transpose(0, 2, 1)[:, :, None, :, None] * row_hot.transpose(1, 0, 2)[None, None]).astype(bf)
    out = jnp.einsum("htrsa,scaq->htcrq", lhs, spread, preferred_element_type=f32)
    return out[0] + out[1]


def body(visibilities, coords, vis_counts, cover_tile, offsets, channel, taper):
    n_span = lax.axis_size("span")
    n_freq = lax.axis_size("freq")
    channels = CH_DEV * n_freq
    freq_pos = lax.axis_index("freq")
    sub_count = visibilities.shape[1]
    groups = sub_count // 32
    vis_loc = visibilities[0].reshape(groups, 32, 2, -1)
    coord_loc = coords[0].reshape(groups, 32, 2, -1)
    count_loc = vis_counts[0].reshape(groups, 32)

    def block_work(inputs):
        return make_subgrids(inputs[0], inputs[1], inputs[2], taper)

    patches = lax.map(block_work, (vis_loc, coord_loc, count_loc)).reshape(sub_count, 2, 32, 32)
    dest = cover_tile[0, :, 0]
    row_off = offsets[0, :, 0]
    col_off = offsets[0, :, 1]
    chan_loc = channel[0]
    cap = 2 * sub_count // n_span
    order = jnp.arange(sub_count, dtype=jnp.int32)
    before = (dest[:, None] == dest[None, :]) & (order[:, None] > order[None, :])
    rank = jnp.sum(before.astype(jnp.int32), axis=1)
    slot = dest * cap + rank
    info = jnp.stack([jnp.ones_like(dest), row_off, col_off, chan_loc], 1).astype(jnp.bfloat16)
    rows = jnp.concatenate([patches.reshape(sub_count, 2048), info], axis=1)
    pick = (slot[None, :] == jnp.arange(n_span * cap, dtype=jnp.int32)[:, None]).astype(jnp.bfloat16)
    send = jnp.dot(pick, rows, preferred_element_type=jnp.float32).astype(jnp.bfloat16)
    got = lax.all_to_all(send.reshape(n_span, cap, 2052), "span", 0, 0, tiled=True)
    got_payload, got_meta = got[:, :, :2048], got[:, :, 2048:]
    slots = n_span * cap
    got_meta = got_meta.reshape(slots, 4).astype(jnp.int32)
    valid = got_meta[:, 0].astype(jnp.float32)
    weight = taylor_weights(got_meta[:, 3], freq_pos, channels) * valid[:, None]
    local = place_all(
        got_payload.reshape(slots, 2, 32, 32), weight, got_meta[:, 1], got_meta[:, 2]
    )
    local = local.reshape(NT, 1, 2, TILE, TILE)
    total = gathered_total(local, "freq")
    scale = TILE / (32.0 * math.sqrt(n_freq * sub_count))
    return total * scale


def solution(mesh):
    return jax.shard_map(
        body,
        mesh=mesh,
        in_specs=(
            P("freq", "span", None, None),
            P("freq", "span", None, None),
            P("freq", "span"),
            P("freq", "span", None),
            P("freq", "span", None),
            P("freq", "span"),
            P(),
        ),
        out_specs=P(None, "span", None, None, None),
        check_vma=False,
    )
```

```python
import math

import jax
import jax.numpy as jnp
from jax import lax
from jax.experimental import pallas as pl
from jax.experimental.pallas import tpu as pltpu
from jax.sharding import PartitionSpec as P

TILE = 128
NT = 2
CH_DEV = 16


def sent_together(arrays, axis, split_dim, concat_dim, along):
    widths = [a.shape[along] for a in arrays]
    both = jnp.concatenate(arrays, axis=along)
    whole = lax.all_to_all(both, axis, split_axis=split_dim, concat_axis=concat_dim, tiled=True)
    return tuple(jnp.split(whole, [sum(widths[:k]) for k in range(1, len(widths))], axis=along))


def gathered_total(shard, axis, scale):
    n = lax.axis_size(axis)
    flat = shard.reshape(-1)
    size = flat.shape[0]
    per = -(-size // (n * 128)) * 128
    flat = jnp.pad(flat, (0, per * n - size))
    got = lax.all_to_all(flat.reshape(n, per // 128, 128), axis, 0, 0, tiled=True)
    part = got.sum(axis=0)
    spread = jnp.broadcast_to((part * scale).astype(jnp.bfloat16)[None], (n, per // 128, 128))
    whole = lax.all_to_all(spread, axis, 0, 0, tiled=True).astype(jnp.float32)
    return whole.reshape(-1)[:size].reshape(shard.shape)


def cmul(ar, ai, br, bi):
    return ar * br - ai * bi, ar * bi + ai * br


def kernel_tables(angle, vis=None):
    c, s = jnp.cos(angle), jnp.sin(angle)
    w1 = (c, s)
    w2 = cmul(*w1, *w1)
    w4 = cmul(*w2, *w2)
    w8 = cmul(*w4, *w4)
    w16 = cmul(*w8, *w8)
    lo = (w16[0], -w16[1])
    if vis is not None:
        lo = cmul(*vis, *lo)
    one = (jnp.ones_like(c), jnp.zeros_like(c))
    small = [one, w1, w2, cmul(*w2, *w1)]
    big = []
    for j in range(8):
        q = lo
        for bit, wp in enumerate((w4, w8, w16)):
            if (j >> bit) & 1:
                q = cmul(*q, *wp)
        big.append(q)
    return small, big


def kernel_rows(small, big, b):
    p_r = jnp.concatenate([small[i % 4][0][b : b + 1] for i in range(8)], axis=0)
    p_i = jnp.concatenate([small[i % 4][1][b : b + 1] for i in range(8)], axis=0)
    first = lax.broadcasted_iota(jnp.int32, p_r.shape, 0) < 4
    res, ims = [], []
    for m in range(4):
        qa, qb = big[2 * m], big[2 * m + 1]
        q_r = jnp.where(first, qa[0][b : b + 1], qb[0][b : b + 1])
        q_i = jnp.where(first, qa[1][b : b + 1], qb[1][b : b + 1])
        r, i = cmul(q_r, q_i, p_r, p_i)
        res.append(r)
        ims.append(i)
    return jnp.concatenate(res + ims, axis=0).astype(jnp.bfloat16)


def s_kernel(coord_ref, vis_ref, count_ref, out):
    kk = coord_ref.shape[-1]
    step = -2.0 * math.pi / 32.0
    per = coord_ref.shape[0]
    sub = lax.broadcasted_iota(jnp.int32, (per, kk), 0)
    limit = jnp.zeros((per, kk), jnp.int32)
    for b in range(per):
        limit = jnp.where(sub == b, count_ref[0, pl.program_id(0) * per + b], limit)
    live = lax.broadcasted_iota(jnp.int32, (per, kk), 1) < limit
    scale_k = 1.0 / math.sqrt(kk)
    vis = vis_ref[...].astype(jnp.float32)
    coord = coord_ref[...]
    vr = jnp.where(live, vis[:, 0, :] * scale_k, 0.0)
    vi = jnp.where(live, vis[:, 1, :] * scale_k, 0.0)
    small_u, big_u = kernel_tables(step * coord[:, 0, :])
    small_v, big_v = kernel_tables(step * coord[:, 1, :], (vr, vi))
    for b in range(out.shape[0]):
        a = kernel_rows(small_u, big_u, b)
        bb = kernel_rows(small_v, big_v, b)
        out[b] = lax.dot_general(
            a, bb, (((1,), (1,)), ((), ())), preferred_element_type=jnp.float32
        )


def s_matrices(coords, vis, counts):
    n, _, kk = coords.shape
    per = 8
    both = pl.BlockSpec((per, 2, kk), lambda g: (g, 0, 0))
    return pl.pallas_call(
        s_kernel,
        grid=(n // per,),
        in_specs=[both, both, pl.BlockSpec(memory_space=pltpu.SMEM)],
        out_specs=pl.BlockSpec((per, 64, 64), lambda g: (g, 0, 0)),
        out_shape=jax.ShapeDtypeStruct((n, 64, 64), jnp.float32),
        cost_estimate=pl.CostEstimate(
            flops=2 * n * 64 * 64 * kk + 24 * n * 64 * kk,
            transcendentals=4 * n * kk,
            bytes_accessed=6 * n * 2 * kk + 4 * n * 64 * 64,
        ),
    )(coords, vis, counts)


def make_subgrids(vis_b, coord_b, count_b, taper):
    s_all = s_matrices(coord_b, vis_b, count_b.reshape(1, -1))
    s_re = s_all[:, :32, :32] - s_all[:, 32:, 32:]
    s_im = s_all[:, :32, 32:] + s_all[:, 32:, :32]
    x2 = jnp.concatenate([taper * s_re, taper * s_im], axis=1)
    centred = jnp.arange(32, dtype=jnp.float32) - 16.0
    angle = -2.0 * math.pi * centred[:, None] * centred[None, :] / 32.0
    f_re, f_im = (jnp.cos(angle), jnp.sin(angle))
    hp = lax.Precision.HIGH
    left = jnp.concatenate(
        [jnp.concatenate([f_re, -f_im], 1), jnp.concatenate([f_im, f_re], 1)], 0
    )
    y2 = jnp.einsum("ij,bjq->biq", left, x2, precision=hp)
    ycat = jnp.concatenate([y2[:, :32], y2[:, 32:]], axis=2)
    right = jnp.concatenate(
        [jnp.concatenate([f_re, f_im], 1), jnp.concatenate([-f_im, f_re], 1)], 0
    )
    z2 = jnp.einsum("baj,jk->bak", ycat, right, precision=hp)
    z = z2.reshape(z2.shape[0], 32, 2, 32).transpose(0, 2, 1, 3)
    return (z / 32.0).astype(jnp.bfloat16)


def taylor_weights(chan_local, freq_pos, channels):
    global_chan = (freq_pos * CH_DEV + chan_local).astype(jnp.float32)
    xval = (2.0 * global_chan + 1.0 - channels) / channels
    powers = jnp.arange(NT, dtype=jnp.float32)
    return jnp.where(powers[None, :] == 0.0, 1.0, xval[:, None] ** powers[None, :])


def place_all(patch, weight, rows, cols):
    bf, f32 = jnp.bfloat16, jnp.float32
    cells = jnp.arange(TILE, dtype=jnp.int32)
    small = jnp.arange(32, dtype=jnp.int32)
    col_hot = (small[None, :, None] + cols[:, None, None] == cells[None, None, :]).astype(bf)
    spread = jnp.einsum("scab,sbq->scaq", patch, col_hot, preferred_element_type=f32).astype(bf)
    row_hot = (cells[None, :, None] == rows[:, None, None] + small[None, None, :]).astype(f32)
    w_hi = weight.astype(bf)
    w_lo = (weight - w_hi.astype(f32)).astype(bf)
    w_both = jnp.stack([w_hi, w_lo], 0).astype(f32)
    lhs = (w_both.transpose(0, 2, 1)[:, :, None, :, None] * row_hot.transpose(1, 0, 2)[None, None]).astype(bf)
    out = jnp.einsum("htrsa,scaq->htcrq", lhs, spread, preferred_element_type=f32)
    return out[0] + out[1]


def body(visibilities, coords, vis_counts, cover_tile, offsets, channel, taper):
    n_span = lax.axis_size("span")
    n_freq = lax.axis_size("freq")
    channels = CH_DEV * n_freq
    freq_pos = lax.axis_index("freq")
    sub_count = visibilities.shape[1]
    groups = sub_count // 32
    vis_loc = visibilities[0].reshape(groups, 32, 2, -1)
    coord_loc = coords[0].reshape(groups, 32, 2, -1)
    count_loc = vis_counts[0].reshape(groups, 32)

    def block_work(inputs):
        return make_subgrids(inputs[0], inputs[1], inputs[2], taper)

    patches = lax.map(block_work, (vis_loc, coord_loc, count_loc)).reshape(sub_count, 2, 32, 32)
    dest = cover_tile[0, :, 0]
    row_off = offsets[0, :, 0]
    col_off = offsets[0, :, 1]
    chan_loc = channel[0]
    cap = 2 * sub_count // n_span
    order = jnp.arange(sub_count, dtype=jnp.int32)
    before = (dest[:, None] == dest[None, :]) & (order[:, None] > order[None, :])
    rank = jnp.sum(before.astype(jnp.int32), axis=1)
    slot = dest * cap + rank
    info = jnp.stack([jnp.ones_like(dest), row_off, col_off, chan_loc], 1).astype(jnp.bfloat16)
    rows = jnp.concatenate([patches.reshape(sub_count, 2048), info], axis=1)
    pick = (slot[None, :] == jnp.arange(n_span * cap, dtype=jnp.int32)[:, None]).astype(jnp.bfloat16)
    send = jnp.dot(pick, rows, preferred_element_type=jnp.float32).astype(jnp.bfloat16)
    got = lax.all_to_all(send.reshape(n_span, cap, 2052), "span", 0, 0, tiled=True)
    got_payload, got_meta = got[:, :, :2048], got[:, :, 2048:]
    slots = n_span * cap
    got_meta = got_meta.reshape(slots, 4).astype(jnp.int32)
    valid = got_meta[:, 0].astype(jnp.float32)
    weight = taylor_weights(got_meta[:, 3], freq_pos, channels) * valid[:, None]
    local = place_all(
        got_payload.reshape(slots, 2, 32, 32), weight, got_meta[:, 1], got_meta[:, 2]
    )
    local = local.reshape(NT, 1, 2, TILE, TILE)
    scale = TILE / (32.0 * math.sqrt(n_freq * sub_count))
    return gathered_total(local, "freq", scale)


def solution(mesh):
    return jax.shard_map(
        body,
        mesh=mesh,
        in_specs=(
            P("freq", "span", None, None),
            P("freq", "span", None, None),
            P("freq", "span"),
            P("freq", "span", None),
            P("freq", "span", None),
            P("freq", "span"),
            P(),
        ),
        out_specs=P(None, "span", None, None, None),
        check_vma=False,
    )
```

```python
import math

import jax
import jax.numpy as jnp
from jax import lax
from jax.experimental import pallas as pl
from jax.experimental.pallas import tpu as pltpu
from jax.sharding import PartitionSpec as P

TILE = 128
NT = 2
CH_DEV = 16


def sent_together(arrays, axis, split_dim, concat_dim, along):
    widths = [a.shape[along] for a in arrays]
    both = jnp.concatenate(arrays, axis=along)
    whole = lax.all_to_all(both, axis, split_axis=split_dim, concat_axis=concat_dim, tiled=True)
    return tuple(jnp.split(whole, [sum(widths[:k]) for k in range(1, len(widths))], axis=along))


def gathered_total(shard, axis):
    n = lax.axis_size(axis)
    flat = shard.reshape(-1)
    size = flat.shape[0]
    per = -(-size // (n * 128)) * 128
    flat = jnp.pad(flat, (0, per * n - size))
    got = lax.all_to_all(flat.reshape(n, per // 128, 128), axis, 0, 0, tiled=True)
    part = got.sum(axis=0)
    spread = jnp.broadcast_to(part.astype(jnp.bfloat16)[None], (n, per // 128, 128))
    whole = lax.all_to_all(spread, axis, 0, 0, tiled=True).astype(jnp.float32)
    return whole.reshape(-1)[:size].reshape(shard.shape)


def cmul(ar, ai, br, bi):
    return ar * br - ai * bi, ar * bi + ai * br


def kernel_tables(angle, vis=None):
    c, s = jnp.cos(angle), jnp.sin(angle)
    w1 = (c, s)
    w2 = cmul(*w1, *w1)
    w4 = cmul(*w2, *w2)
    w8 = cmul(*w4, *w4)
    w16 = cmul(*w8, *w8)
    lo = (w16[0], -w16[1])
    if vis is not None:
        lo = cmul(*vis, *lo)
    one = (jnp.ones_like(c), jnp.zeros_like(c))
    small = [one, w1, w2, cmul(*w2, *w1)]
    big = []
    for j in range(8):
        q = lo
        for bit, wp in enumerate((w4, w8, w16)):
            if (j >> bit) & 1:
                q = cmul(*q, *wp)
        big.append(q)
    return small, big


def kernel_rows(small, big, b):
    p_r = jnp.concatenate([small[i % 4][0][b : b + 1] for i in range(8)], axis=0)
    p_i = jnp.concatenate([small[i % 4][1][b : b + 1] for i in range(8)], axis=0)
    first = lax.broadcasted_iota(jnp.int32, p_r.shape, 0) < 4
    res, ims = [], []
    for m in range(4):
        qa, qb = big[2 * m], big[2 * m + 1]
        q_r = jnp.where(first, qa[0][b : b + 1], qb[0][b : b + 1])
        q_i = jnp.where(first, qa[1][b : b + 1], qb[1][b : b + 1])
        r, i = cmul(q_r, q_i, p_r, p_i)
        res.append(r)
        ims.append(i)
    return jnp.concatenate(res + ims, axis=0).astype(jnp.bfloat16)


def s_kernel(coord_ref, vis_ref, count_ref, out):
    kk = coord_ref.shape[-1]
    step = -2.0 * math.pi / 32.0
    per = coord_ref.shape[0]
    sub = lax.broadcasted_iota(jnp.int32, (per, kk), 0)
    limit = jnp.zeros((per, kk), jnp.int32)
    for b in range(per):
        limit = jnp.where(sub == b, count_ref[0, pl.program_id(0) * per + b], limit)
    live = lax.broadcasted_iota(jnp.int32, (per, kk), 1) < limit
    scale_k = 1.0 / math.sqrt(kk)
    vis = vis_ref[...].astype(jnp.float32)
    coord = coord_ref[...]
    vr = jnp.where(live, vis[:, 0, :] * scale_k, 0.0)
    vi = jnp.where(live, vis[:, 1, :] * scale_k, 0.0)
    small_u, big_u = kernel_tables(step * coord[:, 0, :])
    small_v, big_v = kernel_tables(step * coord[:, 1, :], (vr, vi))
    for b in range(out.shape[0]):
        a = kernel_rows(small_u, big_u, b)
        bb = kernel_rows(small_v, big_v, b)
        out[b] = lax.dot_general(
            a, bb, (((1,), (1,)), ((), ())), preferred_element_type=jnp.float32
        )


def s_matrices(coords, vis, counts):
    n, _, kk = coords.shape
    per = 8
    both = pl.BlockSpec((per, 2, kk), lambda g: (g, 0, 0))
    return pl.pallas_call(
        s_kernel,
        grid=(n // per,),
        in_specs=[both, both, pl.BlockSpec(memory_space=pltpu.SMEM)],
        out_specs=pl.BlockSpec((per, 64, 64), lambda g: (g, 0, 0)),
        out_shape=jax.ShapeDtypeStruct((n, 64, 64), jnp.float32),
        cost_estimate=pl.CostEstimate(
            flops=2 * n * 64 * 64 * kk + 24 * n * 64 * kk,
            transcendentals=4 * n * kk,
            bytes_accessed=6 * n * 2 * kk + 4 * n * 64 * 64,
        ),
    )(coords, vis, counts)


def make_subgrids(vis_b, coord_b, count_b, taper):
    s_all = s_matrices(coord_b, vis_b, count_b.reshape(1, -1))
    s_re = s_all[:, :32, :32] - s_all[:, 32:, 32:]
    s_im = s_all[:, :32, 32:] + s_all[:, 32:, :32]
    x2 = jnp.concatenate([taper * s_re, taper * s_im], axis=1)
    centred = jnp.arange(32, dtype=jnp.float32) - 16.0
    angle = -2.0 * math.pi * centred[:, None] * centred[None, :] / 32.0
    f_re, f_im = (jnp.cos(angle), jnp.sin(angle))
    hp = lax.Precision.HIGH
    left = jnp.concatenate(
        [jnp.concatenate([f_re, -f_im], 1), jnp.concatenate([f_im, f_re], 1)], 0
    )
    y2 = jnp.einsum("ij,bjq->biq", left, x2, precision=hp)
    ycat = jnp.concatenate([y2[:, :32], y2[:, 32:]], axis=2)
    right = jnp.concatenate(
        [jnp.concatenate([f_re, f_im], 1), jnp.concatenate([-f_im, f_re], 1)], 0
    )
    z2 = jnp.einsum("baj,jk->bak", ycat, right, preferred_element_type=jnp.float32)
    z = z2.reshape(z2.shape[0], 32, 2, 32).transpose(0, 2, 1, 3)
    return (z / 32.0).astype(jnp.bfloat16)


def taylor_weights(chan_local, freq_pos, channels):
    global_chan = (freq_pos * CH_DEV + chan_local).astype(jnp.float32)
    xval = (2.0 * global_chan + 1.0 - channels) / channels
    powers = jnp.arange(NT, dtype=jnp.float32)
    return jnp.where(powers[None, :] == 0.0, 1.0, xval[:, None] ** powers[None, :])


def place_all(patch, weight, rows, cols):
    bf, f32 = jnp.bfloat16, jnp.float32
    cells = jnp.arange(TILE, dtype=jnp.int32)
    small = jnp.arange(32, dtype=jnp.int32)
    col_hot = (small[None, :, None] + cols[:, None, None] == cells[None, None, :]).astype(bf)
    spread = jnp.einsum("scab,sbq->scaq", patch, col_hot, preferred_element_type=f32).astype(bf)
    row_hot = (cells[None, :, None] == rows[:, None, None] + small[None, None, :]).astype(f32)
    w_hi = weight.astype(bf)
    w_lo = (weight - w_hi.astype(f32)).astype(bf)
    w_both = jnp.stack([w_hi, w_lo], 0).astype(f32)
    lhs = (w_both.transpose(0, 2, 1)[:, :, None, :, None] * row_hot.transpose(1, 0, 2)[None, None]).astype(bf)
    out = jnp.einsum("htrsa,scaq->htcrq", lhs, spread, preferred_element_type=f32)
    return out[0] + out[1]


def body(visibilities, coords, vis_counts, cover_tile, offsets, channel, taper):
    n_span = lax.axis_size("span")
    n_freq = lax.axis_size("freq")
    channels = CH_DEV * n_freq
    freq_pos = lax.axis_index("freq")
    sub_count = visibilities.shape[1]
    groups = sub_count // 32
    vis_loc = visibilities[0].reshape(groups, 32, 2, -1)
    coord_loc = coords[0].reshape(groups, 32, 2, -1)
    count_loc = vis_counts[0].reshape(groups, 32)

    def block_work(inputs):
        return make_subgrids(inputs[0], inputs[1], inputs[2], taper)

    patches = lax.map(block_work, (vis_loc, coord_loc, count_loc)).reshape(sub_count, 2, 32, 32)
    dest = cover_tile[0, :, 0]
    row_off = offsets[0, :, 0]
    col_off = offsets[0, :, 1]
    chan_loc = channel[0]
    cap = 2 * sub_count // n_span
    order = jnp.arange(sub_count, dtype=jnp.int32)
    before = (dest[:, None] == dest[None, :]) & (order[:, None] > order[None, :])
    rank = jnp.sum(before.astype(jnp.int32), axis=1)
    slot = dest * cap + rank
    info = jnp.stack([jnp.ones_like(dest), row_off, col_off, chan_loc], 1).astype(jnp.bfloat16)
    rows = jnp.concatenate([patches.reshape(sub_count, 2048), info], axis=1)
    pick = (slot[None, :] == jnp.arange(n_span * cap, dtype=jnp.int32)[:, None]).astype(jnp.bfloat16)
    send = jnp.dot(pick, rows, preferred_element_type=jnp.float32).astype(jnp.bfloat16)
    got = lax.all_to_all(send.reshape(n_span, cap, 2052), "span", 0, 0, tiled=True)
    got_payload, got_meta = got[:, :, :2048], got[:, :, 2048:]
    slots = n_span * cap
    got_meta = got_meta.reshape(slots, 4).astype(jnp.int32)
    valid = got_meta[:, 0].astype(jnp.float32)
    weight = taylor_weights(got_meta[:, 3], freq_pos, channels) * valid[:, None]
    local = place_all(
        got_payload.reshape(slots, 2, 32, 32), weight, got_meta[:, 1], got_meta[:, 2]
    )
    local = local.reshape(NT, 1, 2, TILE, TILE)
    total = gathered_total(local, "freq")
    scale = TILE / (32.0 * math.sqrt(n_freq * sub_count))
    return total * scale


def solution(mesh):
    return jax.shard_map(
        body,
        mesh=mesh,
        in_specs=(
            P("freq", "span", None, None),
            P("freq", "span", None, None),
            P("freq", "span"),
            P("freq", "span", None),
            P("freq", "span", None),
            P("freq", "span"),
            P(),
        ),
        out_specs=P(None, "span", None, None, None),
        check_vma=False,
    )
```
